32 devices in a mesh: grp: 2 (over y), seq: 4 (over z), head: 2 (over x), sub: 2 (over core).
Axes of the slice: x: 2, y: 2, z: 4, core: 2. Of those that a mesh axis runs over, the one named last changes fastest.
Arguments:
- query_rows: bfloat16 [3072, 1024], P(('grp', 'seq', 'sub'), 'head'), parts along dimension 0, may hold values from -8 to 8
- key_rows: bfloat16 [3072, 1024], P(('grp', 'seq', 'sub'), 'head'), parts along dimension 0, may hold values from -8 to 8
- value_rows: bfloat16 [3072, 1024], P(('grp', 'seq', 'sub'), 'head'), parts along dimension 0, may hold values from -8 to 8
- clip_lengths: int32 [12], P('grp'), parts along dimension 0, may hold values from 1 to 768, 1536 in all
- block_mask: int32 [48, 24], P(('grp', 'seq')), parts along dimension 0, may hold values from 0 to 1, as said below
- out_weight: bfloat16 [1024, 1024], replicated
- norm_gain: bfloat16 [1024], P('head'), may hold values from 0.099609375 to 1.8984375
Outputs:
- layer_output: bfloat16 [3072, 1024], P(('grp', 'seq', 'sub'), 'head'), parts along dimension 0
The draws below stay inside these ranges and needn't reach their ends.
There are 2 independent parts, one for each index of `grp`. The reference program is written for one: setup_inputs(seed, part) draws one part's arguments, and reference() takes and returns one part's arrays. A program takes and returns all parts, laid end to end along the dimension named above; an argument that names none is the same for every part. Nothing has to cross between parts.
Inputs may be any that keep to these rules, and one draw needn't show every extreme that they name: `clip_lengths`: 6 clip lengths that sum to 1536; the longest is exactly 768. block_mask[i, i] = 1 for every block i.
All inputs are finite; a program needn't handle non-finite values.
Results may differ from the reference program's by a relative error of at most 0.01.
Values may be sent and summed in bfloat16 or wider, within the bound.
No kernel may reach another device: no remote copies, remote signals or barrier semaphores. Data moves between devices by JAX's collectives and lax.ppermute only.
A program may use at most 64 MiB of HBM per device.

```python
import math
import jax
import jax.numpy as jnp
import numpy as np
from jax import lax

D = 1024
H = 16
HD = 64
BLK = 64
F = 64
CLIPS = 6
S = 1536
NB = 24


def draw_query_rows(key, part):
    base = jnp.clip(jax.random.normal(jax.random.fold_in(key, 11), (S, H * HD), jnp.float32), -8.0, 8.0)
    return base.astype(jnp.bfloat16)


def draw_key_rows(key, part):
    base = jnp.clip(jax.random.normal(jax.random.fold_in(key, 12), (S, H * HD), jnp.float32), -8.0, 8.0)
    return base.astype(jnp.bfloat16)


def draw_block_mask(key, part):
    tickets = jax.random.randint(jax.random.fold_in(key, 1), (NB, NB), 0, 100)
    limits = jax.random.randint(jax.random.fold_in(key, 2), (NB, 1), 15, 90)
    row_ids = lax.broadcasted_iota(jnp.int32, (NB, NB), 0)
    col_ids = lax.broadcasted_iota(jnp.int32, (NB, NB), 1)
    return jnp.where((tickets < limits) | (row_ids == col_ids), 1, 0).astype(jnp.int32)


def draw_out_weight(key, part):
    base = jax.random.normal(jax.random.fold_in(key, 21), (H * HD, D), jnp.float32) * (1.0 / math.sqrt(H * HD))
    col_ids = lax.broadcasted_iota(jnp.float32, (1, D), 1)
    rising = 1.0 + 2.0 * col_ids / (D - 1)
    return (base * rising).astype(jnp.bfloat16)


def shard_levels(key, shape, pieces, low, top_value):
    def one(position, blocks):
        steps = jax.random.uniform(jax.random.fold_in(jax.random.fold_in(key, 6), position), (blocks,), jnp.float32, low / len(pieces), top_value / len(pieces))
        return jnp.repeat(jnp.exp(steps), shape[position] // blocks).reshape((-1,) + (1,) * (len(shape) - position - 1))

    factor_of = one(*pieces[0])
    for cut in pieces[1:]:
        factor_of = factor_of * one(*cut)
    return factor_of


def length_profile(count, total, bound, lean):
    portions = [(1 << 20) // math.isqrt(grade ** lean) + 1 for grade in range(2, count + 1)]
    surplus, counts = total - bound - (count - 1), [1] * (count - 1)
    while surplus > 0:
        movable = [i for i in range(count - 1) if counts[i] < bound]
        whole, budget = sum([portions[i] for i in movable]), surplus
        for i in movable:
            more = min(bound - counts[i], max(1, budget * portions[i] // whole), surplus)
            counts[i] = counts[i] + more
            surplus = surplus - more
    return np.array([bound] + counts)


def ragged(key, amount, total, limit, lean):
    if amount == 2:
        one = jax.random.randint(key, (), max(1, total - limit), min(limit, total - 1) + 1)
        return jnp.stack([one, total - one])
    tallies = jnp.asarray(length_profile(amount, total, limit, lean), jnp.int32)
    couples = (amount - 1) // 2
    source_of, taker = tallies[1:1 + 2 * couples:2], tallies[2:2 + 2 * couples:2]
    margin = jnp.minimum(source_of - 1, limit - taker)
    passed = jax.random.randint(jax.random.fold_in(key, 1), (couples,), 0, 1 << 20) % (margin + 1)
    tallies = tallies.at[1:1 + 2 * couples:2].set(source_of - passed).at[2:2 + 2 * couples:2].set(taker + passed)
    return tallies[jax.random.permutation(jax.random.fold_in(key, 2), amount)]


def centred(stream_key, extent, scale, most, split=(), kind=jnp.bfloat16):
    entries = jax.random.normal(stream_key, extent, jnp.float32) * scale
    if len(split) > 0:
        entries = shard_levels(stream_key, extent, split, -0.22, 0.18) * entries
    return jnp.clip(entries, min=-most, max=most).astype(kind)


def setup_inputs(seed: int = 0, part: int = 0) -> dict:
    streams_of = jax.random.split(jax.random.key(seed), 8)
    part_splits = jax.random.split(jax.random.fold_in(streams_of[7], part), 8)
    query_rows = draw_query_rows(jax.random.fold_in(jax.random.fold_in(streams_of[7], part), 71), part)
    key_rows = draw_key_rows(jax.random.fold_in(jax.random.fold_in(streams_of[7], part), 71), part)
    value_rows = centred(part_splits[2], (S, H * HD), 1.0, 8.0, ((0, 8), (1, 2)))
    clip_lengths = ragged(part_splits[3], CLIPS, S, S // 2, 2).astype(jnp.int32)
    block_mask = draw_block_mask(jax.random.fold_in(jax.random.fold_in(streams_of[7], part), 71), part)
    out_weight = draw_out_weight(jax.random.fold_in(streams_of[7], 71), part)
    norm_gain = jnp.clip(1.0 + 0.18 * jax.random.normal(streams_of[6], (D,), jnp.float32), 0.099609375, 1.8984375).astype(jnp.bfloat16)
    return {"query_rows": query_rows, "key_rows": key_rows, "value_rows": value_rows, "clip_lengths": clip_lengths, "block_mask": block_mask, "out_weight": out_weight, "norm_gain": norm_gain}


def clip_index(positions, clip_ends):
    return lax.optimization_barrier(jnp.sum((clip_ends[None, :] <= positions[:, None]).astype(jnp.int32), axis=1))

def reference(query_rows, key_rows, value_rows, clip_lengths, block_mask, out_weight, norm_gain):
    clip_ends = jnp.cumsum(clip_lengths).astype(jnp.int32)
    positions = jnp.arange(S, dtype=jnp.int32)
    clip_of_token = clip_index(positions, clip_ends)
    block_rows = math.gcd(S, 512)
    block_count = S // block_rows
    mask_height = block_rows // BLK
    score_scale = 1.0 / math.sqrt(HD)

    def one_block(flat_index):
        head_index = flat_index // block_count
        query_block = flat_index % block_count
        row_start = (query_block * block_rows).astype(jnp.int32)
        col_start = (head_index * HD).astype(jnp.int32)
        queries = lax.dynamic_slice(query_rows, (row_start, col_start), (block_rows, HD))
        keys_head = lax.dynamic_slice(key_rows, (jnp.int32(0), col_start), (S, HD))
        values_head = lax.dynamic_slice(value_rows, (jnp.int32(0), col_start), (S, HD))
        scores = jnp.dot(queries, keys_head.T, preferred_element_type=jnp.float32) * score_scale
        mask_part = lax.dynamic_slice_in_dim(block_mask, (query_block * mask_height).astype(jnp.int32), mask_height, 0)
        allowed = jnp.repeat(jnp.repeat(mask_part, BLK, axis=0), BLK, axis=1) == 1
        query_clip = lax.dynamic_slice_in_dim(clip_of_token, row_start, block_rows, 0)
        allowed = allowed & (query_clip[:, None] == clip_of_token[None, :])
        masked = jnp.where(allowed, scores, -1e+30)
        row_max = lax.optimization_barrier(jnp.max(masked, axis=1, keepdims=True))
        weights = jnp.where(allowed, jnp.exp(masked - row_max), 0.0)
        denominator = lax.optimization_barrier(jnp.sum(weights, axis=1, keepdims=True))
        numerator = jnp.dot(weights.astype(jnp.bfloat16), values_head, preferred_element_type=jnp.float32)
        return (numerator / denominator).astype(jnp.bfloat16)
    blocks = lax.map(one_block, jnp.arange(H * block_count, dtype=jnp.int32))
    attention = blocks.reshape(H, S, HD).transpose(1, 0, 2).reshape(S, H * HD)
    projected = jnp.dot(attention, out_weight, preferred_element_type=jnp.float32)
    zero_rows = jnp.zeros((F, D), projected.dtype)
    earlier = jnp.concatenate([zero_rows, projected[:-F]], axis=0)
    later = jnp.concatenate([projected[F:], zero_rows], axis=0)
    same_before = clip_index(positions - F, clip_ends) == clip_of_token
    same_after = clip_index(positions + F, clip_ends) == clip_of_token
    blended = projected + 0.5 * (jnp.where(same_before[:, None], earlier, 0.0) + jnp.where(same_after[:, None], later, 0.0))
    mean_square = lax.optimization_barrier(jnp.mean(blended * blended, axis=1, keepdims=True))
    return (blended * lax.rsqrt(mean_square + 1e-06) * norm_gain.astype(jnp.float32)).astype(jnp.bfloat16)
```

```python
import math

import jax
import jax.numpy as jnp
from jax import lax
from jax.sharding import PartitionSpec as P

HD = 64
BLK = 64
F = 64


def clip_index(positions, clip_ends):
    return jnp.sum((clip_ends[None, :] <= positions[:, None]).astype(jnp.int32), axis=1)


def shifted(x, axis, count, step):
    pairs = [(i + step, i) for i in range(count) if 0 <= i + step < count]
    return lax.ppermute(x, axis, pairs)


def rotated(x, axis, count, step):
    return lax.ppermute(x, axis, [(i, (i + step) % count) for i in range(count)])


def attend_chunk(state_now, per_head, query_clip, mask_float, clip_ends, keys, values, key_pos):
    row_count, head_count, _ = per_head.shape
    key_rows = keys.shape[0]
    block_total = mask_float.shape[1]
    one_hot = (
        (key_pos // BLK)[:, None] == jnp.arange(block_total, dtype=jnp.int32)[None, :]
    ).astype(jnp.float32)
    block_live = jnp.dot(mask_float, one_hot.T, precision=lax.Precision.HIGHEST) > 0.5
    allowed = jnp.repeat(block_live, BLK, axis=0) & (
        query_clip[:, None] == clip_index(key_pos, clip_ends)[None, :]
    )
    row_max, running, weighted = state_now
    scores = jnp.einsum(
        "rhd,khd->hrk",
        per_head,
        keys.reshape(key_rows, head_count, HD),
        preferred_element_type=jnp.float32,
    ) * (1.0 / math.sqrt(HD))
    scores = jnp.where(allowed[None], scores, -1e30)
    new_max = jnp.maximum(row_max, jnp.max(scores, axis=2))
    weights_now = jnp.where(allowed[None], jnp.exp(scores - new_max[:, :, None]), 0.0)
    rescale = jnp.exp(row_max - new_max)
    running = running * rescale + jnp.sum(weights_now, axis=2)
    update = jnp.einsum(
        "hrk,khd->rhd",
        weights_now.astype(jnp.bfloat16),
        values.reshape(key_rows, head_count, HD),
        preferred_element_type=jnp.float32,
    )
    weighted = weighted * jnp.repeat(rescale.T, HD, axis=1) + update.reshape(
        row_count, head_count * HD
    )
    return (new_max, running, weighted)


def body(query_rows, key_rows, value_rows, clip_lengths, block_mask, out_weight, norm_gain):
    row_count, col_count = query_rows.shape
    head_count = col_count // HD
    n_seq = lax.axis_size("seq")
    n_sub = lax.axis_size("sub")
    n_head = lax.axis_size("head")
    seq_i = lax.axis_index("seq")
    sub_i = lax.axis_index("sub")
    head_i = lax.axis_index("head")
    chip_rows = row_count * n_sub
    total = chip_rows * n_seq
    longest = total // 2
    reach = min(n_seq - 1, 1 + (longest - 2) // chip_rows)

    clip_ends = jnp.cumsum(clip_lengths)
    token_first = (seq_i * n_sub + sub_i) * row_count
    mask_height = row_count // BLK
    mask_rows = lax.dynamic_slice_in_dim(block_mask, sub_i * mask_height, mask_height, 0)
    mask_float = mask_rows.astype(jnp.float32)
    per_head = query_rows.reshape(row_count, head_count, HD)
    query_clip = clip_index(token_first + jnp.arange(row_count, dtype=jnp.int32), clip_ends)
    local_pos = jnp.arange(row_count, dtype=jnp.int32)

    def block_pos(seq_off, sub_src):
        return ((seq_i + seq_off) * n_sub + sub_src) * row_count + local_pos

    def partner_blocks(blocks):
        stacked = jnp.stack([kv for kv, _ in blocks])
        out = []
        for j in range(1, n_sub):
            got = rotated(stacked, "sub", n_sub, j)
            src = (sub_i - j) % n_sub
            out += [(got[b], off, src) for b, (_, off) in enumerate(blocks)]
        return out

    state = (
        jnp.full((head_count, row_count), -1e30, jnp.float32),
        jnp.zeros((head_count, row_count), jnp.float32),
        jnp.zeros((row_count, col_count), jnp.float32),
    )

    def fold(state_now, chunk):
        keys = jnp.concatenate([kv[0] for kv, _, _ in chunk], axis=0)
        values = jnp.concatenate([kv[1] for kv, _, _ in chunk], axis=0)
        key_pos = jnp.concatenate([block_pos(off, src) for _, off, src in chunk], axis=0)
        return attend_chunk(
            state_now, per_head, query_clip, mask_float, clip_ends, keys, values, key_pos
        )

    own = jnp.stack([key_rows, value_rows])
    mine = [(own, 0)]
    state = fold(state, [(own, 0, sub_i)] + partner_blocks(mine))

    def seq_step(step, carry):
        state_now, left, right = carry
        right = shifted(right, "seq", n_seq, 1)
        left = shifted(left, "seq", n_seq, -1)
        mine = [(left, -step), (right, step)]
        chunk = [(left, -step, sub_i), (right, step, sub_i)] + partner_blocks(mine)
        return (fold(state_now, chunk), left, right)

    carry = (state, own, own)
    if reach <= 4:
        for step in range(1, reach + 1):
            carry = seq_step(step, carry)
    else:
        carry = lax.fori_loop(1, reach + 1, seq_step, carry)
    state = carry[0]

    row_max, running, weighted = state
    attended = (weighted / jnp.repeat(running.T, HD, axis=1)).astype(jnp.bfloat16)

    n_dev = n_seq * n_sub
    prev_tail = shifted(attended[row_count - F :], ("seq", "sub"), n_dev, -1)
    next_head = shifted(attended[:F], ("seq", "sub"), n_dev, 1)
    extended = jnp.concatenate([prev_tail, attended, next_head], axis=0)

    projected = jnp.dot(
        extended,
        lax.dynamic_slice_in_dim(out_weight, head_i * col_count, col_count, 0),
        preferred_element_type=jnp.float32,
    )
    for j in range(1, n_head):
        got = rotated(extended, "head", n_head, j)
        src = (head_i - j) % n_head
        projected = projected + jnp.dot(
            got,
            lax.dynamic_slice_in_dim(out_weight, src * col_count, col_count, 0),
            preferred_element_type=jnp.float32,
        )

    positions = token_first + jnp.arange(row_count, dtype=jnp.int32)
    clip_here = clip_index(positions, clip_ends)
    earlier = jnp.where(
        (clip_index(positions - F, clip_ends) == clip_here)[:, None], projected[:row_count], 0.0
    )
    later = jnp.where(
        (clip_index(positions + F, clip_ends) == clip_here)[:, None], projected[2 * F :], 0.0
    )
    blended = projected[F : F + row_count] + 0.5 * (earlier + later)
    width = out_weight.shape[1]
    squares = jnp.sum(blended * blended, axis=1)
    scale = lax.rsqrt(squares / width + 1e-06)
    own_cols = lax.dynamic_slice_in_dim(blended, head_i * col_count, col_count, 1)
    return (own_cols * scale[:, None] * norm_gain.astype(jnp.float32)).astype(jnp.bfloat16)


def solution(mesh):
    placed = (
        P(("grp", "seq", "sub"), "head"),
        P(("grp", "seq", "sub"), "head"),
        P(("grp", "seq", "sub"), "head"),
        P("grp"),
        P(("grp", "seq"), None),
        P(),
        P("head"),
    )
    return jax.shard_map(
        body,
        mesh=mesh,
        in_specs=placed,
        out_specs=P(("grp", "seq", "sub"), "head"),
        check_vma=False,
    )
```

```python
import functools
import math

import jax
import jax.numpy as jnp
from jax.experimental import pallas as pl
from jax.experimental.pallas import tpu as pltpu
from jax import lax
from jax.sharding import PartitionSpec as P

HD = 64
BLK = 64
F = 64


def clip_index(positions, clip_ends):
    return jnp.sum((clip_ends[None, :] <= positions[:, None]).astype(jnp.int32), axis=1)


def shifted(x, axis, count, step):
    pairs = [(i + step, i) for i in range(count) if 0 <= i + step < count]
    return lax.ppermute(x, axis, pairs)


def rotated(x, axis, count, step):
    return lax.ppermute(x, axis, [(i, (i + step) % count) for i in range(count)])


def chunk_kernel(sources, head_count, flags_ref, q_ref, qclip_ref, code_ref, *refs):
    block_count = len(sources)
    n_in = max(s for s, _ in sources) + 1
    kv_refs = refs[:n_in]
    m_ref, l_ref, acc_ref = refs[n_in + 3 :]
    row_count = q_ref.shape[0]
    sub_rows = code_ref.shape[1]
    piece = row_count // sub_rows
    scale = 1.0 / math.sqrt(HD)
    first = refs[n_in : n_in + 3]
    m_ref[...] = first[0][...]
    l_ref[...] = first[1][...]
    acc_ref[...] = first[2][...]
    qclip = qclip_ref[...]
    for b, (src, idx) in enumerate(sources):

        @pl.when(flags_ref[b] > 0)
        def _():
            code = code_ref[b]
            allowed = jnp.concatenate(
                [
                    jnp.broadcast_to(
                        qclip[i * piece : (i + 1) * piece] == code[i : i + 1, :],
                        (piece, code.shape[1]),
                    )
                    for i in range(sub_rows)
                ],
                axis=0,
            )
            bias = jnp.where(allowed, 0.0, -1e30).astype(jnp.float32)
            for h in range(head_count):
                cols = slice(h * HD, (h + 1) * HD)
                q_h = q_ref[:, cols]
                k_h = kv_refs[src][idx, 0, :, cols]
                v_h = kv_refs[src][idx, 1, :, cols]
                s = lax.dot_general(
                    q_h, k_h, (((1,), (1,)), ((), ())), preferred_element_type=jnp.float32
                )
                s = s * scale + bias
                m_old = m_ref[:, h : h + 1]
                m_new = jnp.maximum(m_old, jnp.max(s, axis=1, keepdims=True))
                alpha = jnp.exp(m_old - m_new)
                p = jnp.exp(s - m_new)
                l_ref[:, h : h + 1] = alpha * l_ref[:, h : h + 1] + jnp.sum(p, axis=1, keepdims=True)
                pv = jnp.dot(p.astype(jnp.bfloat16), v_h, preferred_element_type=jnp.float32)
                acc_ref[:, cols] = alpha * acc_ref[:, cols] + pv
                m_ref[:, h : h + 1] = m_new


def attend_chunk(state_now, query_rows, query_clip, mask_rows, clip_ends, total, inputs, blocks):
    row_count, col_count = query_rows.shape
    head_count = col_count // HD
    block_total = mask_rows.shape[1]
    sub_rows = mask_rows.shape[0]
    key_pos = jnp.stack([pos for _, _, pos in blocks])
    key_block = key_pos // BLK
    valid = (key_pos >= 0) & (key_pos < total)
    live = jnp.take(mask_rows, jnp.clip(key_block, 0, block_total - 1), axis=1)
    live = (live == 1) & valid[None]
    key_clip = clip_index(key_pos.reshape(-1), clip_ends).reshape(key_pos.shape)
    code = jnp.where(live, key_clip[None], -1).transpose(1, 0, 2)
    query_sub = query_clip.reshape(sub_rows, -1)
    flags = jnp.any(
        query_sub[None, :, :, None] == code[:, :, None, :], axis=(1, 2, 3)
    ).astype(jnp.int32)
    sources = tuple((src, idx) for src, idx, _ in blocks)
    m, l, acc = state_now
    n_in = len(inputs)
    return pl.pallas_call(
        functools.partial(chunk_kernel, sources, head_count),
        out_shape=(
            jax.ShapeDtypeStruct(m.shape, m.dtype),
            jax.ShapeDtypeStruct(l.shape, l.dtype),
            jax.ShapeDtypeStruct(acc.shape, acc.dtype),
        ),
        in_specs=[pl.BlockSpec(memory_space=pltpu.SMEM)]
        + [pl.BlockSpec(memory_space=pltpu.VMEM)] * (3 + n_in + 3),
        out_specs=[pl.BlockSpec(memory_space=pltpu.VMEM)] * 3,
        input_output_aliases={4 + n_in: 0, 5 + n_in: 1, 6 + n_in: 2},
    )(flags, query_rows, query_clip[:, None], code, *inputs, m, l, acc)


def body(query_rows, key_rows, value_rows, clip_lengths, block_mask, out_weight, norm_gain):
    row_count, col_count = query_rows.shape
    head_count = col_count // HD
    n_seq = lax.axis_size("seq")
    n_sub = lax.axis_size("sub")
    n_head = lax.axis_size("head")
    seq_i = lax.axis_index("seq")
    sub_i = lax.axis_index("sub")
    head_i = lax.axis_index("head")
    chip_rows = row_count * n_sub
    total = chip_rows * n_seq
    longest = total // 2
    reach = min(n_seq - 1, 1 + (longest - 2) // chip_rows)

    clip_ends = jnp.cumsum(clip_lengths)
    token_first = (seq_i * n_sub + sub_i) * row_count
    mask_height = row_count // BLK
    mask_rows = lax.dynamic_slice_in_dim(block_mask, sub_i * mask_height, mask_height, 0)
    query_clip = clip_index(token_first + jnp.arange(row_count, dtype=jnp.int32), clip_ends)
    local_pos = jnp.arange(row_count, dtype=jnp.int32)

    def block_pos(seq_off, sub_src):
        return ((seq_i + seq_off) * n_sub + sub_src) * row_count + local_pos

    state = (
        jnp.full((row_count, head_count), -1e30, jnp.float32),
        jnp.zeros((row_count, head_count), jnp.float32),
        jnp.zeros((row_count, col_count), jnp.float32),
    )

    def fold(state_now, mine):
        inputs = [kv[None] for kv, _ in mine]
        blocks = [(n, 0, block_pos(off, sub_i)) for n, (_, off) in enumerate(mine)]
        stacked = jnp.stack([kv for kv, _ in mine])
        for j in range(1, n_sub):
            got = rotated(stacked, "sub", n_sub, j)
            src = (sub_i - j) % n_sub
            blocks += [(len(inputs), b, block_pos(off, src)) for b, (_, off) in enumerate(mine)]
            inputs.append(got)
        return attend_chunk(
            state_now, query_rows, query_clip, mask_rows, clip_ends, total, inputs, blocks
        )

    own = jnp.stack([key_rows, value_rows])
    state = fold(state, [(own, 0)])

    def seq_step(step, carry):
        state_now, left, right = carry
        right = shifted(right, "seq", n_seq, 1)
        left = shifted(left, "seq", n_seq, -1)
        return (fold(state_now, [(left, -step), (right, step)]), left, right)

    carry = (state, own, own)
    if reach <= 4:
        for step in range(1, reach + 1):
            carry = seq_step(step, carry)
    else:
        carry = lax.fori_loop(1, reach + 1, seq_step, carry)
    state = carry[0]

    row_max, running, weighted = state
    attended = (weighted / jnp.repeat(running, HD, axis=1)).astype(jnp.bfloat16)

    n_dev = n_seq * n_sub
    prev_tail = shifted(attended[row_count - F :], ("seq", "sub"), n_dev, -1)
    next_head = shifted(attended[:F], ("seq", "sub"), n_dev, 1)
    extended = jnp.concatenate([prev_tail, attended, next_head], axis=0)

    projected = jnp.dot(
        extended,
        lax.dynamic_slice_in_dim(out_weight, head_i * col_count, col_count, 0),
        preferred_element_type=jnp.float32,
    )
    for j in range(1, n_head):
        got = rotated(extended, "head", n_head, j)
        src = (head_i - j) % n_head
        projected = projected + jnp.dot(
            got,
            lax.dynamic_slice_in_dim(out_weight, src * col_count, col_count, 0),
            preferred_element_type=jnp.float32,
        )

    positions = token_first + jnp.arange(row_count, dtype=jnp.int32)
    clip_here = clip_index(positions, clip_ends)
    earlier = jnp.where(
        (clip_index(positions - F, clip_ends) == clip_here)[:, None], projected[:row_count], 0.0
    )
    later = jnp.where(
        (clip_index(positions + F, clip_ends) == clip_here)[:, None], projected[2 * F :], 0.0
    )
    blended = projected[F : F + row_count] + 0.5 * (earlier + later)
    width = out_weight.shape[1]
    squares = jnp.sum(blended * blended, axis=1)
    scale = lax.rsqrt(squares / width + 1e-06)
    own_cols = lax.dynamic_slice_in_dim(blended, head_i * col_count, col_count, 1)
    return (own_cols * scale[:, None] * norm_gain.astype(jnp.float32)).astype(jnp.bfloat16)


def solution(mesh):
    placed = (
        P(("grp", "seq", "sub"), "head"),
        P(("grp", "seq", "sub"), "head"),
        P(("grp", "seq", "sub"), "head"),
        P("grp"),
        P(("grp", "seq"), None),
        P(),
        P("head"),
    )
    return jax.shard_map(
        body,
        mesh=mesh,
        in_specs=placed,
        out_specs=P(("grp", "seq", "sub"), "head"),
        check_vma=False,
    )
```

```python
import functools
import math

import jax
import jax.numpy as jnp
from jax.experimental import pallas as pl
from jax.experimental.pallas import tpu as pltpu
from jax import lax
from jax.sharding import PartitionSpec as P

HD = 64
BLK = 64
F = 64


def clip_index(positions, clip_ends):
    return jnp.sum((clip_ends[None, :] <= positions[:, None]).astype(jnp.int32), axis=1)


def shifted(x, axis, count, step):
    pairs = [(i + step, i) for i in range(count) if 0 <= i + step < count]
    return lax.ppermute(x, axis, pairs)


def rotated(x, axis, count, step):
    return lax.ppermute(x, axis, [(i, (i + step) % count) for i in range(count)])


def chunk_kernel(sources, flags_ref, q_ref, code_ref, qclip_ref, *refs):
    n_in = max(src for src, _ in sources) + 1
    kv_refs = refs[:n_in]
    m_in, l_in, acc_in = refs[n_in : n_in + 3]
    m_ref, l_ref, acc_ref = refs[n_in + 3 :]
    row_count, col_count = acc_ref.shape
    sub_rows = code_ref.shape[1]
    piece = row_count // sub_rows
    pair = 2 * HD
    scale = 1.0 / math.sqrt(HD)
    m_ref[...] = m_in[...]
    l_ref[...] = l_in[...]
    acc_ref[...] = acc_in[...]
    qclip = qclip_ref[...]
    low = lax.broadcasted_iota(jnp.int32, (row_count, pair), 1) < HD
    for b, (src, idx) in enumerate(sources):

        @pl.when(flags_ref[b] > 0)
        def _():
            code = code_ref[b]
            allowed = jnp.concatenate(
                [
                    jnp.broadcast_to(
                        qclip[i * piece : (i + 1) * piece] == code[i : i + 1, :],
                        (piece, code.shape[1]),
                    )
                    for i in range(sub_rows)
                ],
                axis=0,
            )
            bias = jnp.where(allowed, 0.0, -1e30).astype(jnp.float32)
            for hp in range(col_count // pair):
                cols = slice(hp * pair, (hp + 1) * pair)
                k_p = kv_refs[src][idx, 0, :, cols]
                v_p = kv_refs[src][idx, 1, :, cols]
                m_p = m_ref[:, cols]
                halves = []
                for e in range(2):
                    q_e = q_ref[e, :, cols]
                    s = lax.dot_general(
                        q_e, k_p, (((1,), (1,)), ((), ())), preferred_element_type=jnp.float32
                    )
                    s = s * scale + bias
                    m_old = m_p[:, e * HD : e * HD + 1]
                    m_new = jnp.maximum(m_old, jnp.max(s, axis=1, keepdims=True))
                    alpha = jnp.exp(m_old - m_new)
                    p = jnp.exp(s - m_new)
                    total = jnp.sum(p, axis=1, keepdims=True)
                    pv = jnp.dot(p.astype(jnp.bfloat16), v_p, preferred_element_type=jnp.float32)
                    halves.append((m_new, alpha, total, pv))
                (m0, a0, t0, pv0), (m1, a1, t1, pv1) = halves
                alpha = jnp.where(low, a0, a1)
                m_ref[:, cols] = jnp.where(low, m0, m1)
                l_ref[:, cols] = alpha * l_ref[:, cols] + jnp.where(low, t0, t1)
                acc_ref[:, cols] = alpha * acc_ref[:, cols] + jnp.where(low, pv0, pv1)


def attend_chunk(state_now, q_split, query_clip, mask_rows, clip_ends, total, inputs, blocks):
    block_total = mask_rows.shape[1]
    sub_rows = mask_rows.shape[0]
    key_pos = jnp.stack([pos for _, _, pos in blocks])
    key_block = key_pos // BLK
    valid = (key_pos >= 0) & (key_pos < total)
    live = jnp.take(mask_rows, jnp.clip(key_block, 0, block_total - 1), axis=1)
    live = (live == 1) & valid[None]
    key_clip = clip_index(key_pos.reshape(-1), clip_ends).reshape(key_pos.shape)
    code = jnp.where(live, key_clip[None], -1).transpose(1, 0, 2)
    query_sub = query_clip.reshape(sub_rows, -1)
    flags = jnp.any(
        query_sub[None, :, :, None] == code[:, :, None, :], axis=(1, 2, 3)
    ).astype(jnp.int32)
    sources = tuple((src, idx) for src, idx, _ in blocks)
    n_in = len(inputs)
    return pl.pallas_call(
        functools.partial(chunk_kernel, sources),
        out_shape=tuple(jax.ShapeDtypeStruct(x.shape, x.dtype) for x in state_now),
        in_specs=[pl.BlockSpec(memory_space=pltpu.SMEM)]
        + [pl.BlockSpec(memory_space=pltpu.VMEM)] * (3 + n_in + 3),
        out_specs=[pl.BlockSpec(memory_space=pltpu.VMEM)] * 3,
        input_output_aliases={4 + n_in: 0, 5 + n_in: 1, 6 + n_in: 2},
        cost_estimate=pl.CostEstimate(
            flops=len(blocks) * 8 * q_split.shape[1] ** 2 * q_split.shape[2],
            transcendentals=len(blocks) * 2 * q_split.shape[1] ** 2 * q_split.shape[2] // HD,
            bytes_accessed=sum(x.size * x.dtype.itemsize for x in inputs) + 8 * q_split.size,
        ),
    )(flags, q_split, code, query_clip[:, None], *inputs, *state_now)


def body(query_rows, key_rows, value_rows, clip_lengths, block_mask, out_weight, norm_gain):
    row_count, col_count = query_rows.shape
    head_count = col_count // HD
    n_seq = lax.axis_size("seq")
    n_sub = lax.axis_size("sub")
    n_head = lax.axis_size("head")
    seq_i = lax.axis_index("seq")
    sub_i = lax.axis_index("sub")
    head_i = lax.axis_index("head")
    chip_rows = row_count * n_sub
    total = chip_rows * n_seq
    longest = total // 2
    reach = min(n_seq - 1, 1 + (longest - 2) // chip_rows)

    clip_ends = jnp.cumsum(clip_lengths)
    token_first = (seq_i * n_sub + sub_i) * row_count
    mask_height = row_count // BLK
    mask_rows = lax.dynamic_slice_in_dim(block_mask, sub_i * mask_height, mask_height, 0)
    query_clip = clip_index(token_first + jnp.arange(row_count, dtype=jnp.int32), clip_ends)
    local_pos = jnp.arange(row_count, dtype=jnp.int32)

    def block_pos(seq_off, sub_src):
        return ((seq_i + seq_off) * n_sub + sub_src) * row_count + local_pos

    state = (
        jnp.full((row_count, col_count), -1e30, jnp.float32),
        jnp.zeros((row_count, col_count), jnp.float32),
        jnp.zeros((row_count, col_count), jnp.float32),
    )
    lane = lax.broadcasted_iota(jnp.int32, (1, col_count), 1) % (2 * HD)
    q_split = jnp.stack(
        [jnp.where(lane < HD, query_rows, 0), jnp.where(lane >= HD, query_rows, 0)]
    ).astype(jnp.bfloat16)

    def fold(state_now, mine, theirs):
        inputs = [kv[None] for kv, _ in mine]
        blocks = [(n, 0, block_pos(off, sub_i)) for n, (_, off) in enumerate(mine)]
        for got, offs, src in theirs:
            blocks += [(len(inputs), b, block_pos(off, src)) for b, off in enumerate(offs)]
            inputs.append(got)
        return attend_chunk(
            state_now, q_split, query_clip, mask_rows, clip_ends, total, inputs, blocks
        )

    def to_partner(mine):
        stacked = jnp.stack([kv for kv, _ in mine])
        offs = [jnp.asarray(off, jnp.int32) for _, off in mine]
        return [
            (rotated(stacked, "sub", n_sub, j), offs, (sub_i - j) % n_sub)
            for j in range(1, n_sub)
        ]

    own = jnp.stack([key_rows, value_rows])
    state = fold(state, [(own, 0)], [])
    pending = to_partner([(own, 0)])

    def seq_step(step, carry):
        state_now, left, right, pending_now = carry
        right = shifted(right, "seq", n_seq, 1)
        left = shifted(left, "seq", n_seq, -1)
        mine = [(left, -step), (right, step)]
        state_now = fold(state_now, mine, pending_now)
        return (state_now, left, right, to_partner(mine))

    carry = seq_step(1, (state, own, own, pending))
    if reach <= 4:
        for step in range(2, reach + 1):
            carry = seq_step(step, carry)
    else:
        carry = lax.fori_loop(2, reach + 1, seq_step, carry)
    state = fold(carry[0], [], carry[3])
    row_max, running, weighted = state
    attended = (weighted / running).astype(jnp.bfloat16)

    n_dev = n_seq * n_sub
    prev_tail = shifted(attended[row_count - F :], ("seq", "sub"), n_dev, -1)
    next_head = shifted(attended[:F], ("seq", "sub"), n_dev, 1)
    extended = jnp.concatenate([prev_tail, attended, next_head], axis=0)

    projected = jnp.dot(
        extended,
        lax.dynamic_slice_in_dim(out_weight, head_i * col_count, col_count, 0),
        preferred_element_type=jnp.float32,
    )
    for j in range(1, n_head):
        got = rotated(extended, "head", n_head, j)
        src = (head_i - j) % n_head
        projected = projected + jnp.dot(
            got,
            lax.dynamic_slice_in_dim(out_weight, src * col_count, col_count, 0),
            preferred_element_type=jnp.float32,
        )

    positions = token_first + jnp.arange(row_count, dtype=jnp.int32)
    clip_here = clip_index(positions, clip_ends)
    earlier = jnp.where(
        (clip_index(positions - F, clip_ends) == clip_here)[:, None], projected[:row_count], 0.0
    )
    later = jnp.where(
        (clip_index(positions + F, clip_ends) == clip_here)[:, None], projected[2 * F :], 0.0
    )
    blended = projected[F : F + row_count] + 0.5 * (earlier + later)
    width = out_weight.shape[1]
    squares = jnp.sum(blended * blended, axis=1)
    scale = lax.rsqrt(squares / width + 1e-06)
    own_cols = lax.dynamic_slice_in_dim(blended, head_i * col_count, col_count, 1)
    return (own_cols * scale[:, None] * norm_gain.astype(jnp.float32)).astype(jnp.bfloat16)


def solution(mesh):
    placed = (
        P(("grp", "seq", "sub"), "head"),
        P(("grp", "seq", "sub"), "head"),
        P(("grp", "seq", "sub"), "head"),
        P("grp"),
        P(("grp", "seq"), None),
        P(),
        P("head"),
    )
    return jax.shard_map(
        body,
        mesh=mesh,
        in_specs=placed,
        out_specs=P(("grp", "seq", "sub"), "head"),
        check_vma=False,
    )
```

```python
import functools
import math

import jax
import jax.numpy as jnp
from jax.experimental import pallas as pl
from jax.experimental.pallas import tpu as pltpu
from jax import lax
from jax.sharding import PartitionSpec as P

HD = 64
BLK = 64
F = 64


def clip_index(positions, clip_ends):
    return jnp.sum((clip_ends[None, :] <= positions[:, None]).astype(jnp.int32), axis=1)


def shifted(x, axis, count, step):
    pairs = [(i + step, i) for i in range(count) if 0 <= i + step < count]
    return lax.ppermute(x, axis, pairs)


def rotated(x, axis, count, step):
    return lax.ppermute(x, axis, [(i, (i + step) % count) for i in range(count)])


def chunk_kernel(sources, has_state, final, flags_ref, q_ref, code_ref, qclip_ref, *refs):
    n_in = max(src for src, _ in sources) + 1
    kv_refs = refs[:n_in]
    rest = refs[n_in:]
    if has_state:
        m_in, l_in, acc_in = rest[:3]
        rest = rest[3:]
    if final:
        out_ref, m_ref, l_ref, acc_ref = rest
    else:
        m_ref, l_ref, acc_ref = rest
    row_count, col_count = acc_ref.shape
    sub_rows = code_ref.shape[1]
    piece = row_count // sub_rows
    pair = 2 * HD
    scale = 1.0 / math.sqrt(HD)
    if has_state:
        m_ref[...] = m_in[...]
        l_ref[...] = l_in[...]
        acc_ref[...] = acc_in[...]
    else:
        m_ref[...] = jnp.full(m_ref.shape, -1e30, jnp.float32)
        l_ref[...] = jnp.zeros(l_ref.shape, jnp.float32)
        acc_ref[...] = jnp.zeros(acc_ref.shape, jnp.float32)
    qclip = qclip_ref[...]
    low = lax.broadcasted_iota(jnp.int32, (row_count, pair), 1) < HD
    for b, (src, idx) in enumerate(sources):

        @pl.when(flags_ref[b] > 0)
        def _():
            code = code_ref[b]
            allowed = jnp.concatenate(
                [
                    jnp.broadcast_to(
                        qclip[i * piece : (i + 1) * piece] == code[i : i + 1, :],
                        (piece, code.shape[1]),
                    )
                    for i in range(sub_rows)
                ],
                axis=0,
            )
            bias = jnp.where(allowed, 0.0, -1e30).astype(jnp.float32)
            for hp in range(col_count // pair):
                cols = slice(hp * pair, (hp + 1) * pair)
                k_p = kv_refs[src][idx, 0, :, cols]
                v_p = kv_refs[src][idx, 1, :, cols]
                m_p = m_ref[:, cols]
                halves = []
                for e in range(2):
                    q_e = q_ref[e, :, cols]
                    s = lax.dot_general(
                        q_e, k_p, (((1,), (1,)), ((), ())), preferred_element_type=jnp.float32
                    )
                    s = s * scale + bias
                    m_old = m_p[:, e * HD : e * HD + 1]
                    m_new = jnp.maximum(m_old, jnp.max(s, axis=1, keepdims=True))
                    alpha = jnp.exp(m_old - m_new)
                    p = jnp.exp(s - m_new)
                    total = jnp.sum(p, axis=1, keepdims=True)
                    pv = jnp.dot(p.astype(jnp.bfloat16), v_p, preferred_element_type=jnp.float32)
                    halves.append((m_new, alpha, total, pv))
                (m0, a0, t0, pv0), (m1, a1, t1, pv1) = halves
                alpha = jnp.where(low, a0, a1)
                m_ref[:, cols] = jnp.where(low, m0, m1)
                l_ref[:, cols] = alpha * l_ref[:, cols] + jnp.where(low, t0, t1)
                acc_ref[:, cols] = alpha * acc_ref[:, cols] + jnp.where(low, pv0, pv1)

    if final:
        out_ref[...] = (acc_ref[...] / l_ref[...]).astype(out_ref.dtype)


def attend_chunk(state_now, q_split, query_clip, mask_rows, clip_ends, total, inputs, blocks):
    block_total = mask_rows.shape[1]
    sub_rows = mask_rows.shape[0]
    key_pos = jnp.stack([pos for _, _, pos in blocks])
    key_block = key_pos // BLK
    valid = (key_pos >= 0) & (key_pos < total)
    live = jnp.take(mask_rows, jnp.clip(key_block, 0, block_total - 1), axis=1)
    live = (live == 1) & valid[None]
    key_clip = clip_index(key_pos.reshape(-1), clip_ends).reshape(key_pos.shape)
    code = jnp.where(live, key_clip[None], -1).transpose(1, 0, 2)
    query_sub = query_clip.reshape(sub_rows, -1)
    flags = jnp.any(
        query_sub[None, :, :, None] == code[:, :, None, :], axis=(1, 2, 3)
    ).astype(jnp.int32)
    sources = tuple((src, idx) for src, idx, _ in blocks)
    n_in = len(inputs)
    has_state = state_now is not None
    final = not has_state
    row_count, col_count = q_split.shape[1:]
    state_shape = jax.ShapeDtypeStruct((row_count, col_count), jnp.float32)
    if final:
        out_shape = jax.ShapeDtypeStruct((row_count, col_count), jnp.bfloat16)
        out_specs = pl.BlockSpec(memory_space=pltpu.VMEM)
        scratch = [pltpu.VMEM((row_count, col_count), jnp.float32)] * 3
        aliases = {}
        extra = ()
    else:
        out_shape = (state_shape,) * 3
        out_specs = [pl.BlockSpec(memory_space=pltpu.VMEM)] * 3
        scratch = []
        aliases = {4 + n_in: 0, 5 + n_in: 1, 6 + n_in: 2}
        extra = tuple(state_now)
    return pl.pallas_call(
        functools.partial(chunk_kernel, sources, has_state, final),
        out_shape=out_shape,
        in_specs=[pl.BlockSpec(memory_space=pltpu.SMEM)]
        + [pl.BlockSpec(memory_space=pltpu.VMEM)] * (3 + n_in + len(extra)),
        out_specs=out_specs,
        scratch_shapes=scratch,
        input_output_aliases=aliases,
        cost_estimate=pl.CostEstimate(
            flops=len(blocks) * 8 * row_count**2 * col_count,
            transcendentals=len(blocks) * 2 * row_count**2 * col_count // HD,
            bytes_accessed=sum(x.size * x.dtype.itemsize for x in inputs) + 8 * q_split.size,
        ),
    )(flags, q_split, code, query_clip[:, None], *inputs, *extra)


def body(query_rows, key_rows, value_rows, clip_lengths, block_mask, out_weight, norm_gain):
    row_count, col_count = query_rows.shape
    head_count = col_count // HD
    n_seq = lax.axis_size("seq")
    n_sub = lax.axis_size("sub")
    n_head = lax.axis_size("head")
    seq_i = lax.axis_index("seq")
    sub_i = lax.axis_index("sub")
    head_i = lax.axis_index("head")
    chip_rows = row_count * n_sub
    total = chip_rows * n_seq
    longest = total // 2
    reach = min(n_seq - 1, 1 + (longest - 2) // chip_rows)

    clip_ends = jnp.cumsum(clip_lengths)
    token_first = (seq_i * n_sub + sub_i) * row_count
    mask_height = row_count // BLK
    mask_rows = lax.dynamic_slice_in_dim(block_mask, sub_i * mask_height, mask_height, 0)
    query_clip = clip_index(token_first + jnp.arange(row_count, dtype=jnp.int32), clip_ends)
    local_pos = jnp.arange(row_count, dtype=jnp.int32)

    def block_pos(seq_off, sub_src):
        return ((seq_i + seq_off) * n_sub + sub_src) * row_count + local_pos

    lane = lax.broadcasted_iota(jnp.int32, (1, col_count), 1) % (2 * HD)
    q_split = jnp.stack(
        [jnp.where(lane < HD, query_rows, 0), jnp.where(lane >= HD, query_rows, 0)]
    ).astype(jnp.bfloat16)

    def fold(state_now, mine, theirs):
        inputs = [kv[None] for kv, _ in mine]
        blocks = [(n, 0, block_pos(off, sub_i)) for n, (_, off) in enumerate(mine)]
        for got, offs, src in theirs:
            blocks += [(len(inputs), b, block_pos(off, src)) for b, off in enumerate(offs)]
            inputs.append(got)
        return attend_chunk(
            state_now, q_split, query_clip, mask_rows, clip_ends, total, inputs, blocks
        )

    def to_partner(mine):
        offs = [jnp.asarray(off, jnp.int32) for _, off in mine]
        return [
            (jnp.stack([rotated(kv, "sub", n_sub, j) for kv, _ in mine]), offs, (sub_i - j) % n_sub)
            for j in range(1, n_sub)
        ]

    own = jnp.stack([key_rows, value_rows])
    if reach <= 4:
        mine = [(own, 0)]
        theirs = to_partner(mine)
        left = own
        right = own
        for step in range(1, reach + 1):
            right = shifted(right, "seq", n_seq, 1)
            left = shifted(left, "seq", n_seq, -1)
            near = [(left, -step), (right, step)]
            mine += near
            theirs += to_partner(near)
        attended = fold(None, mine, theirs)
    else:
        state = (
            jnp.full((row_count, col_count), -1e30, jnp.float32),
            jnp.zeros((row_count, col_count), jnp.float32),
            jnp.zeros((row_count, col_count), jnp.float32),
        )
        state = fold(state, [(own, 0)], [])
        pending = to_partner([(own, 0)])

        def seq_step(step, carry):
            state_now, left, right, pending_now = carry
            right = shifted(right, "seq", n_seq, 1)
            left = shifted(left, "seq", n_seq, -1)
            near = [(left, -step), (right, step)]
            state_now = fold(state_now, near, pending_now)
            return (state_now, left, right, to_partner(near))

        carry = seq_step(1, (state, own, own, pending))
        carry = lax.fori_loop(2, reach + 1, seq_step, carry)
        state = fold(carry[0], [], carry[3])
        row_max, running, weighted = state
        attended = (weighted / running).astype(jnp.bfloat16)

    n_dev = n_seq * n_sub

    def flat(dev, head):
        return ((dev // n_sub) * n_head + head) * n_sub + dev % n_sub

    pieces = {-1: attended[row_count - F :], 0: attended, 1: attended[:F]}
    width = out_weight.shape[1]
    projected = jnp.zeros((row_count + 2 * F, width), jnp.float32)
    for j in range(n_head):
        parts = []
        for d in (-1, 0, 1):
            if j == 0 and d == 0:
                parts.append(attended)
                continue
            pairs = [
                (flat(i + d, (h + j) % n_head), flat(i, h))
                for i in range(n_dev)
                for h in range(n_head)
                if 0 <= i + d < n_dev
            ]
            parts.append(lax.ppermute(pieces[d], ("seq", "head", "sub"), pairs))
        src = (head_i + j) % n_head
        projected = projected + jnp.dot(
            jnp.concatenate(parts, axis=0),
            lax.dynamic_slice_in_dim(out_weight, src * col_count, col_count, 0),
            preferred_element_type=jnp.float32,
        )

    positions = token_first + jnp.arange(row_count, dtype=jnp.int32)
    clip_here = clip_index(positions, clip_ends)
    earlier = jnp.where(
        (clip_index(positions - F, clip_ends) == clip_here)[:, None], projected[:row_count], 0.0
    )
    later = jnp.where(
        (clip_index(positions + F, clip_ends) == clip_here)[:, None], projected[2 * F :], 0.0
    )
    blended = projected[F : F + row_count] + 0.5 * (earlier + later)
    squares = jnp.sum(blended * blended, axis=1)
    scale = lax.rsqrt(squares / width + 1e-06)
    own_cols = lax.dynamic_slice_in_dim(blended, head_i * col_count, col_count, 1)
    return (own_cols * scale[:, None] * norm_gain.astype(jnp.float32)).astype(jnp.bfloat16)


def solution(mesh):
    placed = (
        P(("grp", "seq", "sub"), "head"),
        P(("grp", "seq", "sub"), "head"),
        P(("grp", "seq", "sub"), "head"),
        P("grp"),
        P(("grp", "seq"), None),
        P(),
        P("head"),
    )
    return jax.shard_map(
        body,
        mesh=mesh,
        in_specs=placed,
        out_specs=P(("grp", "seq", "sub"), "head"),
        check_vma=False,
    )
```

```python
import functools
import math

import jax
import jax.numpy as jnp
from jax.experimental import pallas as pl
from jax.experimental.pallas import tpu as pltpu
from jax import lax
from jax.sharding import PartitionSpec as P

HD = 64
BLK = 64
F = 64


def clip_index(positions, clip_ends):
    return jnp.sum((clip_ends[None, :] <= positions[:, None]).astype(jnp.int32), axis=1)


def shifted(x, axis, count, step):
    pairs = [(i + step, i) for i in range(count) if 0 <= i + step < count]
    return lax.ppermute(x, axis, pairs)


def rotated(x, axis, count, step):
    return lax.ppermute(x, axis, [(i, (i + step) % count) for i in range(count)])


def chunk_kernel(sources, has_state, final, flags_ref, q_ref, code_ref, qclip_ref, *refs):
    n_in = max(src for src, _ in sources) + 1
    kv_refs = refs[:n_in]
    rest = refs[n_in:]
    if has_state:
        m_in, l_in, acc_in = rest[:3]
        rest = rest[3:]
    if final:
        out_ref, m_ref, l_ref, acc_ref = rest
    else:
        m_ref, l_ref, acc_ref = rest
    row_count, col_count = acc_ref.shape
    sub_rows = code_ref.shape[1]
    piece = row_count // sub_rows
    pair = 2 * HD
    scale = 1.0 / math.sqrt(HD)
    if has_state:
        m_ref[...] = m_in[...]
        l_ref[...] = l_in[...]
        acc_ref[...] = acc_in[...]
    else:
        m_ref[...] = jnp.full(m_ref.shape, -1e30, jnp.float32)
        l_ref[...] = jnp.zeros(l_ref.shape, jnp.float32)
        acc_ref[...] = jnp.zeros(acc_ref.shape, jnp.float32)
    qclip = qclip_ref[...]
    low = lax.broadcasted_iota(jnp.int32, (row_count, pair), 1) < HD
    for b, (src, idx) in enumerate(sources):

        @pl.when(flags_ref[b] > 0)
        def _():
            code = code_ref[b]
            allowed = jnp.concatenate(
                [
                    jnp.broadcast_to(
                        qclip[i * piece : (i + 1) * piece] == code[i : i + 1, :],
                        (piece, code.shape[1]),
                    )
                    for i in range(sub_rows)
                ],
                axis=0,
            )
            bias = jnp.where(allowed, 0.0, -1e30).astype(jnp.float32)
            for hp in range(col_count // pair):
                cols = slice(hp * pair, (hp + 1) * pair)
                k_p = kv_refs[src][idx, 0, :, cols]
                v_p = kv_refs[src][idx, 1, :, cols]
                m_p = m_ref[:, cols]
                halves = []
                for e in range(2):
                    q_e = q_ref[e, :, cols]
                    s = lax.dot_general(
                        q_e, k_p, (((1,), (1,)), ((), ())), preferred_element_type=jnp.float32
                    )
                    s = s * scale + bias
                    m_old = m_p[:, e * HD : e * HD + 1]
                    m_new = jnp.maximum(m_old, jnp.max(s, axis=1, keepdims=True))
                    alpha = jnp.exp(m_old - m_new)
                    p = jnp.exp(s - m_new)
                    total = jnp.sum(p, axis=1, keepdims=True)
                    pv = jnp.dot(p.astype(jnp.bfloat16), v_p, preferred_element_type=jnp.float32)
                    halves.append((m_new, alpha, total, pv))
                (m0, a0, t0, pv0), (m1, a1, t1, pv1) = halves
                alpha = jnp.where(low, a0, a1)
                m_ref[:, cols] = jnp.where(low, m0, m1)
                l_ref[:, cols] = alpha * l_ref[:, cols] + jnp.where(low, t0, t1)
                acc_ref[:, cols] = alpha * acc_ref[:, cols] + jnp.where(low, pv0, pv1)

    if final:
        out_ref[...] = (acc_ref[...] / l_ref[...]).astype(out_ref.dtype)


def whole_kernel(sources, flags_ref, q_ref, code_ref, qclip_ref, *refs):
    n_in = max(src for src, _ in sources) + 1
    kv_refs = refs[:n_in]
    out_ref, bias_ref, m_ref, l_ref, acc_ref = refs[n_in:]
    row_count, col_count = out_ref.shape
    sub_rows = code_ref.shape[1]
    piece = row_count // sub_rows
    pair = 2 * HD
    qclip = qclip_ref[...]
    low = lax.broadcasted_iota(jnp.int32, (row_count, pair), 1) < HD
    for b in range(len(sources)):

        @pl.when(flags_ref[b] > 0)
        def _():
            code = code_ref[b]
            allowed = jnp.concatenate(
                [
                    jnp.broadcast_to(
                        qclip[i * piece : (i + 1) * piece] == code[i : i + 1, :],
                        (piece, code.shape[1]),
                    )
                    for i in range(sub_rows)
                ],
                axis=0,
            )
            bias_ref[b] = jnp.where(allowed, 0.0, -1e30).astype(jnp.float32)

    m_ref[...] = jnp.full(m_ref.shape, -1e30, jnp.float32)
    l_ref[...] = jnp.zeros(l_ref.shape, jnp.float32)
    acc_ref[...] = jnp.zeros(acc_ref.shape, jnp.float32)

    def scores(b, hp, e):
        src, idx = sources[b]
        cols = slice(hp * pair, (hp + 1) * pair)
        k_p = kv_refs[src][idx, 0, :, cols]
        s = lax.dot_general(
            q_ref[e, :, cols], k_p, (((1,), (1,)), ((), ())), preferred_element_type=jnp.float32
        )
        return s + bias_ref[b]

    for b in range(len(sources)):

        @pl.when(flags_ref[b] > 0)
        def _():
            for hp in range(col_count // pair):
                for e in range(2):
                    h = 2 * hp + e
                    m_ref[h] = jnp.maximum(m_ref[h], jnp.max(scores(b, hp, e), axis=1, keepdims=True))

    for b in range(len(sources)):

        @pl.when(flags_ref[b] > 0)
        def _():
            src, idx = sources[b]
            for hp in range(col_count // pair):
                cols = slice(hp * pair, (hp + 1) * pair)
                v_p = kv_refs[src][idx, 1, :, cols]
                pvs = []
                for e in range(2):
                    h = 2 * hp + e
                    p = jnp.exp(scores(b, hp, e) - m_ref[h])
                    l_ref[h] = l_ref[h] + jnp.sum(p, axis=1, keepdims=True)
                    pvs.append(
                        jnp.dot(p.astype(jnp.bfloat16), v_p, preferred_element_type=jnp.float32)
                    )
                acc_ref[:, cols] = acc_ref[:, cols] + jnp.where(low, pvs[0], pvs[1])

    for hp in range(col_count // pair):
        cols = slice(hp * pair, (hp + 1) * pair)
        den = jnp.where(low, l_ref[2 * hp], l_ref[2 * hp + 1])
        out_ref[:, cols] = (acc_ref[:, cols] / den).astype(out_ref.dtype)


def attend_chunk(state_now, q_split, query_clip, mask_rows, clip_ends, total, inputs, blocks):
    block_total = mask_rows.shape[1]
    sub_rows = mask_rows.shape[0]
    key_pos = jnp.stack([pos for _, _, pos in blocks])
    key_block = key_pos // BLK
    valid = (key_pos >= 0) & (key_pos < total)
    live = jnp.take(mask_rows, jnp.clip(key_block, 0, block_total - 1), axis=1)
    live = (live == 1) & valid[None]
    key_clip = clip_index(key_pos.reshape(-1), clip_ends).reshape(key_pos.shape)
    code = jnp.where(live, key_clip[None], -1).transpose(1, 0, 2)
    query_sub = query_clip.reshape(sub_rows, -1)
    flags = jnp.any(
        query_sub[None, :, :, None] == code[:, :, None, :], axis=(1, 2, 3)
    ).astype(jnp.int32)
    sources = tuple((src, idx) for src, idx, _ in blocks)
    n_in = len(inputs)
    has_state = state_now is not None
    final = not has_state
    row_count, col_count = q_split.shape[1:]
    state_shape = jax.ShapeDtypeStruct((row_count, col_count), jnp.float32)
    if final:
        out_shape = jax.ShapeDtypeStruct((row_count, col_count), jnp.bfloat16)
        out_specs = pl.BlockSpec(memory_space=pltpu.VMEM)
        head_count = col_count // HD
        scratch = [
            pltpu.VMEM((len(blocks), row_count, row_count), jnp.float32),
            pltpu.VMEM((head_count, row_count, 1), jnp.float32),
            pltpu.VMEM((head_count, row_count, 1), jnp.float32),
            pltpu.VMEM((row_count, col_count), jnp.float32),
        ]
        aliases = {}
        extra = ()
        q_split = (q_split.astype(jnp.float32) * (1.0 / math.sqrt(HD))).astype(jnp.bfloat16)
    else:
        out_shape = (state_shape,) * 3
        out_specs = [pl.BlockSpec(memory_space=pltpu.VMEM)] * 3
        scratch = []
        aliases = {4 + n_in: 0, 5 + n_in: 1, 6 + n_in: 2}
        extra = tuple(state_now)
    return pl.pallas_call(
        functools.partial(whole_kernel, sources)
        if final
        else functools.partial(chunk_kernel, sources, has_state, final),
        out_shape=out_shape,
        in_specs=[pl.BlockSpec(memory_space=pltpu.SMEM)]
        + [pl.BlockSpec(memory_space=pltpu.VMEM)] * (3 + n_in + len(extra)),
        out_specs=out_specs,
        scratch_shapes=scratch,
        input_output_aliases=aliases,
        cost_estimate=pl.CostEstimate(
            flops=len(blocks) * 8 * row_count**2 * col_count,
            transcendentals=len(blocks) * 2 * row_count**2 * col_count // HD,
            bytes_accessed=sum(x.size * x.dtype.itemsize for x in inputs) + 8 * q_split.size,
        ),
    )(flags, q_split, code, query_clip[:, None], *inputs, *extra)


def body(query_rows, key_rows, value_rows, clip_lengths, block_mask, out_weight, norm_gain):
    row_count, col_count = query_rows.shape
    head_count = col_count // HD
    n_seq = lax.axis_size("seq")
    n_sub = lax.axis_size("sub")
    n_head = lax.axis_size("head")
    seq_i = lax.axis_index("seq")
    sub_i = lax.axis_index("sub")
    head_i = lax.axis_index("head")
    chip_rows = row_count * n_sub
    total = chip_rows * n_seq
    longest = total // 2
    reach = min(n_seq - 1, 1 + (longest - 2) // chip_rows)

    clip_ends = jnp.cumsum(clip_lengths)
    token_first = (seq_i * n_sub + sub_i) * row_count
    mask_height = row_count // BLK
    mask_rows = lax.dynamic_slice_in_dim(block_mask, sub_i * mask_height, mask_height, 0)
    query_clip = clip_index(token_first + jnp.arange(row_count, dtype=jnp.int32), clip_ends)
    local_pos = jnp.arange(row_count, dtype=jnp.int32)

    def block_pos(seq_off, sub_src):
        return ((seq_i + seq_off) * n_sub + sub_src) * row_count + local_pos

    lane = lax.broadcasted_iota(jnp.int32, (1, col_count), 1) % (2 * HD)
    q_split = jnp.stack(
        [jnp.where(lane < HD, query_rows, 0), jnp.where(lane >= HD, query_rows, 0)]
    ).astype(jnp.bfloat16)

    def fold(state_now, mine, theirs):
        inputs = [kv[None] for kv, _ in mine]
        blocks = [(n, 0, block_pos(off, sub_i)) for n, (_, off) in enumerate(mine)]
        for got, offs, src in theirs:
            blocks += [(len(inputs), b, block_pos(off, src)) for b, off in enumerate(offs)]
            inputs.append(got)
        return attend_chunk(
            state_now, q_split, query_clip, mask_rows, clip_ends, total, inputs, blocks
        )

    def to_partner(mine):
        offs = [jnp.asarray(off, jnp.int32) for _, off in mine]
        return [
            (jnp.stack([rotated(kv, "sub", n_sub, j) for kv, _ in mine]), offs, (sub_i - j) % n_sub)
            for j in range(1, n_sub)
        ]

    own = jnp.stack([key_rows, value_rows])
    if reach <= 4:
        mine = [(own, 0)]
        theirs = to_partner(mine)
        left = own
        right = own
        for step in range(1, reach + 1):
            right = shifted(right, "seq", n_seq, 1)
            left = shifted(left, "seq", n_seq, -1)
            near = [(left, -step), (right, step)]
            mine += near
            theirs += to_partner(near)
        attended = fold(None, mine, theirs)
    else:
        state = (
            jnp.full((row_count, col_count), -1e30, jnp.float32),
            jnp.zeros((row_count, col_count), jnp.float32),
            jnp.zeros((row_count, col_count), jnp.float32),
        )
        state = fold(state, [(own, 0)], [])
        pending = to_partner([(own, 0)])

        def seq_step(step, carry):
            state_now, left, right, pending_now = carry
            right = shifted(right, "seq", n_seq, 1)
            left = shifted(left, "seq", n_seq, -1)
            near = [(left, -step), (right, step)]
            state_now = fold(state_now, near, pending_now)
            return (state_now, left, right, to_partner(near))

        carry = seq_step(1, (state, own, own, pending))
        carry = lax.fori_loop(2, reach + 1, seq_step, carry)
        state = fold(carry[0], [], carry[3])
        row_max, running, weighted = state
        attended = (weighted / running).astype(jnp.bfloat16)

    n_dev = n_seq * n_sub

    def flat(dev, head):
        return ((dev // n_sub) * n_head + head) * n_sub + dev % n_sub

    pieces = {-1: attended[row_count - F :], 0: attended, 1: attended[:F]}
    width = out_weight.shape[1]
    projected = jnp.zeros((row_count + 2 * F, width), jnp.float32)
    for j in range(n_head):
        parts = []
        for d in (-1, 0, 1):
            if j == 0 and d == 0:
                parts.append(attended)
                continue
            pairs = [
                (flat(i + d, (h + j) % n_head), flat(i, h))
                for i in range(n_dev)
                for h in range(n_head)
                if 0 <= i + d < n_dev
            ]
            parts.append(lax.ppermute(pieces[d], ("seq", "head", "sub"), pairs))
        src = (head_i + j) % n_head
        projected = projected + jnp.dot(
            jnp.concatenate(parts, axis=0),
            lax.dynamic_slice_in_dim(out_weight, src * col_count, col_count, 0),
            preferred_element_type=jnp.float32,
        )

    positions = token_first + jnp.arange(row_count, dtype=jnp.int32)
    clip_here = clip_index(positions, clip_ends)
    earlier = jnp.where(
        (clip_index(positions - F, clip_ends) == clip_here)[:, None], projected[:row_count], 0.0
    )
    later = jnp.where(
        (clip_index(positions + F, clip_ends) == clip_here)[:, None], projected[2 * F :], 0.0
    )
    blended = projected[F : F + row_count] + 0.5 * (earlier + later)
    squares = jnp.sum(blended * blended, axis=1)
    scale = lax.rsqrt(squares / width + 1e-06)
    own_cols = lax.dynamic_slice_in_dim(blended, head_i * col_count, col_count, 1)
    return (own_cols * scale[:, None] * norm_gain.astype(jnp.float32)).astype(jnp.bfloat16)


def solution(mesh):
    placed = (
        P(("grp", "seq", "sub"), "head"),
        P(("grp", "seq", "sub"), "head"),
        P(("grp", "seq", "sub"), "head"),
        P("grp"),
        P(("grp", "seq"), None),
        P(),
        P("head"),
    )
    return jax.shard_map(
        body,
        mesh=mesh,
        in_specs=placed,
        out_specs=P(("grp", "seq", "sub"), "head"),
        check_vma=False,
    )
```

```python
import functools
import math

import jax
import jax.numpy as jnp
from jax.experimental import pallas as pl
from jax.experimental.pallas import tpu as pltpu
from jax import lax
from jax.sharding import PartitionSpec as P

HD = 64
BLK = 64
F = 64


def clip_index(positions, clip_ends):
    return jnp.sum((clip_ends[None, :] <= positions[:, None]).astype(jnp.int32), axis=1)


def shifted(x, axis, count, step):
    pairs = [(i + step, i) for i in range(count) if 0 <= i + step < count]
    return lax.ppermute(x, axis, pairs)


def rotated(x, axis, count, step):
    return lax.ppermute(x, axis, [(i, (i + step) % count) for i in range(count)])


def chunk_kernel(sources, has_state, final, flags_ref, q_ref, code_ref, qclip_ref, *refs):
    n_in = max(src for src, _ in sources) + 1
    kv_refs = refs[:n_in]
    rest = refs[n_in:]
    if has_state:
        m_in, l_in, acc_in = rest[:3]
        rest = rest[3:]
    if final:
        out_ref, m_ref, l_ref, acc_ref = rest
    else:
        m_ref, l_ref, acc_ref = rest
    row_count, col_count = acc_ref.shape
    sub_rows = code_ref.shape[1]
    piece = row_count // sub_rows
    pair = 2 * HD
    scale = 1.0 / math.sqrt(HD)
    if has_state:
        m_ref[...] = m_in[...]
        l_ref[...] = l_in[...]
        acc_ref[...] = acc_in[...]
    else:
        m_ref[...] = jnp.full(m_ref.shape, -1e30, jnp.float32)
        l_ref[...] = jnp.zeros(l_ref.shape, jnp.float32)
        acc_ref[...] = jnp.zeros(acc_ref.shape, jnp.float32)
    qclip = qclip_ref[...]
    low = lax.broadcasted_iota(jnp.int32, (row_count, pair), 1) < HD
    for b, (src, idx) in enumerate(sources):

        @pl.when(flags_ref[b] > 0)
        def _():
            code = code_ref[b]
            allowed = jnp.concatenate(
                [
                    jnp.broadcast_to(
                        qclip[i * piece : (i + 1) * piece] == code[i : i + 1, :],
                        (piece, code.shape[1]),
                    )
                    for i in range(sub_rows)
                ],
                axis=0,
            )
            bias = jnp.where(allowed, 0.0, -1e30).astype(jnp.float32)
            for hp in range(col_count // pair):
                cols = slice(hp * pair, (hp + 1) * pair)
                k_p = kv_refs[src][idx, 0, :, cols]
                v_p = kv_refs[src][idx, 1, :, cols]
                m_p = m_ref[:, cols]
                halves = []
                for e in range(2):
                    q_e = q_ref[e, :, cols]
                    s = lax.dot_general(
                        q_e, k_p, (((1,), (1,)), ((), ())), preferred_element_type=jnp.float32
                    )
                    s = s * scale + bias
                    m_old = m_p[:, e * HD : e * HD + 1]
                    m_new = jnp.maximum(m_old, jnp.max(s, axis=1, keepdims=True))
                    alpha = jnp.exp(m_old - m_new)
                    p = jnp.exp(s - m_new)
                    total = jnp.sum(p, axis=1, keepdims=True)
                    pv = jnp.dot(p.astype(jnp.bfloat16), v_p, preferred_element_type=jnp.float32)
                    halves.append((m_new, alpha, total, pv))
                (m0, a0, t0, pv0), (m1, a1, t1, pv1) = halves
                alpha = jnp.where(low, a0, a1)
                m_ref[:, cols] = jnp.where(low, m0, m1)
                l_ref[:, cols] = alpha * l_ref[:, cols] + jnp.where(low, t0, t1)
                acc_ref[:, cols] = alpha * acc_ref[:, cols] + jnp.where(low, pv0, pv1)

    if final:
        out_ref[...] = (acc_ref[...] / l_ref[...]).astype(out_ref.dtype)


def whole_kernel(sources, flags_ref, q_ref, code_ref, qclip_ref, *refs):
    n_in = max(src for src, _ in sources) + 1
    kv_refs = refs[:n_in]
    out_ref, bias_ref, m_ref, l_ref, acc_ref = refs[n_in:]
    row_count, col_count = out_ref.shape
    sub_rows = code_ref.shape[1]
    piece = row_count // sub_rows
    pair = 2 * HD
    qclip = qclip_ref[...]
    low = lax.broadcasted_iota(jnp.int32, (row_count, pair), 1) < HD
    for b in range(len(sources)):

        @pl.when(flags_ref[b] > 0)
        def _():
            code = code_ref[b]
            allowed = jnp.concatenate(
                [
                    jnp.broadcast_to(
                        qclip[i * piece : (i + 1) * piece] == code[i : i + 1, :],
                        (piece, code.shape[1]),
                    )
                    for i in range(sub_rows)
                ],
                axis=0,
            )
            bias_ref[b] = jnp.where(allowed, 0.0, -1e30).astype(jnp.float32)

    m_ref[...] = jnp.full(m_ref.shape, -1e30, jnp.float32)
    l_ref[...] = jnp.zeros(l_ref.shape, jnp.float32)
    acc_ref[...] = jnp.zeros(acc_ref.shape, jnp.float32)

    def scores(b, hp, e):
        src, idx = sources[b]
        cols = slice(hp * pair, (hp + 1) * pair)
        k_p = kv_refs[src][idx, 0, :, cols]
        s = lax.dot_general(
            q_ref[e, :, cols], k_p, (((1,), (1,)), ((), ())), preferred_element_type=jnp.float32
        )
        return s + bias_ref[b]

    for b in range(len(sources)):

        @pl.when(flags_ref[b] > 0)
        def _():
            for hp in range(col_count // pair):
                for e in range(2):
                    h = 2 * hp + e
                    m_ref[h] = jnp.maximum(m_ref[h], jnp.max(scores(b, hp, e), axis=1, keepdims=True))

    for b in range(len(sources)):

        @pl.when(flags_ref[b] > 0)
        def _():
            src, idx = sources[b]
            for hp in range(col_count // pair):
                cols = slice(hp * pair, (hp + 1) * pair)
                v_p = kv_refs[src][idx, 1, :, cols]
                pvs = []
                for e in range(2):
                    h = 2 * hp + e
                    p = jnp.exp(scores(b, hp, e) - m_ref[h])
                    l_ref[h] = l_ref[h] + jnp.sum(p, axis=1, keepdims=True)
                    pvs.append(
                        jnp.dot(p.astype(jnp.bfloat16), v_p, preferred_element_type=jnp.float32)
                    )
                acc_ref[:, cols] = acc_ref[:, cols] + jnp.where(low, pvs[0], pvs[1])

    for hp in range(col_count // pair):
        cols = slice(hp * pair, (hp + 1) * pair)
        den = jnp.where(low, l_ref[2 * hp], l_ref[2 * hp + 1])
        out_ref[:, cols] = (acc_ref[:, cols] / den).astype(out_ref.dtype)


def attend_chunk(state_now, q_split, query_clip, mask_rows, clip_ends, total, inputs, blocks):
    block_total = mask_rows.shape[1]
    sub_rows = mask_rows.shape[0]
    key_pos = jnp.stack([pos for _, _, pos in blocks])
    key_block = key_pos[:, ::BLK] // BLK
    valid = (key_block >= 0) & (key_block < block_total)
    live = jnp.take(mask_rows, jnp.clip(key_block, 0, block_total - 1), axis=1)
    live = jnp.repeat((live == 1) & valid[None], BLK, axis=2)
    key_clip = clip_index(key_pos.reshape(-1), clip_ends).reshape(key_pos.shape)
    code = jnp.where(live, key_clip[None], -1).transpose(1, 0, 2)
    query_sub = query_clip.reshape(sub_rows, -1)
    flags = jnp.any(
        query_sub[None, :, :, None] == code[:, :, None, :], axis=(1, 2, 3)
    ).astype(jnp.int32)
    sources = tuple((src, idx) for src, idx, _ in blocks)
    n_in = len(inputs)
    has_state = state_now is not None
    final = not has_state
    row_count, col_count = q_split.shape[1:]
    state_shape = jax.ShapeDtypeStruct((row_count, col_count), jnp.float32)
    if final:
        out_shape = jax.ShapeDtypeStruct((row_count, col_count), jnp.bfloat16)
        out_specs = pl.BlockSpec(memory_space=pltpu.VMEM)
        head_count = col_count // HD
        scratch = [
            pltpu.VMEM((len(blocks), row_count, row_count), jnp.float32),
            pltpu.VMEM((head_count, row_count, 1), jnp.float32),
            pltpu.VMEM((head_count, row_count, 1), jnp.float32),
            pltpu.VMEM((row_count, col_count), jnp.float32),
        ]
        aliases = {}
        extra = ()
        q_split = (q_split.astype(jnp.float32) * (1.0 / math.sqrt(HD))).astype(jnp.bfloat16)
    else:
        out_shape = (state_shape,) * 3
        out_specs = [pl.BlockSpec(memory_space=pltpu.VMEM)] * 3
        scratch = []
        aliases = {4 + n_in: 0, 5 + n_in: 1, 6 + n_in: 2}
        extra = tuple(state_now)
    return pl.pallas_call(
        functools.partial(whole_kernel, sources)
        if final
        else functools.partial(chunk_kernel, sources, has_state, final),
        out_shape=out_shape,
        in_specs=[pl.BlockSpec(memory_space=pltpu.SMEM)]
        + [pl.BlockSpec(memory_space=pltpu.VMEM)] * (3 + n_in + len(extra)),
        out_specs=out_specs,
        scratch_shapes=scratch,
        input_output_aliases=aliases,
        cost_estimate=pl.CostEstimate(
            flops=len(blocks) * 8 * row_count**2 * col_count,
            transcendentals=len(blocks) * 2 * row_count**2 * col_count // HD,
            bytes_accessed=sum(x.size * x.dtype.itemsize for x in inputs) + 8 * q_split.size,
        ),
    )(flags, q_split, code, query_clip[:, None], *inputs, *extra)


def body(query_rows, key_rows, value_rows, clip_lengths, block_mask, out_weight, norm_gain):
    row_count, col_count = query_rows.shape
    head_count = col_count // HD
    n_seq = lax.axis_size("seq")
    n_sub = lax.axis_size("sub")
    n_head = lax.axis_size("head")
    seq_i = lax.axis_index("seq")
    sub_i = lax.axis_index("sub")
    head_i = lax.axis_index("head")
    chip_rows = row_count * n_sub
    total = chip_rows * n_seq
    longest = total // 2
    reach = min(n_seq - 1, 1 + (longest - 2) // chip_rows)

    clip_ends = jnp.cumsum(clip_lengths)
    token_first = (seq_i * n_sub + sub_i) * row_count
    mask_height = row_count // BLK
    mask_rows = lax.dynamic_slice_in_dim(block_mask, sub_i * mask_height, mask_height, 0)
    query_clip = clip_index(token_first + jnp.arange(row_count, dtype=jnp.int32), clip_ends)
    local_pos = jnp.arange(row_count, dtype=jnp.int32)

    def block_pos(seq_off, sub_src):
        return ((seq_i + seq_off) * n_sub + sub_src) * row_count + local_pos

    lane = lax.broadcasted_iota(jnp.int32, (1, col_count), 1) % (2 * HD)
    q_split = jnp.stack(
        [jnp.where(lane < HD, query_rows, 0), jnp.where(lane >= HD, query_rows, 0)]
    ).astype(jnp.bfloat16)

    def fold(state_now, mine, theirs):
        inputs = [kv[None] for kv, _ in mine]
        blocks = [(n, 0, block_pos(off, sub_i)) for n, (_, off) in enumerate(mine)]
        for got, offs, src in theirs:
            if isinstance(got, list):
                for piece, off in zip(got, offs):
                    blocks.append((len(inputs), 0, block_pos(off, src)))
                    inputs.append(piece[None])
            else:
                blocks += [(len(inputs), b, block_pos(off, src)) for b, off in enumerate(offs)]
                inputs.append(got)
        return attend_chunk(
            state_now, q_split, query_clip, mask_rows, clip_ends, total, inputs, blocks
        )

    def to_partner(mine):
        offs = [jnp.asarray(off, jnp.int32) for _, off in mine]
        return [
            (jnp.stack([rotated(kv, "sub", n_sub, j) for kv, _ in mine]), offs, (sub_i - j) % n_sub)
            for j in range(1, n_sub)
        ]

    def to_partner_apart(mine):
        offs = [off for _, off in mine]
        return [
            ([rotated(kv, "sub", n_sub, j) for kv, _ in mine], offs, (sub_i - j) % n_sub)
            for j in range(1, n_sub)
        ]

    own = jnp.stack([key_rows, value_rows])
    if reach <= 4:
        to_partner = to_partner_apart
        mine = [(own, 0)]
        theirs = to_partner(mine)
        left = own
        right = own
        for step in range(1, reach + 1):
            right = shifted(right, "seq", n_seq, 1)
            left = shifted(left, "seq", n_seq, -1)
            near = [(left, -step), (right, step)]
            mine += near
            theirs += to_partner(near)
        attended = fold(None, mine, theirs)
    else:
        state = (
            jnp.full((row_count, col_count), -1e30, jnp.float32),
            jnp.zeros((row_count, col_count), jnp.float32),
            jnp.zeros((row_count, col_count), jnp.float32),
        )
        state = fold(state, [(own, 0)], [])
        pending = to_partner([(own, 0)])

        def seq_step(step, carry):
            state_now, left, right, pending_now = carry
            right = shifted(right, "seq", n_seq, 1)
            left = shifted(left, "seq", n_seq, -1)
            near = [(left, -step), (right, step)]
            state_now = fold(state_now, near, pending_now)
            return (state_now, left, right, to_partner(near))

        carry = seq_step(1, (state, own, own, pending))
        carry = lax.fori_loop(2, reach + 1, seq_step, carry)
        state = fold(carry[0], [], carry[3])
        row_max, running, weighted = state
        attended = (weighted / running).astype(jnp.bfloat16)

    n_dev = n_seq * n_sub

    def flat(dev, head):
        return ((dev // n_sub) * n_head + head) * n_sub + dev % n_sub

    pieces = {-1: attended[row_count - F :], 0: attended, 1: attended[:F]}
    width = out_weight.shape[1]
    projected = jnp.zeros((row_count + 2 * F, width), jnp.float32)
    for j in range(n_head):
        parts = []
        for d in (-1, 0, 1):
            if j == 0 and d == 0:
                parts.append(attended)
                continue
            pairs = [
                (flat(i + d, (h + j) % n_head), flat(i, h))
                for i in range(n_dev)
                for h in range(n_head)
                if 0 <= i + d < n_dev
            ]
            parts.append(lax.ppermute(pieces[d], ("seq", "head", "sub"), pairs))
        src = (head_i + j) % n_head
        projected = projected + jnp.dot(
            jnp.concatenate(parts, axis=0),
            lax.dynamic_slice_in_dim(out_weight, src * col_count, col_count, 0),
            preferred_element_type=jnp.float32,
        )

    positions = token_first + jnp.arange(row_count, dtype=jnp.int32)
    clip_here = clip_index(positions, clip_ends)
    earlier = jnp.where(
        (clip_index(positions - F, clip_ends) == clip_here)[:, None], projected[:row_count], 0.0
    )
    later = jnp.where(
        (clip_index(positions + F, clip_ends) == clip_here)[:, None], projected[2 * F :], 0.0
    )
    blended = projected[F : F + row_count] + 0.5 * (earlier + later)
    squares = jnp.sum(blended * blended, axis=1)
    scale = lax.rsqrt(squares / width + 1e-06)
    own_cols = lax.dynamic_slice_in_dim(blended, head_i * col_count, col_count, 1)
    return (own_cols * scale[:, None] * norm_gain.astype(jnp.float32)).astype(jnp.bfloat16)


def solution(mesh):
    placed = (
        P(("grp", "seq", "sub"), "head"),
        P(("grp", "seq", "sub"), "head"),
        P(("grp", "seq", "sub"), "head"),
        P("grp"),
        P(("grp", "seq"), None),
        P(),
        P("head"),
    )
    return jax.shard_map(
        body,
        mesh=mesh,
        in_specs=placed,
        out_specs=P(("grp", "seq", "sub"), "head"),
        check_vma=False,
    )
```

```python
import functools
import math

import jax
import jax.numpy as jnp
from jax.experimental import pallas as pl
from jax.experimental.pallas import tpu as pltpu
from jax import lax
from jax.sharding import PartitionSpec as P

HD = 64
BLK = 64
F = 64


def clip_index(positions, clip_ends):
    return jnp.sum((clip_ends[None, :] <= positions[:, None]).astype(jnp.int32), axis=1)


def shifted(x, axis, count, step):
    pairs = [(i + step, i) for i in range(count) if 0 <= i + step < count]
    return lax.ppermute(x, axis, pairs)


def rotated(x, axis, count, step):
    return lax.ppermute(x, axis, [(i, (i + step) % count) for i in range(count)])


def chunk_kernel(sources, has_state, final, flags_ref, q_ref, code_ref, qclip_ref, *refs):
    n_in = max(src for src, _ in sources) + 1
    kv_refs = refs[:n_in]
    rest = refs[n_in:]
    if has_state:
        m_in, l_in, acc_in = rest[:3]
        rest = rest[3:]
    if final:
        out_ref, m_ref, l_ref, acc_ref = rest
    else:
        m_ref, l_ref, acc_ref = rest
    row_count, col_count = acc_ref.shape
    sub_rows = code_ref.shape[1]
    piece = row_count // sub_rows
    pair = 2 * HD
    scale = 1.0 / math.sqrt(HD)
    if has_state:
        m_ref[...] = m_in[...]
        l_ref[...] = l_in[...]
        acc_ref[...] = acc_in[...]
    else:
        m_ref[...] = jnp.full(m_ref.shape, -1e30, jnp.float32)
        l_ref[...] = jnp.zeros(l_ref.shape, jnp.float32)
        acc_ref[...] = jnp.zeros(acc_ref.shape, jnp.float32)
    qclip = qclip_ref[...]
    low = lax.broadcasted_iota(jnp.int32, (row_count, pair), 1) < HD
    for b, (src, idx) in enumerate(sources):

        @pl.when(flags_ref[b] > 0)
        def _():
            code = code_ref[b]
            allowed = jnp.concatenate(
                [
                    jnp.broadcast_to(
                        qclip[i * piece : (i + 1) * piece] == code[i : i + 1, :],
                        (piece, code.shape[1]),
                    )
                    for i in range(sub_rows)
                ],
                axis=0,
            )
            bias = jnp.where(allowed, 0.0, -1e30).astype(jnp.float32)
            for hp in range(col_count // pair):
                cols = slice(hp * pair, (hp + 1) * pair)
                k_p = kv_refs[src][idx, 0, :, cols]
                v_p = kv_refs[src][idx, 1, :, cols]
                m_p = m_ref[:, cols]
                halves = []
                for e in range(2):
                    q_e = q_ref[e, :, cols]
                    s = lax.dot_general(
                        q_e, k_p, (((1,), (1,)), ((), ())), preferred_element_type=jnp.float32
                    )
                    s = s * scale + bias
                    m_old = m_p[:, e * HD : e * HD + 1]
                    m_new = jnp.maximum(m_old, jnp.max(s, axis=1, keepdims=True))
                    alpha = jnp.exp(m_old - m_new)
                    p = jnp.exp(s - m_new)
                    total = jnp.sum(p, axis=1, keepdims=True)
                    pv = jnp.dot(p.astype(jnp.bfloat16), v_p, preferred_element_type=jnp.float32)
                    halves.append((m_new, alpha, total, pv))
                (m0, a0, t0, pv0), (m1, a1, t1, pv1) = halves
                alpha = jnp.where(low, a0, a1)
                m_ref[:, cols] = jnp.where(low, m0, m1)
                l_ref[:, cols] = alpha * l_ref[:, cols] + jnp.where(low, t0, t1)
                acc_ref[:, cols] = alpha * acc_ref[:, cols] + jnp.where(low, pv0, pv1)

    if final:
        out_ref[...] = (acc_ref[...] / l_ref[...]).astype(out_ref.dtype)


def whole_kernel(sources, flags_ref, q_ref, code_ref, qclip_ref, *refs):
    n_in = max(src for src, _ in sources) + 1
    kv_refs = refs[:n_in]
    out_ref, bias_ref, m_ref, l_ref, acc_ref, s_ref = refs[n_in:]
    row_count, col_count = out_ref.shape
    sub_rows = code_ref.shape[1]
    piece = row_count // sub_rows
    pair = 2 * HD
    qclip = qclip_ref[...]
    low = lax.broadcasted_iota(jnp.int32, (row_count, pair), 1) < HD
    for b in range(len(sources)):

        @pl.when(flags_ref[b] > 0)
        def _():
            code = code_ref[b]
            allowed = jnp.concatenate(
                [
                    jnp.broadcast_to(
                        qclip[i * piece : (i + 1) * piece] == code[i : i + 1, :],
                        (piece, code.shape[1]),
                    )
                    for i in range(sub_rows)
                ],
                axis=0,
            )
            bias_ref[b] = jnp.where(allowed, 0.0, -1e30).astype(jnp.float32)

    m_ref[...] = jnp.full(m_ref.shape, -1e30, jnp.float32)
    l_ref[...] = jnp.zeros(l_ref.shape, jnp.float32)
    acc_ref[...] = jnp.zeros(acc_ref.shape, jnp.float32)

    def scores(b, hp, e):
        src, idx = sources[b]
        cols = slice(hp * pair, (hp + 1) * pair)
        k_p = kv_refs[src][idx, 0, :, cols]
        s = lax.dot_general(
            q_ref[e, :, cols], k_p, (((1,), (1,)), ((), ())), preferred_element_type=jnp.float32
        )
        return s + bias_ref[b]

    for b in range(len(sources)):

        @pl.when(flags_ref[b] > 0)
        def _():
            for hp in range(col_count // pair):
                for e in range(2):
                    h = 2 * hp + e
                    s_now = scores(b, hp, e)
                    s_ref[b, h] = s_now
                    m_ref[h] = jnp.maximum(m_ref[h], jnp.max(s_now, axis=1, keepdims=True))

    for b in range(len(sources)):

        @pl.when(flags_ref[b] > 0)
        def _():
            src, idx = sources[b]
            for hp in range(col_count // pair):
                cols = slice(hp * pair, (hp + 1) * pair)
                v_p = kv_refs[src][idx, 1, :, cols]
                pvs = []
                for e in range(2):
                    h = 2 * hp + e
                    p = jnp.exp(s_ref[b, h] - m_ref[h])
                    l_ref[h] = l_ref[h] + jnp.sum(p, axis=1, keepdims=True)
                    pvs.append(
                        jnp.dot(p.astype(jnp.bfloat16), v_p, preferred_element_type=jnp.float32)
                    )
                acc_ref[:, cols] = acc_ref[:, cols] + jnp.where(low, pvs[0], pvs[1])

    for hp in range(col_count // pair):
        cols = slice(hp * pair, (hp + 1) * pair)
        den = jnp.where(low, l_ref[2 * hp], l_ref[2 * hp + 1])
        out_ref[:, cols] = (acc_ref[:, cols] / den).astype(out_ref.dtype)


def attend_chunk(state_now, q_split, query_clip, mask_rows, clip_ends, total, inputs, blocks):
    block_total = mask_rows.shape[1]
    sub_rows = mask_rows.shape[0]
    key_pos = jnp.stack([pos for _, _, pos in blocks])
    key_block = key_pos[:, ::BLK] // BLK
    valid = (key_block >= 0) & (key_block < block_total)
    live = jnp.take(mask_rows, jnp.clip(key_block, 0, block_total - 1), axis=1)
    live = jnp.repeat((live == 1) & valid[None], BLK, axis=2)
    key_clip = clip_index(key_pos.reshape(-1), clip_ends).reshape(key_pos.shape)
    code = jnp.where(live, key_clip[None], -1).transpose(1, 0, 2)
    query_sub = query_clip.reshape(sub_rows, -1)
    flags = jnp.any(
        query_sub[None, :, :, None] == code[:, :, None, :], axis=(1, 2, 3)
    ).astype(jnp.int32)
    sources = tuple((src, idx) for src, idx, _ in blocks)
    n_in = len(inputs)
    has_state = state_now is not None
    final = not has_state
    row_count, col_count = q_split.shape[1:]
    state_shape = jax.ShapeDtypeStruct((row_count, col_count), jnp.float32)
    if final:
        out_shape = jax.ShapeDtypeStruct((row_count, col_count), jnp.bfloat16)
        out_specs = pl.BlockSpec(memory_space=pltpu.VMEM)
        head_count = col_count // HD
        scratch = [
            pltpu.VMEM((len(blocks), row_count, row_count), jnp.float32),
            pltpu.VMEM((head_count, row_count, 1), jnp.float32),
            pltpu.VMEM((head_count, row_count, 1), jnp.float32),
            pltpu.VMEM((row_count, col_count), jnp.float32),
            pltpu.VMEM((len(blocks), head_count, row_count, row_count), jnp.float32),
        ]
        aliases = {}
        extra = ()
        q_split = (q_split.astype(jnp.float32) * (1.0 / math.sqrt(HD))).astype(jnp.bfloat16)
    else:
        out_shape = (state_shape,) * 3
        out_specs = [pl.BlockSpec(memory_space=pltpu.VMEM)] * 3
        scratch = []
        aliases = {4 + n_in: 0, 5 + n_in: 1, 6 + n_in: 2}
        extra = tuple(state_now)
    return pl.pallas_call(
        functools.partial(whole_kernel, sources)
        if final
        else functools.partial(chunk_kernel, sources, has_state, final),
        out_shape=out_shape,
        in_specs=[pl.BlockSpec(memory_space=pltpu.SMEM)]
        + [pl.BlockSpec(memory_space=pltpu.VMEM)] * (3 + n_in + len(extra)),
        out_specs=out_specs,
        scratch_shapes=scratch,
        input_output_aliases=aliases,
        cost_estimate=pl.CostEstimate(
            flops=len(blocks) * 8 * row_count**2 * col_count,
            transcendentals=len(blocks) * 2 * row_count**2 * col_count // HD,
            bytes_accessed=sum(x.size * x.dtype.itemsize for x in inputs) + 8 * q_split.size,
        ),
    )(flags, q_split, code, query_clip[:, None], *inputs, *extra)


def body(query_rows, key_rows, value_rows, clip_lengths, block_mask, out_weight, norm_gain):
    row_count, col_count = query_rows.shape
    head_count = col_count // HD
    n_seq = lax.axis_size("seq")
    n_sub = lax.axis_size("sub")
    n_head = lax.axis_size("head")
    seq_i = lax.axis_index("seq")
    sub_i = lax.axis_index("sub")
    head_i = lax.axis_index("head")
    chip_rows = row_count * n_sub
    total = chip_rows * n_seq
    longest = total // 2
    reach = min(n_seq - 1, 1 + (longest - 2) // chip_rows)

    clip_ends = jnp.cumsum(clip_lengths)
    token_first = (seq_i * n_sub + sub_i) * row_count
    mask_height = row_count // BLK
    mask_rows = lax.dynamic_slice_in_dim(block_mask, sub_i * mask_height, mask_height, 0)
    query_clip = clip_index(token_first + jnp.arange(row_count, dtype=jnp.int32), clip_ends)
    local_pos = jnp.arange(row_count, dtype=jnp.int32)

    def block_pos(seq_off, sub_src):
        return ((seq_i + seq_off) * n_sub + sub_src) * row_count + local_pos

    lane = lax.broadcasted_iota(jnp.int32, (1, col_count), 1) % (2 * HD)
    q_split = jnp.stack(
        [jnp.where(lane < HD, query_rows, 0), jnp.where(lane >= HD, query_rows, 0)]
    ).astype(jnp.bfloat16)

    def fold(state_now, mine, theirs):
        inputs = [kv[None] for kv, _ in mine]
        blocks = [(n, 0, block_pos(off, sub_i)) for n, (_, off) in enumerate(mine)]
        for got, offs, src in theirs:
            if isinstance(got, list):
                for piece, off in zip(got, offs):
                    blocks.append((len(inputs), 0, block_pos(off, src)))
                    inputs.append(piece[None])
            else:
                blocks += [(len(inputs), b, block_pos(off, src)) for b, off in enumerate(offs)]
                inputs.append(got)
        return attend_chunk(
            state_now, q_split, query_clip, mask_rows, clip_ends, total, inputs, blocks
        )

    def to_partner(mine):
        offs = [jnp.asarray(off, jnp.int32) for _, off in mine]
        return [
            (jnp.stack([rotated(kv, "sub", n_sub, j) for kv, _ in mine]), offs, (sub_i - j) % n_sub)
            for j in range(1, n_sub)
        ]

    def to_partner_apart(mine):
        offs = [off for _, off in mine]
        return [
            ([rotated(kv, "sub", n_sub, j) for kv, _ in mine], offs, (sub_i - j) % n_sub)
            for j in range(1, n_sub)
        ]

    own = jnp.stack([key_rows, value_rows])
    if reach <= 4:
        to_partner = to_partner_apart
        mine = [(own, 0)]
        theirs = to_partner(mine)
        left = own
        right = own
        for step in range(1, reach + 1):
            right = shifted(right, "seq", n_seq, 1)
            left = shifted(left, "seq", n_seq, -1)
            near = [(left, -step), (right, step)]
            mine += near
            theirs += to_partner(near)
        attended = fold(None, mine, theirs)
    else:
        state = (
            jnp.full((row_count, col_count), -1e30, jnp.float32),
            jnp.zeros((row_count, col_count), jnp.float32),
            jnp.zeros((row_count, col_count), jnp.float32),
        )
        state = fold(state, [(own, 0)], [])
        pending = to_partner([(own, 0)])

        def seq_step(step, carry):
            state_now, left, right, pending_now = carry
            right = shifted(right, "seq", n_seq, 1)
            left = shifted(left, "seq", n_seq, -1)
            near = [(left, -step), (right, step)]
            state_now = fold(state_now, near, pending_now)
            return (state_now, left, right, to_partner(near))

        carry = seq_step(1, (state, own, own, pending))
        carry = lax.fori_loop(2, reach + 1, seq_step, carry)
        state = fold(carry[0], [], carry[3])
        row_max, running, weighted = state
        attended = (weighted / running).astype(jnp.bfloat16)

    n_dev = n_seq * n_sub

    def flat(dev, head):
        return ((dev // n_sub) * n_head + head) * n_sub + dev % n_sub

    pieces = {-1: attended[row_count - F :], 0: attended, 1: attended[:F]}
    width = out_weight.shape[1]
    projected = jnp.zeros((row_count + 2 * F, width), jnp.float32)
    for j in range(n_head):
        parts = []
        for d in (-1, 0, 1):
            if j == 0 and d == 0:
                parts.append(attended)
                continue
            pairs = [
                (flat(i + d, (h + j) % n_head), flat(i, h))
                for i in range(n_dev)
                for h in range(n_head)
                if 0 <= i + d < n_dev
            ]
            parts.append(lax.ppermute(pieces[d], ("seq", "head", "sub"), pairs))
        src = (head_i + j) % n_head
        projected = projected + jnp.dot(
            jnp.concatenate(parts, axis=0),
            lax.dynamic_slice_in_dim(out_weight, src * col_count, col_count, 0),
            preferred_element_type=jnp.float32,
        )

    positions = token_first + jnp.arange(row_count, dtype=jnp.int32)
    clip_here = clip_index(positions, clip_ends)
    earlier = jnp.where(
        (clip_index(positions - F, clip_ends) == clip_here)[:, None], projected[:row_count], 0.0
    )
    later = jnp.where(
        (clip_index(positions + F, clip_ends) == clip_here)[:, None], projected[2 * F :], 0.0
    )
    blended = projected[F : F + row_count] + 0.5 * (earlier + later)
    squares = jnp.sum(blended * blended, axis=1)
    scale = lax.rsqrt(squares / width + 1e-06)
    own_cols = lax.dynamic_slice_in_dim(blended, head_i * col_count, col_count, 1)
    return (own_cols * scale[:, None] * norm_gain.astype(jnp.float32)).astype(jnp.bfloat16)


def solution(mesh):
    placed = (
        P(("grp", "seq", "sub"), "head"),
        P(("grp", "seq", "sub"), "head"),
        P(("grp", "seq", "sub"), "head"),
        P("grp"),
        P(("grp", "seq"), None),
        P(),
        P("head"),
    )
    return jax.shard_map(
        body,
        mesh=mesh,
        in_specs=placed,
        out_specs=P(("grp", "seq", "sub"), "head"),
        check_vma=False,
    )
```

```python
import functools
import math

import jax
import jax.numpy as jnp
from jax.experimental import pallas as pl
from jax.experimental.pallas import tpu as pltpu
from jax import lax
from jax.sharding import PartitionSpec as P

HD = 64
BLK = 64
F = 64


def clip_index(positions, clip_ends):
    return jnp.sum((clip_ends[None, :] <= positions[:, None]).astype(jnp.int32), axis=1)


def shifted(x, axis, count, step):
    pairs = [(i + step, i) for i in range(count) if 0 <= i + step < count]
    return lax.ppermute(x, axis, pairs)


def rotated(x, axis, count, step):
    return lax.ppermute(x, axis, [(i, (i + step) % count) for i in range(count)])


def chunk_kernel(sources, has_state, final, flags_ref, q_ref, code_ref, qclip_ref, *refs):
    n_in = max(src for src, _ in sources) + 1
    kv_refs = refs[:n_in]
    rest = refs[n_in:]
    if has_state:
        m_in, l_in, acc_in = rest[:3]
        rest = rest[3:]
    if final:
        out_ref, m_ref, l_ref, acc_ref = rest
    else:
        m_ref, l_ref, acc_ref = rest
    row_count, col_count = acc_ref.shape
    sub_rows = code_ref.shape[1]
    piece = row_count // sub_rows
    pair = 2 * HD
    scale = 1.0 / math.sqrt(HD)
    if has_state:
        m_ref[...] = m_in[...]
        l_ref[...] = l_in[...]
        acc_ref[...] = acc_in[...]
    else:
        m_ref[...] = jnp.full(m_ref.shape, -1e30, jnp.float32)
        l_ref[...] = jnp.zeros(l_ref.shape, jnp.float32)
        acc_ref[...] = jnp.zeros(acc_ref.shape, jnp.float32)
    qclip = qclip_ref[...]
    low = lax.broadcasted_iota(jnp.int32, (row_count, pair), 1) < HD
    for b, (src, idx) in enumerate(sources):

        @pl.when(flags_ref[b] > 0)
        def _():
            code = code_ref[b]
            allowed = jnp.concatenate(
                [
                    jnp.broadcast_to(
                        qclip[i * piece : (i + 1) * piece] == code[i : i + 1, :],
                        (piece, code.shape[1]),
                    )
                    for i in range(sub_rows)
                ],
                axis=0,
            )
            bias = jnp.where(allowed, 0.0, -1e30).astype(jnp.float32)
            for hp in range(col_count // pair):
                cols = slice(hp * pair, (hp + 1) * pair)
                k_p = kv_refs[src][idx, 0, :, cols]
                v_p = kv_refs[src][idx, 1, :, cols]
                m_p = m_ref[:, cols]
                halves = []
                for e in range(2):
                    q_e = q_ref[e, :, cols]
                    s = lax.dot_general(
                        q_e, k_p, (((1,), (1,)), ((), ())), preferred_element_type=jnp.float32
                    )
                    s = s * scale + bias
                    m_old = m_p[:, e * HD : e * HD + 1]
                    m_new = jnp.maximum(m_old, jnp.max(s, axis=1, keepdims=True))
                    alpha = jnp.exp(m_old - m_new)
                    p = jnp.exp(s - m_new)
                    total = jnp.sum(p, axis=1, keepdims=True)
                    pv = jnp.dot(p.astype(jnp.bfloat16), v_p, preferred_element_type=jnp.float32)
                    halves.append((m_new, alpha, total, pv))
                (m0, a0, t0, pv0), (m1, a1, t1, pv1) = halves
                alpha = jnp.where(low, a0, a1)
                m_ref[:, cols] = jnp.where(low, m0, m1)
                l_ref[:, cols] = alpha * l_ref[:, cols] + jnp.where(low, t0, t1)
                acc_ref[:, cols] = alpha * acc_ref[:, cols] + jnp.where(low, pv0, pv1)

    if final:
        out_ref[...] = (acc_ref[...] / l_ref[...]).astype(out_ref.dtype)


def whole_kernel(sources, flags_ref, q_ref, code_ref, qclip_ref, *refs):
    n_in = max(src for src, _ in sources) + 1
    kv_hbm = refs[:n_in]
    out_ref, bias_ref, m_ref, l_ref, acc_ref, kv_buf, sems = refs[n_in:]
    row_count, col_count = out_ref.shape
    sub_rows = code_ref.shape[1]
    piece = row_count // sub_rows
    pair = 2 * HD
    qclip = qclip_ref[...]
    low = lax.broadcasted_iota(jnp.int32, (row_count, pair), 1) < HD

    def fetch(b):
        src, idx = sources[b]
        return pltpu.make_async_copy(kv_hbm[src].at[idx], kv_buf.at[b], sems.at[b])

    for b in range(len(sources)):

        @pl.when(flags_ref[b] > 0)
        def _():
            fetch(b).start()

    for b in range(len(sources)):

        @pl.when(flags_ref[b] > 0)
        def _():
            code = code_ref[b]
            allowed = jnp.concatenate(
                [
                    jnp.broadcast_to(
                        qclip[i * piece : (i + 1) * piece] == code[i : i + 1, :],
                        (piece, code.shape[1]),
                    )
                    for i in range(sub_rows)
                ],
                axis=0,
            )
            bias_ref[b] = jnp.where(allowed, 0.0, -1e30).astype(jnp.float32)

    m_ref[...] = jnp.full(m_ref.shape, -1e30, jnp.float32)
    l_ref[...] = jnp.zeros(l_ref.shape, jnp.float32)
    acc_ref[...] = jnp.zeros(acc_ref.shape, jnp.float32)

    def scores(b, hp, e):
        cols = slice(hp * pair, (hp + 1) * pair)
        k_p = kv_buf[b, 0, :, cols]
        s = lax.dot_general(
            q_ref[e, :, cols], k_p, (((1,), (1,)), ((), ())), preferred_element_type=jnp.float32
        )
        return s + bias_ref[b]

    for b in range(len(sources)):

        @pl.when(flags_ref[b] > 0)
        def _():
            fetch(b).wait()
            for hp in range(col_count // pair):
                for e in range(2):
                    h = 2 * hp + e
                    m_ref[h] = jnp.maximum(m_ref[h], jnp.max(scores(b, hp, e), axis=1, keepdims=True))

    for b in range(len(sources)):

        @pl.when(flags_ref[b] > 0)
        def _():
            for hp in range(col_count // pair):
                cols = slice(hp * pair, (hp + 1) * pair)
                v_p = kv_buf[b, 1, :, cols]
                pvs = []
                for e in range(2):
                    h = 2 * hp + e
                    p = jnp.exp(scores(b, hp, e) - m_ref[h])
                    l_ref[h] = l_ref[h] + jnp.sum(p, axis=1, keepdims=True)
                    pvs.append(
                        jnp.dot(p.astype(jnp.bfloat16), v_p, preferred_element_type=jnp.float32)
                    )
                acc_ref[:, cols] = acc_ref[:, cols] + jnp.where(low, pvs[0], pvs[1])

    for hp in range(col_count // pair):
        cols = slice(hp * pair, (hp + 1) * pair)
        den = jnp.where(low, l_ref[2 * hp], l_ref[2 * hp + 1])
        out_ref[:, cols] = (acc_ref[:, cols] / den).astype(out_ref.dtype)


def attend_chunk(state_now, q_split, query_clip, mask_rows, clip_ends, total, inputs, blocks):
    block_total = mask_rows.shape[1]
    sub_rows = mask_rows.shape[0]
    key_pos = jnp.stack([pos for _, _, pos in blocks])
    key_block = key_pos[:, ::BLK] // BLK
    valid = (key_block >= 0) & (key_block < block_total)
    live = jnp.take(mask_rows, jnp.clip(key_block, 0, block_total - 1), axis=1)
    live = jnp.repeat((live == 1) & valid[None], BLK, axis=2)
    key_clip = clip_index(key_pos.reshape(-1), clip_ends).reshape(key_pos.shape)
    code = jnp.where(live, key_clip[None], -1).transpose(1, 0, 2)
    query_sub = query_clip.reshape(sub_rows, -1)
    flags = jnp.any(
        query_sub[None, :, :, None] == code[:, :, None, :], axis=(1, 2, 3)
    ).astype(jnp.int32)
    sources = tuple((src, idx) for src, idx, _ in blocks)
    n_in = len(inputs)
    has_state = state_now is not None
    final = not has_state
    row_count, col_count = q_split.shape[1:]
    state_shape = jax.ShapeDtypeStruct((row_count, col_count), jnp.float32)
    if final:
        out_shape = jax.ShapeDtypeStruct((row_count, col_count), jnp.bfloat16)
        out_specs = pl.BlockSpec(memory_space=pltpu.VMEM)
        head_count = col_count // HD
        scratch = [
            pltpu.VMEM((len(blocks), row_count, row_count), jnp.float32),
            pltpu.VMEM((head_count, row_count, 1), jnp.float32),
            pltpu.VMEM((head_count, row_count, 1), jnp.float32),
            pltpu.VMEM((row_count, col_count), jnp.float32),
            pltpu.VMEM((len(blocks),) + inputs[0].shape[1:], inputs[0].dtype),
            pltpu.SemaphoreType.DMA((len(blocks),)),
        ]
        aliases = {}
        extra = ()
        q_split = (q_split.astype(jnp.float32) * (1.0 / math.sqrt(HD))).astype(jnp.bfloat16)
    else:
        out_shape = (state_shape,) * 3
        out_specs = [pl.BlockSpec(memory_space=pltpu.VMEM)] * 3
        scratch = []
        aliases = {4 + n_in: 0, 5 + n_in: 1, 6 + n_in: 2}
        extra = tuple(state_now)
    return pl.pallas_call(
        functools.partial(whole_kernel, sources)
        if final
        else functools.partial(chunk_kernel, sources, has_state, final),
        out_shape=out_shape,
        in_specs=[pl.BlockSpec(memory_space=pltpu.SMEM)]
        + [pl.BlockSpec(memory_space=pltpu.VMEM)] * 3
        + [pl.BlockSpec(memory_space=pl.ANY if final else pltpu.VMEM)] * n_in
        + [pl.BlockSpec(memory_space=pltpu.VMEM)] * len(extra),
        out_specs=out_specs,
        scratch_shapes=scratch,
        input_output_aliases=aliases,
        cost_estimate=pl.CostEstimate(
            flops=len(blocks) * 8 * row_count**2 * col_count,
            transcendentals=len(blocks) * 2 * row_count**2 * col_count // HD,
            bytes_accessed=sum(x.size * x.dtype.itemsize for x in inputs) + 8 * q_split.size,
        ),
    )(flags, q_split, code, query_clip[:, None], *inputs, *extra)


def body(query_rows, key_rows, value_rows, clip_lengths, block_mask, out_weight, norm_gain):
    row_count, col_count = query_rows.shape
    head_count = col_count // HD
    n_seq = lax.axis_size("seq")
    n_sub = lax.axis_size("sub")
    n_head = lax.axis_size("head")
    seq_i = lax.axis_index("seq")
    sub_i = lax.axis_index("sub")
    head_i = lax.axis_index("head")
    chip_rows = row_count * n_sub
    total = chip_rows * n_seq
    longest = total // 2
    reach = min(n_seq - 1, 1 + (longest - 2) // chip_rows)

    clip_ends = jnp.cumsum(clip_lengths)
    token_first = (seq_i * n_sub + sub_i) * row_count
    mask_height = row_count // BLK
    mask_rows = lax.dynamic_slice_in_dim(block_mask, sub_i * mask_height, mask_height, 0)
    query_clip = clip_index(token_first + jnp.arange(row_count, dtype=jnp.int32), clip_ends)
    local_pos = jnp.arange(row_count, dtype=jnp.int32)

    def block_pos(seq_off, sub_src):
        return ((seq_i + seq_off) * n_sub + sub_src) * row_count + local_pos

    lane = lax.broadcasted_iota(jnp.int32, (1, col_count), 1) % (2 * HD)
    q_split = jnp.stack(
        [jnp.where(lane < HD, query_rows, 0), jnp.where(lane >= HD, query_rows, 0)]
    ).astype(jnp.bfloat16)

    def fold(state_now, mine, theirs):
        inputs = [kv[None] for kv, _ in mine]
        blocks = [(n, 0, block_pos(off, sub_i)) for n, (_, off) in enumerate(mine)]
        for got, offs, src in theirs:
            if isinstance(got, list):
                for piece, off in zip(got, offs):
                    blocks.append((len(inputs), 0, block_pos(off, src)))
                    inputs.append(piece[None])
            else:
                blocks += [(len(inputs), b, block_pos(off, src)) for b, off in enumerate(offs)]
                inputs.append(got)
        return attend_chunk(
            state_now, q_split, query_clip, mask_rows, clip_ends, total, inputs, blocks
        )

    def to_partner(mine):
        offs = [jnp.asarray(off, jnp.int32) for _, off in mine]
        return [
            (jnp.stack([rotated(kv, "sub", n_sub, j) for kv, _ in mine]), offs, (sub_i - j) % n_sub)
            for j in range(1, n_sub)
        ]

    def to_partner_apart(mine):
        offs = [off for _, off in mine]
        return [
            ([rotated(kv, "sub", n_sub, j) for kv, _ in mine], offs, (sub_i - j) % n_sub)
            for j in range(1, n_sub)
        ]

    own = jnp.stack([key_rows, value_rows])
    if reach <= 4:
        to_partner = to_partner_apart
        mine = [(own, 0)]
        theirs = to_partner(mine)
        left = own
        right = own
        for step in range(1, reach + 1):
            right = shifted(right, "seq", n_seq, 1)
            left = shifted(left, "seq", n_seq, -1)
            near = [(left, -step), (right, step)]
            mine += near
            theirs += to_partner(near)
        attended = fold(None, mine, theirs)
    else:
        state = (
            jnp.full((row_count, col_count), -1e30, jnp.float32),
            jnp.zeros((row_count, col_count), jnp.float32),
            jnp.zeros((row_count, col_count), jnp.float32),
        )
        state = fold(state, [(own, 0)], [])
        pending = to_partner([(own, 0)])

        def seq_step(step, carry):
            state_now, left, right, pending_now = carry
            right = shifted(right, "seq", n_seq, 1)
            left = shifted(left, "seq", n_seq, -1)
            near = [(left, -step), (right, step)]
            state_now = fold(state_now, near, pending_now)
            return (state_now, left, right, to_partner(near))

        carry = seq_step(1, (state, own, own, pending))
        carry = lax.fori_loop(2, reach + 1, seq_step, carry)
        state = fold(carry[0], [], carry[3])
        row_max, running, weighted = state
        attended = (weighted / running).astype(jnp.bfloat16)

    n_dev = n_seq * n_sub

    def flat(dev, head):
        return ((dev // n_sub) * n_head + head) * n_sub + dev % n_sub

    pieces = {-1: attended[row_count - F :], 0: attended, 1: attended[:F]}
    width = out_weight.shape[1]
    projected = jnp.zeros((row_count + 2 * F, width), jnp.float32)
    for j in range(n_head):
        parts = []
        for d in (-1, 0, 1):
            if j == 0 and d == 0:
                parts.append(attended)
                continue
            pairs = [
                (flat(i + d, (h + j) % n_head), flat(i, h))
                for i in range(n_dev)
                for h in range(n_head)
                if 0 <= i + d < n_dev
            ]
            parts.append(lax.ppermute(pieces[d], ("seq", "head", "sub"), pairs))
        src = (head_i + j) % n_head
        projected = projected + jnp.dot(
            jnp.concatenate(parts, axis=0),
            lax.dynamic_slice_in_dim(out_weight, src * col_count, col_count, 0),
            preferred_element_type=jnp.float32,
        )

    positions = token_first + jnp.arange(row_count, dtype=jnp.int32)
    clip_here = clip_index(positions, clip_ends)
    earlier = jnp.where(
        (clip_index(positions - F, clip_ends) == clip_here)[:, None], projected[:row_count], 0.0
    )
    later = jnp.where(
        (clip_index(positions + F, clip_ends) == clip_here)[:, None], projected[2 * F :], 0.0
    )
    blended = projected[F : F + row_count] + 0.5 * (earlier + later)
    squares = jnp.sum(blended * blended, axis=1)
    scale = lax.rsqrt(squares / width + 1e-06)
    own_cols = lax.dynamic_slice_in_dim(blended, head_i * col_count, col_count, 1)
    return (own_cols * scale[:, None] * norm_gain.astype(jnp.float32)).astype(jnp.bfloat16)


def solution(mesh):
    placed = (
        P(("grp", "seq", "sub"), "head"),
        P(("grp", "seq", "sub"), "head"),
        P(("grp", "seq", "sub"), "head"),
        P("grp"),
        P(("grp", "seq"), None),
        P(),
        P("head"),
    )
    return jax.shard_map(
        body,
        mesh=mesh,
        in_specs=placed,
        out_specs=P(("grp", "seq", "sub"), "head"),
        check_vma=False,
    )
```

```python
import functools
import math

import jax
import jax.numpy as jnp
from jax.experimental import pallas as pl
from jax.experimental.pallas import tpu as pltpu
from jax import lax
from jax.sharding import PartitionSpec as P

HD = 64
BLK = 64
F = 64


def clip_index(positions, clip_ends):
    return jnp.sum((clip_ends[None, :] <= positions[:, None]).astype(jnp.int32), axis=1)


def shifted(x, axis, count, step):
    pairs = [(i + step, i) for i in range(count) if 0 <= i + step < count]
    return lax.ppermute(x, axis, pairs)


def rotated(x, axis, count, step):
    return lax.ppermute(x, axis, [(i, (i + step) % count) for i in range(count)])


def chunk_kernel(sources, has_state, final, flags_ref, q_ref, code_ref, qclip_ref, *refs):
    n_in = max(src for src, _ in sources) + 1
    kv_refs = refs[:n_in]
    rest = refs[n_in:]
    if has_state:
        m_in, l_in, acc_in = rest[:3]
        rest = rest[3:]
    if final:
        out_ref, m_ref, l_ref, acc_ref = rest
    else:
        m_ref, l_ref, acc_ref = rest
    row_count, col_count = acc_ref.shape
    sub_rows = code_ref.shape[1]
    piece = row_count // sub_rows
    pair = 2 * HD
    scale = 1.0 / math.sqrt(HD)
    if has_state:
        m_ref[...] = m_in[...]
        l_ref[...] = l_in[...]
        acc_ref[...] = acc_in[...]
    else:
        m_ref[...] = jnp.full(m_ref.shape, -1e30, jnp.float32)
        l_ref[...] = jnp.zeros(l_ref.shape, jnp.float32)
        acc_ref[...] = jnp.zeros(acc_ref.shape, jnp.float32)
    qclip = qclip_ref[...]
    low = lax.broadcasted_iota(jnp.int32, (row_count, pair), 1) < HD
    for b, (src, idx) in enumerate(sources):

        @pl.when(flags_ref[b] > 0)
        def _():
            code = code_ref[b]
            allowed = jnp.concatenate(
                [
                    jnp.broadcast_to(
                        qclip[i * piece : (i + 1) * piece] == code[i : i + 1, :],
                        (piece, code.shape[1]),
                    )
                    for i in range(sub_rows)
                ],
                axis=0,
            )
            bias = jnp.where(allowed, 0.0, -1e30).astype(jnp.float32)
            for hp in range(col_count // pair):
                cols = slice(hp * pair, (hp + 1) * pair)
                k_p = kv_refs[src][idx, 0, :, cols]
                v_p = kv_refs[src][idx, 1, :, cols]
                m_p = m_ref[:, cols]
                halves = []
                for e in range(2):
                    q_e = q_ref[e, :, cols]
                    s = lax.dot_general(
                        q_e, k_p, (((1,), (1,)), ((), ())), preferred_element_type=jnp.float32
                    )
                    s = s * scale + bias
                    m_old = m_p[:, e * HD : e * HD + 1]
                    m_new = jnp.maximum(m_old, jnp.max(s, axis=1, keepdims=True))
                    alpha = jnp.exp(m_old - m_new)
                    p = jnp.exp(s - m_new)
                    total = jnp.sum(p, axis=1, keepdims=True)
                    pv = jnp.dot(p.astype(jnp.bfloat16), v_p, preferred_element_type=jnp.float32)
                    halves.append((m_new, alpha, total, pv))
                (m0, a0, t0, pv0), (m1, a1, t1, pv1) = halves
                alpha = jnp.where(low, a0, a1)
                m_ref[:, cols] = jnp.where(low, m0, m1)
                l_ref[:, cols] = alpha * l_ref[:, cols] + jnp.where(low, t0, t1)
                acc_ref[:, cols] = alpha * acc_ref[:, cols] + jnp.where(low, pv0, pv1)

    if final:
        out_ref[...] = (acc_ref[...] / l_ref[...]).astype(out_ref.dtype)


def whole_kernel(sources, flags_ref, q_ref, code_ref, qclip_ref, *refs):
    n_in = max(src for src, _ in sources) + 1
    kv_hbm = refs[:n_in]
    out_ref, bias_ref, m_ref, l_ref, acc_ref, kv_buf, sems = refs[n_in:]
    row_count, col_count = out_ref.shape
    sub_rows = code_ref.shape[1]
    piece = row_count // sub_rows
    pair = 2 * HD
    qclip = qclip_ref[...]
    low = lax.broadcasted_iota(jnp.int32, (row_count, pair), 1) < HD

    def fetch(b):
        src, idx = sources[b]
        return pltpu.make_async_copy(kv_hbm[src].at[idx], kv_buf.at[b], sems.at[b])

    for b in range(len(sources)):

        @pl.when(flags_ref[b] > 0)
        def _():
            fetch(b).start()

    for b in range(len(sources)):

        @pl.when(flags_ref[b] > 0)
        def _():
            code = code_ref[b]
            allowed = jnp.concatenate(
                [
                    jnp.broadcast_to(
                        qclip[i * piece : (i + 1) * piece] == code[i : i + 1, :],
                        (piece, code.shape[1]),
                    )
                    for i in range(sub_rows)
                ],
                axis=0,
            )
            bias_ref[b] = jnp.where(allowed, 0.0, -1e30).astype(jnp.float32)

    m_ref[...] = jnp.full(m_ref.shape, -1e30, jnp.float32)
    l_ref[...] = jnp.zeros(l_ref.shape, jnp.float32)
    acc_ref[...] = jnp.zeros(acc_ref.shape, jnp.float32)

    def scores(b, hp, e):
        cols = slice(hp * pair, (hp + 1) * pair)
        k_p = kv_buf[b, 0, :, cols]
        s = lax.dot_general(
            q_ref[e, :, cols], k_p, (((1,), (1,)), ((), ())), preferred_element_type=jnp.float32
        )
        return s + bias_ref[b]

    for b in range(len(sources)):

        @pl.when(flags_ref[b] > 0)
        def _():
            fetch(b).wait()
            for hp in range(col_count // pair):
                for e in range(2):
                    h = 2 * hp + e
                    m_ref[h] = jnp.maximum(m_ref[h], jnp.max(scores(b, hp, e), axis=1, keepdims=True))

    for b in range(len(sources)):

        @pl.when(flags_ref[b] > 0)
        def _():
            for hp in range(col_count // pair):
                cols = slice(hp * pair, (hp + 1) * pair)
                v_p = kv_buf[b, 1, :, cols]
                pvs = []
                for e in range(2):
                    h = 2 * hp + e
                    p = jnp.exp(scores(b, hp, e) - m_ref[h])
                    l_ref[h] = l_ref[h] + jnp.sum(p, axis=1, keepdims=True)
                    pvs.append(
                        jnp.dot(p.astype(jnp.bfloat16), v_p, preferred_element_type=jnp.float32)
                    )
                acc_ref[:, cols] = acc_ref[:, cols] + jnp.where(low, pvs[0], pvs[1])

    for hp in range(col_count // pair):
        cols = slice(hp * pair, (hp + 1) * pair)
        den = jnp.where(low, l_ref[2 * hp], l_ref[2 * hp + 1])
        out_ref[:, cols] = (acc_ref[:, cols] / den).astype(out_ref.dtype)


def attend_chunk(state_now, q_split, query_clip, mask_rows, clip_ends, total, inputs, blocks):
    block_total = mask_rows.shape[1]
    sub_rows = mask_rows.shape[0]
    key_pos = jnp.stack([pos for _, _, pos in blocks])
    key_block = key_pos[:, ::BLK] // BLK
    valid = (key_block >= 0) & (key_block < block_total)
    live = jnp.take(mask_rows, jnp.clip(key_block, 0, block_total - 1), axis=1)
    live = jnp.repeat((live == 1) & valid[None], BLK, axis=2)
    key_clip = clip_index(key_pos.reshape(-1), clip_ends).reshape(key_pos.shape)
    code = jnp.where(live, key_clip[None], -1).transpose(1, 0, 2)
    query_sub = query_clip.reshape(sub_rows, -1)
    flags = jnp.any(
        query_sub[None, :, :, None] == code[:, :, None, :], axis=(1, 2, 3)
    ).astype(jnp.int32)
    sources = tuple((src, idx) for src, idx, _ in blocks)
    n_in = len(inputs)
    has_state = state_now is not None
    final = not has_state
    row_count, col_count = q_split.shape[1:]
    state_shape = jax.ShapeDtypeStruct((row_count, col_count), jnp.float32)
    if final:
        out_shape = jax.ShapeDtypeStruct((row_count, col_count), jnp.bfloat16)
        out_specs = pl.BlockSpec(memory_space=pltpu.VMEM)
        head_count = col_count // HD
        scratch = [
            pltpu.VMEM((len(blocks), row_count, row_count), jnp.float32),
            pltpu.VMEM((head_count, row_count, 1), jnp.float32),
            pltpu.VMEM((head_count, row_count, 1), jnp.float32),
            pltpu.VMEM((row_count, col_count), jnp.float32),
            pltpu.VMEM((len(blocks),) + inputs[0].shape[1:], inputs[0].dtype),
            pltpu.SemaphoreType.DMA((len(blocks),)),
        ]
        aliases = {}
        extra = ()
        q_split = (q_split.astype(jnp.float32) * (1.0 / math.sqrt(HD))).astype(jnp.bfloat16)
    else:
        out_shape = (state_shape,) * 3
        out_specs = [pl.BlockSpec(memory_space=pltpu.VMEM)] * 3
        scratch = []
        aliases = {4 + n_in: 0, 5 + n_in: 1, 6 + n_in: 2}
        extra = tuple(state_now)
    return pl.pallas_call(
        functools.partial(whole_kernel, sources)
        if final
        else functools.partial(chunk_kernel, sources, has_state, final),
        out_shape=out_shape,
        in_specs=[pl.BlockSpec(memory_space=pltpu.SMEM)]
        + [pl.BlockSpec(memory_space=pltpu.VMEM)] * 3
        + [pl.BlockSpec(memory_space=pl.ANY if final else pltpu.VMEM)] * n_in
        + [pl.BlockSpec(memory_space=pltpu.VMEM)] * len(extra),
        out_specs=out_specs,
        scratch_shapes=scratch,
        input_output_aliases=aliases,
        cost_estimate=pl.CostEstimate(
            flops=len(blocks) * 8 * row_count**2 * col_count,
            transcendentals=len(blocks) * 2 * row_count**2 * col_count // HD,
            bytes_accessed=sum(x.size * x.dtype.itemsize for x in inputs) + 8 * q_split.size,
        ),
    )(flags, q_split, code, query_clip[:, None], *inputs, *extra)


def body(query_rows, key_rows, value_rows, clip_lengths, block_mask, out_weight, norm_gain):
    row_count, col_count = query_rows.shape
    head_count = col_count // HD
    n_seq = lax.axis_size("seq")
    n_sub = lax.axis_size("sub")
    n_head = lax.axis_size("head")
    seq_i = lax.axis_index("seq")
    sub_i = lax.axis_index("sub")
    head_i = lax.axis_index("head")
    chip_rows = row_count * n_sub
    total = chip_rows * n_seq
    longest = total // 2
    reach = min(n_seq - 1, 1 + (longest - 2) // chip_rows)

    clip_ends = jnp.cumsum(clip_lengths)
    token_first = (seq_i * n_sub + sub_i) * row_count
    mask_height = row_count // BLK
    mask_rows = lax.dynamic_slice_in_dim(block_mask, sub_i * mask_height, mask_height, 0)
    query_clip = clip_index(token_first + jnp.arange(row_count, dtype=jnp.int32), clip_ends)
    local_pos = jnp.arange(row_count, dtype=jnp.int32)

    def block_pos(seq_off, sub_src):
        return ((seq_i + seq_off) * n_sub + sub_src) * row_count + local_pos

    lane = lax.broadcasted_iota(jnp.int32, (1, col_count), 1) % (2 * HD)
    q_split = jnp.stack(
        [jnp.where(lane < HD, query_rows, 0), jnp.where(lane >= HD, query_rows, 0)]
    ).astype(jnp.bfloat16)

    def fold(state_now, mine, theirs):
        inputs = [kv[None] for kv, _ in mine]
        blocks = [(n, 0, block_pos(off, sub_i)) for n, (_, off) in enumerate(mine)]
        for got, offs, src in theirs:
            if isinstance(got, list):
                for piece, off in zip(got, offs):
                    blocks.append((len(inputs), 0, block_pos(off, src)))
                    inputs.append(piece[None])
            else:
                blocks += [(len(inputs), b, block_pos(off, src)) for b, off in enumerate(offs)]
                inputs.append(got)
        return attend_chunk(
            state_now, q_split, query_clip, mask_rows, clip_ends, total, inputs, blocks
        )

    def to_partner(mine):
        offs = [jnp.asarray(off, jnp.int32) for _, off in mine]
        return [
            (jnp.stack([rotated(kv, "sub", n_sub, j) for kv, _ in mine]), offs, (sub_i - j) % n_sub)
            for j in range(1, n_sub)
        ]

    def to_partner_apart(mine):
        offs = [off for _, off in mine]
        return [
            ([rotated(kv, "sub", n_sub, j) for kv, _ in mine], offs, (sub_i - j) % n_sub)
            for j in range(1, n_sub)
        ]

    own = jnp.stack([key_rows, value_rows])
    if reach <= 4:
        to_partner = to_partner_apart
        mine = [(own, 0)]
        theirs = to_partner(mine)
        left = own
        right = own
        for step in range(1, reach + 1):
            right = shifted(right, "seq", n_seq, 1)
            left = shifted(left, "seq", n_seq, -1)
            near = [(left, -step), (right, step)]
            mine += near
            theirs += to_partner(near)
        attended = fold(None, mine, theirs)
    else:
        state = (
            jnp.full((row_count, col_count), -1e30, jnp.float32),
            jnp.zeros((row_count, col_count), jnp.float32),
            jnp.zeros((row_count, col_count), jnp.float32),
        )
        state = fold(state, [(own, 0)], [])
        pending = to_partner([(own, 0)])

        def seq_step(step, carry):
            state_now, left, right, pending_now = carry
            right = shifted(right, "seq", n_seq, 1)
            left = shifted(left, "seq", n_seq, -1)
            near = [(left, -step), (right, step)]
            state_now = fold(state_now, near, pending_now)
            return (state_now, left, right, to_partner(near))

        carry = seq_step(1, (state, own, own, pending))
        carry = lax.fori_loop(2, reach + 1, seq_step, carry)
        state = fold(carry[0], [], carry[3])
        row_max, running, weighted = state
        attended = (weighted / running).astype(jnp.bfloat16)

    n_dev = n_seq * n_sub
    width = out_weight.shape[1]
    projected = jnp.dot(
        attended,
        lax.dynamic_slice_in_dim(out_weight, head_i * col_count, col_count, 0),
        preferred_element_type=jnp.float32,
    )
    for j in range(1, n_head):
        got = rotated(attended, "head", n_head, j)
        src = (head_i - j) % n_head
        projected = projected + jnp.dot(
            got,
            lax.dynamic_slice_in_dim(out_weight, src * col_count, col_count, 0),
            preferred_element_type=jnp.float32,
        )
    prev_tail = shifted(projected[row_count - F :], ("seq", "sub"), n_dev, -1)
    next_head = shifted(projected[:F], ("seq", "sub"), n_dev, 1)
    projected = jnp.concatenate([prev_tail, projected, next_head], axis=0)

    positions = token_first + jnp.arange(row_count, dtype=jnp.int32)
    clip_here = clip_index(positions, clip_ends)
    earlier = jnp.where(
        (clip_index(positions - F, clip_ends) == clip_here)[:, None], projected[:row_count], 0.0
    )
    later = jnp.where(
        (clip_index(positions + F, clip_ends) == clip_here)[:, None], projected[2 * F :], 0.0
    )
    blended = projected[F : F + row_count] + 0.5 * (earlier + later)
    squares = jnp.sum(blended * blended, axis=1)
    scale = lax.rsqrt(squares / width + 1e-06)
    own_cols = lax.dynamic_slice_in_dim(blended, head_i * col_count, col_count, 1)
    return (own_cols * scale[:, None] * norm_gain.astype(jnp.float32)).astype(jnp.bfloat16)


def solution(mesh):
    placed = (
        P(("grp", "seq", "sub"), "head"),
        P(("grp", "seq", "sub"), "head"),
        P(("grp", "seq", "sub"), "head"),
        P("grp"),
        P(("grp", "seq"), None),
        P(),
        P("head"),
    )
    return jax.shard_map(
        body,
        mesh=mesh,
        in_specs=placed,
        out_specs=P(("grp", "seq", "sub"), "head"),
        check_vma=False,
    )
```

```python
import functools
import math

import jax
import jax.numpy as jnp
from jax.experimental import pallas as pl
from jax.experimental.pallas import tpu as pltpu
from jax import lax
from jax.sharding import PartitionSpec as P

HD = 64
BLK = 64
F = 64


def clip_index(positions, clip_ends):
    return jnp.sum((clip_ends[None, :] <= positions[:, None]).astype(jnp.int32), axis=1)


def shifted(x, axis, count, step):
    pairs = [(i + step, i) for i in range(count) if 0 <= i + step < count]
    return lax.ppermute(x, axis, pairs)


def rotated(x, axis, count, step):
    return lax.ppermute(x, axis, [(i, (i + step) % count) for i in range(count)])


def chunk_kernel(sources, has_state, final, flags_ref, q_ref, code_ref, qclip_ref, *refs):
    n_in = max(src for src, _ in sources) + 1
    kv_refs = refs[:n_in]
    rest = refs[n_in:]
    if has_state:
        m_in, l_in, acc_in = rest[:3]
        rest = rest[3:]
    if final:
        out_ref, m_ref, l_ref, acc_ref = rest
    else:
        m_ref, l_ref, acc_ref = rest
    row_count, col_count = acc_ref.shape
    sub_rows = code_ref.shape[1]
    piece = row_count // sub_rows
    pair = 2 * HD
    scale = 1.0 / math.sqrt(HD)
    if has_state:
        m_ref[...] = m_in[...]
        l_ref[...] = l_in[...]
        acc_ref[...] = acc_in[...]
    else:
        m_ref[...] = jnp.full(m_ref.shape, -1e30, jnp.float32)
        l_ref[...] = jnp.zeros(l_ref.shape, jnp.float32)
        acc_ref[...] = jnp.zeros(acc_ref.shape, jnp.float32)
    qclip = qclip_ref[...]
    low = lax.broadcasted_iota(jnp.int32, (row_count, pair), 1) < HD
    for b, (src, idx) in enumerate(sources):

        @pl.when(flags_ref[b] > 0)
        def _():
            code = code_ref[b]
            allowed = jnp.concatenate(
                [
                    jnp.broadcast_to(
                        qclip[i * piece : (i + 1) * piece] == code[i : i + 1, :],
                        (piece, code.shape[1]),
                    )
                    for i in range(sub_rows)
                ],
                axis=0,
            )
            bias = jnp.where(allowed, 0.0, -1e30).astype(jnp.float32)
            for hp in range(col_count // pair):
                cols = slice(hp * pair, (hp + 1) * pair)
                k_p = kv_refs[src][idx, 0, :, cols]
                v_p = kv_refs[src][idx, 1, :, cols]
                m_p = m_ref[:, cols]
                halves = []
                for e in range(2):
                    q_e = q_ref[e, :, cols]
                    s = lax.dot_general(
                        q_e, k_p, (((1,), (1,)), ((), ())), preferred_element_type=jnp.float32
                    )
                    s = s * scale + bias
                    m_old = m_p[:, e * HD : e * HD + 1]
                    m_new = jnp.maximum(m_old, jnp.max(s, axis=1, keepdims=True))
                    alpha = jnp.exp(m_old - m_new)
                    p = jnp.exp(s - m_new)
                    total = jnp.sum(p, axis=1, keepdims=True)
                    pv = jnp.dot(p.astype(jnp.bfloat16), v_p, preferred_element_type=jnp.float32)
                    halves.append((m_new, alpha, total, pv))
                (m0, a0, t0, pv0), (m1, a1, t1, pv1) = halves
                alpha = jnp.where(low, a0, a1)
                m_ref[:, cols] = jnp.where(low, m0, m1)
                l_ref[:, cols] = alpha * l_ref[:, cols] + jnp.where(low, t0, t1)
                acc_ref[:, cols] = alpha * acc_ref[:, cols] + jnp.where(low, pv0, pv1)

    if final:
        out_ref[...] = (acc_ref[...] / l_ref[...]).astype(out_ref.dtype)


def whole_kernel(sources, flags_ref, q_ref, code_ref, qclip_ref, *refs):
    n_in = max(src for src, _ in sources) + 1
    kv_hbm = refs[:n_in]
    out_ref, bias_ref, m_ref, l_ref, acc_ref, kv_buf, sems = refs[n_in:]
    row_count, col_count = out_ref.shape
    sub_rows = code_ref.shape[1]
    piece = row_count // sub_rows
    pair = 2 * HD
    qclip = qclip_ref[...]
    low = lax.broadcasted_iota(jnp.int32, (row_count, pair), 1) < HD

    def fetch(b):
        src, idx = sources[b]
        return pltpu.make_async_copy(kv_hbm[src].at[idx], kv_buf.at[b], sems.at[b])

    for b in range(len(sources)):

        @pl.when(flags_ref[b] > 0)
        def _():
            fetch(b).start()

    for b in range(len(sources)):

        @pl.when(flags_ref[b] > 0)
        def _():
            code = code_ref[b]
            allowed = jnp.concatenate(
                [
                    jnp.broadcast_to(
                        qclip[i * piece : (i + 1) * piece] == code[i : i + 1, :],
                        (piece, code.shape[1]),
                    )
                    for i in range(sub_rows)
                ],
                axis=0,
            )
            bias_ref[b] = jnp.where(allowed, 0.0, -1e30).astype(jnp.float32)

    m_ref[...] = jnp.full(m_ref.shape, -1e30, jnp.float32)
    l_ref[...] = jnp.zeros(l_ref.shape, jnp.float32)
    acc_ref[...] = jnp.zeros(acc_ref.shape, jnp.float32)

    def scores(b, hp, e):
        cols = slice(hp * pair, (hp + 1) * pair)
        k_p = kv_buf[b, 0, :, cols]
        s = lax.dot_general(
            q_ref[e, :, cols], k_p, (((1,), (1,)), ((), ())), preferred_element_type=jnp.float32
        )
        return s + bias_ref[b]

    for b in range(len(sources)):

        @pl.when(flags_ref[b] > 0)
        def _():
            fetch(b).wait()
            for hp in range(col_count // pair):
                for e in range(2):
                    h = 2 * hp + e
                    m_ref[h] = jnp.maximum(m_ref[h], jnp.max(scores(b, hp, e), axis=1, keepdims=True))

    for b in range(len(sources)):

        @pl.when(flags_ref[b] > 0)
        def _():
            for hp in range(col_count // pair):
                cols = slice(hp * pair, (hp + 1) * pair)
                v_p = kv_buf[b, 1, :, cols]
                pvs = []
                for e in range(2):
                    h = 2 * hp + e
                    p = jnp.exp(scores(b, hp, e) - m_ref[h])
                    l_ref[h] = l_ref[h] + jnp.sum(p, axis=1, keepdims=True)
                    pvs.append(
                        jnp.dot(p.astype(jnp.bfloat16), v_p, preferred_element_type=jnp.float32)
                    )
                acc_ref[:, cols] = acc_ref[:, cols] + jnp.where(low, pvs[0], pvs[1])

    for hp in range(col_count // pair):
        cols = slice(hp * pair, (hp + 1) * pair)
        den = jnp.where(low, l_ref[2 * hp], l_ref[2 * hp + 1])
        out_ref[:, cols] = (acc_ref[:, cols] / den).astype(out_ref.dtype)


def attend_chunk(state_now, q_split, query_clip, mask_rows, clip_ends, total, inputs, blocks):
    block_total = mask_rows.shape[1]
    sub_rows = mask_rows.shape[0]
    key_pos = jnp.stack([pos for _, _, pos in blocks])
    key_block = key_pos[:, ::BLK] // BLK
    valid = (key_block >= 0) & (key_block < block_total)
    live = jnp.take(mask_rows, jnp.clip(key_block, 0, block_total - 1), axis=1)
    live = jnp.repeat((live == 1) & valid[None], BLK, axis=2)
    key_clip = clip_index(key_pos.reshape(-1), clip_ends).reshape(key_pos.shape)
    code = jnp.where(live, key_clip[None], -1).transpose(1, 0, 2)
    query_sub = query_clip.reshape(sub_rows, -1)
    flags = jnp.any(
        query_sub[None, :, :, None] == code[:, :, None, :], axis=(1, 2, 3)
    ).astype(jnp.int32)
    sources = tuple((src, idx) for src, idx, _ in blocks)
    n_in = len(inputs)
    has_state = state_now is not None
    final = not has_state
    row_count, col_count = q_split.shape[1:]
    state_shape = jax.ShapeDtypeStruct((row_count, col_count), jnp.float32)
    if final:
        out_shape = jax.ShapeDtypeStruct((row_count, col_count), jnp.bfloat16)
        out_specs = pl.BlockSpec(memory_space=pltpu.VMEM)
        head_count = col_count // HD
        scratch = [
            pltpu.VMEM((len(blocks), row_count, row_count), jnp.float32),
            pltpu.VMEM((head_count, row_count, 1), jnp.float32),
            pltpu.VMEM((head_count, row_count, 1), jnp.float32),
            pltpu.VMEM((row_count, col_count), jnp.float32),
            pltpu.VMEM((len(blocks),) + inputs[0].shape[1:], inputs[0].dtype),
            pltpu.SemaphoreType.DMA((len(blocks),)),
        ]
        aliases = {}
        extra = ()
        q_split = (q_split.astype(jnp.float32) * (1.0 / math.sqrt(HD))).astype(jnp.bfloat16)
    else:
        out_shape = (state_shape,) * 3
        out_specs = [pl.BlockSpec(memory_space=pltpu.VMEM)] * 3
        scratch = []
        aliases = {4 + n_in: 0, 5 + n_in: 1, 6 + n_in: 2}
        extra = tuple(state_now)
    return pl.pallas_call(
        functools.partial(whole_kernel, sources)
        if final
        else functools.partial(chunk_kernel, sources, has_state, final),
        out_shape=out_shape,
        in_specs=[pl.BlockSpec(memory_space=pltpu.SMEM)]
        + [pl.BlockSpec(memory_space=pltpu.VMEM)] * 3
        + [pl.BlockSpec(memory_space=pl.ANY if final else pltpu.VMEM)] * n_in
        + [pl.BlockSpec(memory_space=pltpu.VMEM)] * len(extra),
        out_specs=out_specs,
        scratch_shapes=scratch,
        input_output_aliases=aliases,
        cost_estimate=pl.CostEstimate(
            flops=len(blocks) * 8 * row_count**2 * col_count,
            transcendentals=len(blocks) * 2 * row_count**2 * col_count // HD,
            bytes_accessed=sum(x.size * x.dtype.itemsize for x in inputs) + 8 * q_split.size,
        ),
    )(flags, q_split, code, query_clip[:, None], *inputs, *extra)


def body(query_rows, key_rows, value_rows, clip_lengths, block_mask, out_weight, norm_gain):
    row_count, col_count = query_rows.shape
    head_count = col_count // HD
    n_seq = lax.axis_size("seq")
    n_sub = lax.axis_size("sub")
    n_head = lax.axis_size("head")
    seq_i = lax.axis_index("seq")
    sub_i = lax.axis_index("sub")
    head_i = lax.axis_index("head")
    chip_rows = row_count * n_sub
    total = chip_rows * n_seq
    longest = total // 2
    reach = min(n_seq - 1, 1 + (longest - 2) // chip_rows)

    clip_ends = jnp.cumsum(clip_lengths)
    token_first = (seq_i * n_sub + sub_i) * row_count
    mask_height = row_count // BLK
    mask_rows = lax.dynamic_slice_in_dim(block_mask, sub_i * mask_height, mask_height, 0)
    query_clip = clip_index(token_first + jnp.arange(row_count, dtype=jnp.int32), clip_ends)
    local_pos = jnp.arange(row_count, dtype=jnp.int32)

    def block_pos(seq_off, sub_src):
        return ((seq_i + seq_off) * n_sub + sub_src) * row_count + local_pos

    lane = lax.broadcasted_iota(jnp.int32, (1, col_count), 1) % (2 * HD)
    q_split = jnp.stack(
        [jnp.where(lane < HD, query_rows, 0), jnp.where(lane >= HD, query_rows, 0)]
    ).astype(jnp.bfloat16)

    def fold(state_now, mine, theirs):
        inputs = [kv[None] for kv, _ in mine]
        blocks = [(n, 0, block_pos(off, sub_i)) for n, (_, off) in enumerate(mine)]
        for got, offs, src in theirs:
            if isinstance(got, list):
                for piece, off in zip(got, offs):
                    blocks.append((len(inputs), 0, block_pos(off, src)))
                    inputs.append(piece[None])
            else:
                blocks += [(len(inputs), b, block_pos(off, src)) for b, off in enumerate(offs)]
                inputs.append(got)
        return attend_chunk(
            state_now, q_split, query_clip, mask_rows, clip_ends, total, inputs, blocks
        )

    def to_partner(mine):
        offs = [jnp.asarray(off, jnp.int32) for _, off in mine]
        return [
            (jnp.stack([rotated(kv, "sub", n_sub, j) for kv, _ in mine]), offs, (sub_i - j) % n_sub)
            for j in range(1, n_sub)
        ]

    def to_partner_apart(mine):
        offs = [off for _, off in mine]
        return [
            ([rotated(kv, "sub", n_sub, j) for kv, _ in mine], offs, (sub_i - j) % n_sub)
            for j in range(1, n_sub)
        ]

    own = jnp.stack([key_rows, value_rows])
    dev_reach = 1 + (longest - 2) // row_count
    if reach <= 4:
        to_partner = to_partner_apart
        mine = [(own, 0)]
        theirs = to_partner(mine)
        left = own
        right = own
        for step in range(1, reach + 1):
            right = shifted(right, "seq", n_seq, 1)
            left = shifted(left, "seq", n_seq, -1)
            near = [(left, -step), (right, step)]
            mine += near
            if n_sub == 2 and 2 * step + 1 > dev_reach:
                sent = jnp.where(sub_i == 0, right, left)
                off = jnp.where(sub_i == 0, -step, step)
                theirs.append(([rotated(sent, "sub", n_sub, 1)], [off], 1 - sub_i))
            else:
                theirs += to_partner(near)
        attended = fold(None, mine, theirs)
    else:
        state = (
            jnp.full((row_count, col_count), -1e30, jnp.float32),
            jnp.zeros((row_count, col_count), jnp.float32),
            jnp.zeros((row_count, col_count), jnp.float32),
        )
        state = fold(state, [(own, 0)], [])
        pending = to_partner([(own, 0)])

        def seq_step(step, carry):
            state_now, left, right, pending_now = carry
            right = shifted(right, "seq", n_seq, 1)
            left = shifted(left, "seq", n_seq, -1)
            near = [(left, -step), (right, step)]
            state_now = fold(state_now, near, pending_now)
            return (state_now, left, right, to_partner(near))

        carry = seq_step(1, (state, own, own, pending))
        carry = lax.fori_loop(2, reach + 1, seq_step, carry)
        state = fold(carry[0], [], carry[3])
        row_max, running, weighted = state
        attended = (weighted / running).astype(jnp.bfloat16)

    n_dev = n_seq * n_sub
    width = out_weight.shape[1]
    projected = jnp.dot(
        attended,
        lax.dynamic_slice_in_dim(out_weight, head_i * col_count, col_count, 0),
        preferred_element_type=jnp.float32,
    )
    for j in range(1, n_head):
        got = rotated(attended, "head", n_head, j)
        src = (head_i - j) % n_head
        projected = projected + jnp.dot(
            got,
            lax.dynamic_slice_in_dim(out_weight, src * col_count, col_count, 0),
            preferred_element_type=jnp.float32,
        )
    prev_tail = shifted(projected[row_count - F :], ("seq", "sub"), n_dev, -1)
    next_head = shifted(projected[:F], ("seq", "sub"), n_dev, 1)
    projected = jnp.concatenate([prev_tail, projected, next_head], axis=0)

    positions = token_first + jnp.arange(row_count, dtype=jnp.int32)
    clip_here = clip_index(positions, clip_ends)
    earlier = jnp.where(
        (clip_index(positions - F, clip_ends) == clip_here)[:, None], projected[:row_count], 0.0
    )
    later = jnp.where(
        (clip_index(positions + F, clip_ends) == clip_here)[:, None], projected[2 * F :], 0.0
    )
    blended = projected[F : F + row_count] + 0.5 * (earlier + later)
    squares = jnp.sum(blended * blended, axis=1)
    scale = lax.rsqrt(squares / width + 1e-06)
    own_cols = lax.dynamic_slice_in_dim(blended, head_i * col_count, col_count, 1)
    return (own_cols * scale[:, None] * norm_gain.astype(jnp.float32)).astype(jnp.bfloat16)


def solution(mesh):
    placed = (
        P(("grp", "seq", "sub"), "head"),
        P(("grp", "seq", "sub"), "head"),
        P(("grp", "seq", "sub"), "head"),
        P("grp"),
        P(("grp", "seq"), None),
        P(),
        P("head"),
    )
    return jax.shard_map(
        body,
        mesh=mesh,
        in_specs=placed,
        out_specs=P(("grp", "seq", "sub"), "head"),
        check_vma=False,
    )
```

```python
import functools
import math

import jax
import jax.numpy as jnp
from jax.experimental import pallas as pl
from jax.experimental.pallas import tpu as pltpu
from jax import lax
from jax.sharding import PartitionSpec as P

HD = 64
BLK = 64
F = 64


def clip_index(positions, clip_ends):
    return jnp.sum((clip_ends[None, :] <= positions[:, None]).astype(jnp.int32), axis=1)


def shifted(x, axis, count, step):
    pairs = [(i + step, i) for i in range(count) if 0 <= i + step < count]
    return lax.ppermute(x, axis, pairs)


def rotated(x, axis, count, step):
    return lax.ppermute(x, axis, [(i, (i + step) % count) for i in range(count)])


def chunk_kernel(sources, has_state, final, flags_ref, q_ref, code_ref, qclip_ref, *refs):
    n_in = max(src for src, _ in sources) + 1
    kv_refs = refs[:n_in]
    rest = refs[n_in:]
    if has_state:
        m_in, l_in, acc_in = rest[:3]
        rest = rest[3:]
    if final:
        out_ref, m_ref, l_ref, acc_ref = rest
    else:
        m_ref, l_ref, acc_ref = rest
    row_count, col_count = acc_ref.shape
    sub_rows = code_ref.shape[1]
    piece = row_count // sub_rows
    pair = 2 * HD
    scale = 1.0 / math.sqrt(HD)
    if has_state:
        m_ref[...] = m_in[...]
        l_ref[...] = l_in[...]
        acc_ref[...] = acc_in[...]
    else:
        m_ref[...] = jnp.full(m_ref.shape, -1e30, jnp.float32)
        l_ref[...] = jnp.zeros(l_ref.shape, jnp.float32)
        acc_ref[...] = jnp.zeros(acc_ref.shape, jnp.float32)
    qclip = qclip_ref[...]
    low = lax.broadcasted_iota(jnp.int32, (row_count, pair), 1) < HD
    for b, (src, idx) in enumerate(sources):

        @pl.when(flags_ref[b] > 0)
        def _():
            code = code_ref[b]
            allowed = jnp.concatenate(
                [
                    jnp.broadcast_to(
                        qclip[i * piece : (i + 1) * piece] == code[i : i + 1, :],
                        (piece, code.shape[1]),
                    )
                    for i in range(sub_rows)
                ],
                axis=0,
            )
            bias = jnp.where(allowed, 0.0, -1e30).astype(jnp.float32)
            for hp in range(col_count // pair):
                cols = slice(hp * pair, (hp + 1) * pair)
                k_p = kv_refs[src][idx, 0, :, cols]
                v_p = kv_refs[src][idx, 1, :, cols]
                m_p = m_ref[:, cols]
                halves = []
                for e in range(2):
                    q_e = q_ref[e, :, cols]
                    s = lax.dot_general(
                        q_e, k_p, (((1,), (1,)), ((), ())), preferred_element_type=jnp.float32
                    )
                    s = s * scale + bias
                    m_old = m_p[:, e * HD : e * HD + 1]
                    m_new = jnp.maximum(m_old, jnp.max(s, axis=1, keepdims=True))
                    alpha = jnp.exp(m_old - m_new)
                    p = jnp.exp(s - m_new)
                    total = jnp.sum(p, axis=1, keepdims=True)
                    pv = jnp.dot(p.astype(jnp.bfloat16), v_p, preferred_element_type=jnp.float32)
                    halves.append((m_new, alpha, total, pv))
                (m0, a0, t0, pv0), (m1, a1, t1, pv1) = halves
                alpha = jnp.where(low, a0, a1)
                m_ref[:, cols] = jnp.where(low, m0, m1)
                l_ref[:, cols] = alpha * l_ref[:, cols] + jnp.where(low, t0, t1)
                acc_ref[:, cols] = alpha * acc_ref[:, cols] + jnp.where(low, pv0, pv1)

    if final:
        out_ref[...] = (acc_ref[...] / l_ref[...]).astype(out_ref.dtype)


def whole_kernel(sources, flags_ref, q_in, code_ref, meta_ref, *refs):
    n_in = max(src for src, _ in sources) + 1
    kv_hbm = refs[:n_in]
    out_ref, bias_ref, m_ref, l_ref, acc_ref, kv_buf, sems, q_ref = refs[n_in:]
    row_count, col_count = out_ref.shape
    sub_rows = code_ref.shape[1]
    piece = row_count // sub_rows
    pair = 2 * HD
    low = lax.broadcasted_iota(jnp.int32, (row_count, pair), 1) < HD

    def fetch(b):
        src, idx = sources[b]
        return pltpu.make_async_copy(kv_hbm[src].at[idx], kv_buf.at[b], sems.at[b])

    for b in range(len(sources)):

        @pl.when(flags_ref[b] > 0)
        def _():
            fetch(b).start()

    lane_low = lax.broadcasted_iota(jnp.int32, (row_count, col_count), 1) % pair < HD
    q_scaled = q_in[...].astype(jnp.float32) * (1.0 / math.sqrt(HD))
    q_ref[0] = jnp.where(lane_low, q_scaled, 0.0).astype(q_ref.dtype)
    q_ref[1] = jnp.where(lane_low, 0.0, q_scaled).astype(q_ref.dtype)
    q_pos = meta_ref[0] + lax.broadcasted_iota(jnp.int32, (row_count, 1), 0)
    qclip = jnp.zeros((row_count, 1), jnp.int32)
    for j in range(1, meta_ref.shape[0]):
        qclip = qclip + (q_pos >= meta_ref[j]).astype(jnp.int32)

    for b in range(len(sources)):

        @pl.when(flags_ref[b] > 0)
        def _():
            code = code_ref[b]
            allowed = jnp.concatenate(
                [
                    jnp.broadcast_to(
                        qclip[i * piece : (i + 1) * piece] == code[i : i + 1, :],
                        (piece, code.shape[1]),
                    )
                    for i in range(sub_rows)
                ],
                axis=0,
            )
            bias_ref[b] = jnp.where(allowed, 0.0, -1e30).astype(jnp.float32)

    m_ref[...] = jnp.full(m_ref.shape, -1e30, jnp.float32)
    l_ref[...] = jnp.zeros(l_ref.shape, jnp.float32)
    acc_ref[...] = jnp.zeros(acc_ref.shape, jnp.float32)

    def scores(b, hp, e):
        cols = slice(hp * pair, (hp + 1) * pair)
        k_p = kv_buf[b, 0, :, cols]
        s = lax.dot_general(
            q_ref[e, :, cols], k_p, (((1,), (1,)), ((), ())), preferred_element_type=jnp.float32
        )
        return s + bias_ref[b]

    for b in range(len(sources)):

        @pl.when(flags_ref[b] > 0)
        def _():
            fetch(b).wait()
            for hp in range(col_count // pair):
                for e in range(2):
                    h = 2 * hp + e
                    m_ref[h] = jnp.maximum(m_ref[h], jnp.max(scores(b, hp, e), axis=1, keepdims=True))

    for b in range(len(sources)):

        @pl.when(flags_ref[b] > 0)
        def _():
            for hp in range(col_count // pair):
                cols = slice(hp * pair, (hp + 1) * pair)
                v_p = kv_buf[b, 1, :, cols]
                pvs = []
                for e in range(2):
                    h = 2 * hp + e
                    p = jnp.exp(scores(b, hp, e) - m_ref[h])
                    l_ref[h] = l_ref[h] + jnp.sum(p, axis=1, keepdims=True)
                    pvs.append(
                        jnp.dot(p.astype(jnp.bfloat16), v_p, preferred_element_type=jnp.float32)
                    )
                acc_ref[:, cols] = acc_ref[:, cols] + jnp.where(low, pvs[0], pvs[1])

    for hp in range(col_count // pair):
        cols = slice(hp * pair, (hp + 1) * pair)
        den = jnp.where(low, l_ref[2 * hp], l_ref[2 * hp + 1])
        out_ref[:, cols] = (acc_ref[:, cols] / den).astype(out_ref.dtype)


def attend_chunk(
    state_now, q_split, query_clip, mask_rows, clip_ends, total, inputs, blocks, q_raw, meta
):
    block_total = mask_rows.shape[1]
    sub_rows = mask_rows.shape[0]
    key_pos = jnp.stack([pos for _, _, pos in blocks])
    key_block = key_pos[:, ::BLK] // BLK
    valid = (key_block >= 0) & (key_block < block_total)
    live = jnp.take(mask_rows, jnp.clip(key_block, 0, block_total - 1), axis=1)
    live = jnp.repeat((live == 1) & valid[None], BLK, axis=2)
    key_clip = clip_index(key_pos.reshape(-1), clip_ends).reshape(key_pos.shape)
    code = jnp.where(live, key_clip[None], -1).transpose(1, 0, 2)
    query_sub = query_clip.reshape(sub_rows, -1)
    flags = jnp.any(
        query_sub[None, :, :, None] == code[:, :, None, :], axis=(1, 2, 3)
    ).astype(jnp.int32)
    sources = tuple((src, idx) for src, idx, _ in blocks)
    n_in = len(inputs)
    has_state = state_now is not None
    final = not has_state
    row_count, col_count = q_split.shape[1:]
    state_shape = jax.ShapeDtypeStruct((row_count, col_count), jnp.float32)
    if final:
        out_shape = jax.ShapeDtypeStruct((row_count, col_count), jnp.bfloat16)
        out_specs = pl.BlockSpec(memory_space=pltpu.VMEM)
        head_count = col_count // HD
        scratch = [
            pltpu.VMEM((len(blocks), row_count, row_count), jnp.float32),
            pltpu.VMEM((head_count, row_count, 1), jnp.float32),
            pltpu.VMEM((head_count, row_count, 1), jnp.float32),
            pltpu.VMEM((row_count, col_count), jnp.float32),
            pltpu.VMEM((len(blocks),) + inputs[0].shape[1:], inputs[0].dtype),
            pltpu.SemaphoreType.DMA((len(blocks),)),
            pltpu.VMEM((2, row_count, col_count), jnp.bfloat16),
        ]
        aliases = {}
        extra = ()
    else:
        out_shape = (state_shape,) * 3
        out_specs = [pl.BlockSpec(memory_space=pltpu.VMEM)] * 3
        scratch = []
        aliases = {4 + n_in: 0, 5 + n_in: 1, 6 + n_in: 2}
        extra = tuple(state_now)
    return pl.pallas_call(
        functools.partial(whole_kernel, sources)
        if final
        else functools.partial(chunk_kernel, sources, has_state, final),
        out_shape=out_shape,
        in_specs=[pl.BlockSpec(memory_space=pltpu.SMEM)]
        + [pl.BlockSpec(memory_space=pltpu.VMEM)] * 2
        + [pl.BlockSpec(memory_space=pltpu.SMEM if final else pltpu.VMEM)]
        + [pl.BlockSpec(memory_space=pl.ANY if final else pltpu.VMEM)] * n_in
        + [pl.BlockSpec(memory_space=pltpu.VMEM)] * len(extra),
        out_specs=out_specs,
        scratch_shapes=scratch,
        input_output_aliases=aliases,
        cost_estimate=pl.CostEstimate(
            flops=len(blocks) * 8 * row_count**2 * col_count,
            transcendentals=len(blocks) * 2 * row_count**2 * col_count // HD,
            bytes_accessed=sum(x.size * x.dtype.itemsize for x in inputs) + 8 * q_split.size,
        ),
    )(flags, q_raw if final else q_split, code, meta if final else query_clip[:, None], *inputs, *extra)


def body(query_rows, key_rows, value_rows, clip_lengths, block_mask, out_weight, norm_gain):
    row_count, col_count = query_rows.shape
    head_count = col_count // HD
    n_seq = lax.axis_size("seq")
    n_sub = lax.axis_size("sub")
    n_head = lax.axis_size("head")
    seq_i = lax.axis_index("seq")
    sub_i = lax.axis_index("sub")
    head_i = lax.axis_index("head")
    chip_rows = row_count * n_sub
    total = chip_rows * n_seq
    longest = total // 2
    reach = min(n_seq - 1, 1 + (longest - 2) // chip_rows)

    clip_ends = jnp.cumsum(clip_lengths)
    token_first = (seq_i * n_sub + sub_i) * row_count
    mask_height = row_count // BLK
    mask_rows = lax.dynamic_slice_in_dim(block_mask, sub_i * mask_height, mask_height, 0)
    query_clip = clip_index(token_first + jnp.arange(row_count, dtype=jnp.int32), clip_ends)
    local_pos = jnp.arange(row_count, dtype=jnp.int32)

    def block_pos(seq_off, sub_src):
        return ((seq_i + seq_off) * n_sub + sub_src) * row_count + local_pos

    lane = lax.broadcasted_iota(jnp.int32, (1, col_count), 1) % (2 * HD)
    q_split = jnp.stack(
        [jnp.where(lane < HD, query_rows, 0), jnp.where(lane >= HD, query_rows, 0)]
    ).astype(jnp.bfloat16)

    def fold(state_now, mine, theirs):
        inputs = [kv[None] for kv, _ in mine]
        blocks = [(n, 0, block_pos(off, sub_i)) for n, (_, off) in enumerate(mine)]
        for got, offs, src in theirs:
            if isinstance(got, list):
                for piece, off in zip(got, offs):
                    blocks.append((len(inputs), 0, block_pos(off, src)))
                    inputs.append(piece[None])
            else:
                blocks += [(len(inputs), b, block_pos(off, src)) for b, off in enumerate(offs)]
                inputs.append(got)
        return attend_chunk(
            state_now, q_split, query_clip, mask_rows, clip_ends, total, inputs, blocks,
            query_rows, jnp.concatenate([token_first[None], clip_ends]).astype(jnp.int32),
        )

    def to_partner(mine):
        offs = [jnp.asarray(off, jnp.int32) for _, off in mine]
        return [
            (jnp.stack([rotated(kv, "sub", n_sub, j) for kv, _ in mine]), offs, (sub_i - j) % n_sub)
            for j in range(1, n_sub)
        ]

    def to_partner_apart(mine):
        offs = [off for _, off in mine]
        return [
            ([rotated(kv, "sub", n_sub, j) for kv, _ in mine], offs, (sub_i - j) % n_sub)
            for j in range(1, n_sub)
        ]

    own = jnp.stack([key_rows, value_rows])
    if reach <= 4:
        to_partner = to_partner_apart
        mine = [(own, 0)]
        theirs = to_partner(mine)
        left = own
        right = own
        for step in range(1, reach + 1):
            right = shifted(right, "seq", n_seq, 1)
            left = shifted(left, "seq", n_seq, -1)
            near = [(left, -step), (right, step)]
            mine += near
            theirs += to_partner(near)
        attended = fold(None, mine, theirs)
    else:
        state = (
            jnp.full((row_count, col_count), -1e30, jnp.float32),
            jnp.zeros((row_count, col_count), jnp.float32),
            jnp.zeros((row_count, col_count), jnp.float32),
        )
        state = fold(state, [(own, 0)], [])
        pending = to_partner([(own, 0)])

        def seq_step(step, carry):
            state_now, left, right, pending_now = carry
            right = shifted(right, "seq", n_seq, 1)
            left = shifted(left, "seq", n_seq, -1)
            near = [(left, -step), (right, step)]
            state_now = fold(state_now, near, pending_now)
            return (state_now, left, right, to_partner(near))

        carry = seq_step(1, (state, own, own, pending))
        carry = lax.fori_loop(2, reach + 1, seq_step, carry)
        state = fold(carry[0], [], carry[3])
        row_max, running, weighted = state
        attended = (weighted / running).astype(jnp.bfloat16)

    n_dev = n_seq * n_sub
    width = out_weight.shape[1]
    projected = jnp.dot(
        attended,
        lax.dynamic_slice_in_dim(out_weight, head_i * col_count, col_count, 0),
        preferred_element_type=jnp.float32,
    )
    for j in range(1, n_head):
        got = rotated(attended, "head", n_head, j)
        src = (head_i - j) % n_head
        projected = projected + jnp.dot(
            got,
            lax.dynamic_slice_in_dim(out_weight, src * col_count, col_count, 0),
            preferred_element_type=jnp.float32,
        )
    prev_tail = shifted(projected[row_count - F :], ("seq", "sub"), n_dev, -1)
    next_head = shifted(projected[:F], ("seq", "sub"), n_dev, 1)
    projected = jnp.concatenate([prev_tail, projected, next_head], axis=0)

    positions = token_first + jnp.arange(row_count, dtype=jnp.int32)
    clip_here = clip_index(positions, clip_ends)
    earlier = jnp.where(
        (clip_index(positions - F, clip_ends) == clip_here)[:, None], projected[:row_count], 0.0
    )
    later = jnp.where(
        (clip_index(positions + F, clip_ends) == clip_here)[:, None], projected[2 * F :], 0.0
    )
    blended = projected[F : F + row_count] + 0.5 * (earlier + later)
    squares = jnp.sum(blended * blended, axis=1)
    scale = lax.rsqrt(squares / width + 1e-06)
    own_cols = lax.dynamic_slice_in_dim(blended, head_i * col_count, col_count, 1)
    return (own_cols * scale[:, None] * norm_gain.astype(jnp.float32)).astype(jnp.bfloat16)


def solution(mesh):
    placed = (
        P(("grp", "seq", "sub"), "head"),
        P(("grp", "seq", "sub"), "head"),
        P(("grp", "seq", "sub"), "head"),
        P("grp"),
        P(("grp", "seq"), None),
        P(),
        P("head"),
    )
    return jax.shard_map(
        body,
        mesh=mesh,
        in_specs=placed,
        out_specs=P(("grp", "seq", "sub"), "head"),
        check_vma=False,
    )
```

```python
import functools
import math

import jax
import jax.numpy as jnp
from jax.experimental import pallas as pl
from jax.experimental.pallas import tpu as pltpu
from jax import lax
from jax.sharding import PartitionSpec as P

HD = 64
BLK = 64
F = 64


def clip_index(positions, clip_ends):
    return jnp.sum((clip_ends[None, :] <= positions[:, None]).astype(jnp.int32), axis=1)


def shifted(x, axis, count, step):
    pairs = [(i + step, i) for i in range(count) if 0 <= i + step < count]
    return lax.ppermute(x, axis, pairs)


def rotated(x, axis, count, step):
    return lax.ppermute(x, axis, [(i, (i + step) % count) for i in range(count)])


def chunk_kernel(sources, has_state, final, flags_ref, q_ref, code_ref, qclip_ref, *refs):
    n_in = max(src for src, _ in sources) + 1
    kv_refs = refs[:n_in]
    rest = refs[n_in:]
    if has_state:
        m_in, l_in, acc_in = rest[:3]
        rest = rest[3:]
    if final:
        out_ref, m_ref, l_ref, acc_ref = rest
    else:
        m_ref, l_ref, acc_ref = rest
    row_count, col_count = acc_ref.shape
    sub_rows = code_ref.shape[1]
    piece = row_count // sub_rows
    pair = 2 * HD
    scale = 1.0 / math.sqrt(HD)
    if has_state:
        m_ref[...] = m_in[...]
        l_ref[...] = l_in[...]
        acc_ref[...] = acc_in[...]
    else:
        m_ref[...] = jnp.full(m_ref.shape, -1e30, jnp.float32)
        l_ref[...] = jnp.zeros(l_ref.shape, jnp.float32)
        acc_ref[...] = jnp.zeros(acc_ref.shape, jnp.float32)
    qclip = qclip_ref[...]
    low = lax.broadcasted_iota(jnp.int32, (row_count, pair), 1) < HD
    for b, (src, idx) in enumerate(sources):

        @pl.when(flags_ref[b] > 0)
        def _():
            code = code_ref[b]
            allowed = jnp.concatenate(
                [
                    jnp.broadcast_to(
                        qclip[i * piece : (i + 1) * piece] == code[i : i + 1, :],
                        (piece, code.shape[1]),
                    )
                    for i in range(sub_rows)
                ],
                axis=0,
            )
            bias = jnp.where(allowed, 0.0, -1e30).astype(jnp.float32)
            for hp in range(col_count // pair):
                cols = slice(hp * pair, (hp + 1) * pair)
                k_p = kv_refs[src][idx, 0, :, cols]
                v_p = kv_refs[src][idx, 1, :, cols]
                m_p = m_ref[:, cols]
                halves = []
                for e in range(2):
                    q_e = q_ref[e, :, cols]
                    s = lax.dot_general(
                        q_e, k_p, (((1,), (1,)), ((), ())), preferred_element_type=jnp.float32
                    )
                    s = s * scale + bias
                    m_old = m_p[:, e * HD : e * HD + 1]
                    m_new = jnp.maximum(m_old, jnp.max(s, axis=1, keepdims=True))
                    alpha = jnp.exp(m_old - m_new)
                    p = jnp.exp(s - m_new)
                    total = jnp.sum(p, axis=1, keepdims=True)
                    pv = jnp.dot(p.astype(jnp.bfloat16), v_p, preferred_element_type=jnp.float32)
                    halves.append((m_new, alpha, total, pv))
                (m0, a0, t0, pv0), (m1, a1, t1, pv1) = halves
                alpha = jnp.where(low, a0, a1)
                m_ref[:, cols] = jnp.where(low, m0, m1)
                l_ref[:, cols] = alpha * l_ref[:, cols] + jnp.where(low, t0, t1)
                acc_ref[:, cols] = alpha * acc_ref[:, cols] + jnp.where(low, pv0, pv1)

    if final:
        out_ref[...] = (acc_ref[...] / l_ref[...]).astype(out_ref.dtype)


def whole_kernel(sources, flags_ref, q_ref, code_ref, qclip_ref, *refs):
    n_in = max(src for src, _ in sources) + 1
    kv_hbm = refs[:n_in]
    k_own, v_own = refs[n_in : n_in + 2]
    out_ref, bias_ref, m_ref, l_ref, acc_ref, kv_buf, sems = refs[n_in + 2 :]
    row_count, col_count = out_ref.shape
    sub_rows = code_ref.shape[1]
    piece = row_count // sub_rows
    pair = 2 * HD
    qclip = qclip_ref[...]
    low = lax.broadcasted_iota(jnp.int32, (row_count, pair), 1) < HD

    def fetch(b):
        src, idx = sources[b]
        if src < 0:
            return [
                pltpu.make_async_copy(k_own, kv_buf.at[b, 0], sems.at[b, 0]),
                pltpu.make_async_copy(v_own, kv_buf.at[b, 1], sems.at[b, 1]),
            ]
        return [pltpu.make_async_copy(kv_hbm[src].at[idx], kv_buf.at[b], sems.at[b, 0])]

    for b in range(len(sources)):

        @pl.when(flags_ref[b] > 0)
        def _():
            for copy in fetch(b):
                copy.start()

    for b in range(len(sources)):

        @pl.when(flags_ref[b] > 0)
        def _():
            code = code_ref[b]
            allowed = jnp.concatenate(
                [
                    jnp.broadcast_to(
                        qclip[i * piece : (i + 1) * piece] == code[i : i + 1, :],
                        (piece, code.shape[1]),
                    )
                    for i in range(sub_rows)
                ],
                axis=0,
            )
            bias_ref[b] = jnp.where(allowed, 0.0, -1e30).astype(jnp.float32)

    m_ref[...] = jnp.full(m_ref.shape, -1e30, jnp.float32)
    l_ref[...] = jnp.zeros(l_ref.shape, jnp.float32)
    acc_ref[...] = jnp.zeros(acc_ref.shape, jnp.float32)

    def scores(b, hp, e):
        cols = slice(hp * pair, (hp + 1) * pair)
        k_p = kv_buf[b, 0, :, cols]
        s = lax.dot_general(
            q_ref[e, :, cols], k_p, (((1,), (1,)), ((), ())), preferred_element_type=jnp.float32
        )
        return s + bias_ref[b]

    for b in range(len(sources)):

        @pl.when(flags_ref[b] > 0)
        def _():
            for copy in fetch(b):
                copy.wait()
            for hp in range(col_count // pair):
                for e in range(2):
                    h = 2 * hp + e
                    m_ref[h] = jnp.maximum(m_ref[h], jnp.max(scores(b, hp, e), axis=1, keepdims=True))

    for b in range(len(sources)):

        @pl.when(flags_ref[b] > 0)
        def _():
            for hp in range(col_count // pair):
                cols = slice(hp * pair, (hp + 1) * pair)
                v_p = kv_buf[b, 1, :, cols]
                pvs = []
                for e in range(2):
                    h = 2 * hp + e
                    p = jnp.exp(scores(b, hp, e) - m_ref[h])
                    l_ref[h] = l_ref[h] + jnp.sum(p, axis=1, keepdims=True)
                    pvs.append(
                        jnp.dot(p.astype(jnp.bfloat16), v_p, preferred_element_type=jnp.float32)
                    )
                acc_ref[:, cols] = acc_ref[:, cols] + jnp.where(low, pvs[0], pvs[1])

    for hp in range(col_count // pair):
        cols = slice(hp * pair, (hp + 1) * pair)
        den = jnp.where(low, l_ref[2 * hp], l_ref[2 * hp + 1])
        out_ref[:, cols] = (acc_ref[:, cols] / den).astype(out_ref.dtype)


def attend_chunk(
    state_now, q_split, query_clip, mask_rows, clip_ends, total, inputs, blocks, own_raw
):
    block_total = mask_rows.shape[1]
    sub_rows = mask_rows.shape[0]
    key_pos = jnp.stack([pos for _, _, pos in blocks])
    key_block = key_pos[:, ::BLK] // BLK
    valid = (key_block >= 0) & (key_block < block_total)
    live = jnp.take(mask_rows, jnp.clip(key_block, 0, block_total - 1), axis=1)
    live = jnp.repeat((live == 1) & valid[None], BLK, axis=2)
    key_clip = clip_index(key_pos.reshape(-1), clip_ends).reshape(key_pos.shape)
    code = jnp.where(live, key_clip[None], -1).transpose(1, 0, 2)
    query_sub = query_clip.reshape(sub_rows, -1)
    flags = jnp.any(
        query_sub[None, :, :, None] == code[:, :, None, :], axis=(1, 2, 3)
    ).astype(jnp.int32)
    sources = tuple((src, idx) for src, idx, _ in blocks)
    n_in = len(inputs)
    has_state = state_now is not None
    final = not has_state
    row_count, col_count = q_split.shape[1:]
    state_shape = jax.ShapeDtypeStruct((row_count, col_count), jnp.float32)
    if final:
        out_shape = jax.ShapeDtypeStruct((row_count, col_count), jnp.bfloat16)
        out_specs = pl.BlockSpec(memory_space=pltpu.VMEM)
        head_count = col_count // HD
        scratch = [
            pltpu.VMEM((len(blocks), row_count, row_count), jnp.float32),
            pltpu.VMEM((head_count, row_count, 1), jnp.float32),
            pltpu.VMEM((head_count, row_count, 1), jnp.float32),
            pltpu.VMEM((row_count, col_count), jnp.float32),
            pltpu.VMEM((len(blocks),) + inputs[0].shape[1:], inputs[0].dtype),
            pltpu.SemaphoreType.DMA((len(blocks), 2)),
        ]
        aliases = {}
        extra = own_raw
        q_split = (q_split.astype(jnp.float32) * (1.0 / math.sqrt(HD))).astype(jnp.bfloat16)
    else:
        out_shape = (state_shape,) * 3
        out_specs = [pl.BlockSpec(memory_space=pltpu.VMEM)] * 3
        scratch = []
        aliases = {4 + n_in: 0, 5 + n_in: 1, 6 + n_in: 2}
        extra = tuple(state_now)
    return pl.pallas_call(
        functools.partial(whole_kernel, sources)
        if final
        else functools.partial(chunk_kernel, sources, has_state, final),
        out_shape=out_shape,
        in_specs=[pl.BlockSpec(memory_space=pltpu.SMEM)]
        + [pl.BlockSpec(memory_space=pltpu.VMEM)] * 3
        + [pl.BlockSpec(memory_space=pl.ANY if final else pltpu.VMEM)] * (n_in + len(extra)),
        out_specs=out_specs,
        scratch_shapes=scratch,
        input_output_aliases=aliases,
        cost_estimate=pl.CostEstimate(
            flops=len(blocks) * 8 * row_count**2 * col_count,
            transcendentals=len(blocks) * 2 * row_count**2 * col_count // HD,
            bytes_accessed=sum(x.size * x.dtype.itemsize for x in inputs) + 8 * q_split.size,
        ),
    )(flags, q_split, code, query_clip[:, None], *inputs, *extra)


def body(query_rows, key_rows, value_rows, clip_lengths, block_mask, out_weight, norm_gain):
    row_count, col_count = query_rows.shape
    head_count = col_count // HD
    n_seq = lax.axis_size("seq")
    n_sub = lax.axis_size("sub")
    n_head = lax.axis_size("head")
    seq_i = lax.axis_index("seq")
    sub_i = lax.axis_index("sub")
    head_i = lax.axis_index("head")
    chip_rows = row_count * n_sub
    total = chip_rows * n_seq
    longest = total // 2
    reach = min(n_seq - 1, 1 + (longest - 2) // chip_rows)

    clip_ends = jnp.cumsum(clip_lengths)
    token_first = (seq_i * n_sub + sub_i) * row_count
    mask_height = row_count // BLK
    mask_rows = lax.dynamic_slice_in_dim(block_mask, sub_i * mask_height, mask_height, 0)
    query_clip = clip_index(token_first + jnp.arange(row_count, dtype=jnp.int32), clip_ends)
    local_pos = jnp.arange(row_count, dtype=jnp.int32)

    def block_pos(seq_off, sub_src):
        return ((seq_i + seq_off) * n_sub + sub_src) * row_count + local_pos

    lane = lax.broadcasted_iota(jnp.int32, (1, col_count), 1) % (2 * HD)
    q_split = jnp.stack(
        [jnp.where(lane < HD, query_rows, 0), jnp.where(lane >= HD, query_rows, 0)]
    ).astype(jnp.bfloat16)

    def fold(state_now, mine, theirs):
        if state_now is None:
            inputs = [kv[None] for kv, _ in mine[1:]]
            blocks = [(-1, 0, block_pos(mine[0][1], sub_i))]
            blocks += [(n, 0, block_pos(off, sub_i)) for n, (_, off) in enumerate(mine[1:])]
        else:
            inputs = [kv[None] for kv, _ in mine]
            blocks = [(n, 0, block_pos(off, sub_i)) for n, (_, off) in enumerate(mine)]
        for got, offs, src in theirs:
            if isinstance(got, list):
                for piece, off in zip(got, offs):
                    blocks.append((len(inputs), 0, block_pos(off, src)))
                    inputs.append(piece[None])
            else:
                blocks += [(len(inputs), b, block_pos(off, src)) for b, off in enumerate(offs)]
                inputs.append(got)
        return attend_chunk(
            state_now, q_split, query_clip, mask_rows, clip_ends, total, inputs, blocks,
            (key_rows, value_rows),
        )

    def to_partner(mine):
        offs = [jnp.asarray(off, jnp.int32) for _, off in mine]
        return [
            (jnp.stack([rotated(kv, "sub", n_sub, j) for kv, _ in mine]), offs, (sub_i - j) % n_sub)
            for j in range(1, n_sub)
        ]

    def to_partner_apart(mine):
        offs = [off for _, off in mine]
        return [
            ([rotated(kv, "sub", n_sub, j) for kv, _ in mine], offs, (sub_i - j) % n_sub)
            for j in range(1, n_sub)
        ]

    own = jnp.stack([key_rows, value_rows])
    if reach <= 4:
        to_partner = to_partner_apart
        mine = [(own, 0)]
        theirs = to_partner(mine)
        left = own
        right = own
        for step in range(1, reach + 1):
            right = shifted(right, "seq", n_seq, 1)
            left = shifted(left, "seq", n_seq, -1)
            near = [(left, -step), (right, step)]
            mine += near
            theirs += to_partner(near)
        attended = fold(None, mine, theirs)
    else:
        state = (
            jnp.full((row_count, col_count), -1e30, jnp.float32),
            jnp.zeros((row_count, col_count), jnp.float32),
            jnp.zeros((row_count, col_count), jnp.float32),
        )
        state = fold(state, [(own, 0)], [])
        pending = to_partner([(own, 0)])

        def seq_step(step, carry):
            state_now, left, right, pending_now = carry
            right = shifted(right, "seq", n_seq, 1)
            left = shifted(left, "seq", n_seq, -1)
            near = [(left, -step), (right, step)]
            state_now = fold(state_now, near, pending_now)
            return (state_now, left, right, to_partner(near))

        carry = seq_step(1, (state, own, own, pending))
        carry = lax.fori_loop(2, reach + 1, seq_step, carry)
        state = fold(carry[0], [], carry[3])
        row_max, running, weighted = state
        attended = (weighted / running).astype(jnp.bfloat16)

    n_dev = n_seq * n_sub
    width = out_weight.shape[1]
    projected = jnp.dot(
        attended,
        lax.dynamic_slice_in_dim(out_weight, head_i * col_count, col_count, 0),
        preferred_element_type=jnp.float32,
    )
    for j in range(1, n_head):
        got = rotated(attended, "head", n_head, j)
        src = (head_i - j) % n_head
        projected = projected + jnp.dot(
            got,
            lax.dynamic_slice_in_dim(out_weight, src * col_count, col_count, 0),
            preferred_element_type=jnp.float32,
        )
    prev_tail = shifted(projected[row_count - F :], ("seq", "sub"), n_dev, -1)
    next_head = shifted(projected[:F], ("seq", "sub"), n_dev, 1)
    projected = jnp.concatenate([prev_tail, projected, next_head], axis=0)

    positions = token_first + jnp.arange(row_count, dtype=jnp.int32)
    clip_here = clip_index(positions, clip_ends)
    earlier = jnp.where(
        (clip_index(positions - F, clip_ends) == clip_here)[:, None], projected[:row_count], 0.0
    )
    later = jnp.where(
        (clip_index(positions + F, clip_ends) == clip_here)[:, None], projected[2 * F :], 0.0
    )
    blended = projected[F : F + row_count] + 0.5 * (earlier + later)
    squares = jnp.sum(blended * blended, axis=1)
    scale = lax.rsqrt(squares / width + 1e-06)
    own_cols = lax.dynamic_slice_in_dim(blended, head_i * col_count, col_count, 1)
    return (own_cols * scale[:, None] * norm_gain.astype(jnp.float32)).astype(jnp.bfloat16)


def solution(mesh):
    placed = (
        P(("grp", "seq", "sub"), "head"),
        P(("grp", "seq", "sub"), "head"),
        P(("grp", "seq", "sub"), "head"),
        P("grp"),
        P(("grp", "seq"), None),
        P(),
        P("head"),
    )
    return jax.shard_map(
        body,
        mesh=mesh,
        in_specs=placed,
        out_specs=P(("grp", "seq", "sub"), "head"),
        check_vma=False,
    )
```

```python
import functools
import math

import jax
import jax.numpy as jnp
from jax.experimental import pallas as pl
from jax.experimental.pallas import tpu as pltpu
from jax import lax
from jax.sharding import PartitionSpec as P

HD = 64
BLK = 64
F = 64


def clip_index(positions, clip_ends):
    return jnp.sum((clip_ends[None, :] <= positions[:, None]).astype(jnp.int32), axis=1)


def shifted(x, axis, count, step):
    pairs = [(i + step, i) for i in range(count) if 0 <= i + step < count]
    return lax.ppermute(x, axis, pairs)


def rotated(x, axis, count, step):
    return lax.ppermute(x, axis, [(i, (i + step) % count) for i in range(count)])


def chunk_kernel(sources, has_state, final, flags_ref, q_ref, code_ref, qclip_ref, *refs):
    n_in = max(src for src, _ in sources) + 1
    kv_refs = refs[:n_in]
    rest = refs[n_in:]
    if has_state:
        m_in, l_in, acc_in = rest[:3]
        rest = rest[3:]
    if final:
        out_ref, m_ref, l_ref, acc_ref = rest
    else:
        m_ref, l_ref, acc_ref = rest
    row_count, col_count = acc_ref.shape
    sub_rows = code_ref.shape[1]
    piece = row_count // sub_rows
    pair = 2 * HD
    scale = 1.0 / math.sqrt(HD)
    if has_state:
        m_ref[...] = m_in[...]
        l_ref[...] = l_in[...]
        acc_ref[...] = acc_in[...]
    else:
        m_ref[...] = jnp.full(m_ref.shape, -1e30, jnp.float32)
        l_ref[...] = jnp.zeros(l_ref.shape, jnp.float32)
        acc_ref[...] = jnp.zeros(acc_ref.shape, jnp.float32)
    qclip = qclip_ref[...]
    low = lax.broadcasted_iota(jnp.int32, (row_count, pair), 1) < HD
    for b, (src, idx) in enumerate(sources):

        @pl.when(flags_ref[b] > 0)
        def _():
            code = code_ref[b]
            allowed = jnp.concatenate(
                [
                    jnp.broadcast_to(
                        qclip[i * piece : (i + 1) * piece] == code[i : i + 1, :],
                        (piece, code.shape[1]),
                    )
                    for i in range(sub_rows)
                ],
                axis=0,
            )
            bias = jnp.where(allowed, 0.0, -1e30).astype(jnp.float32)
            for hp in range(col_count // pair):
                cols = slice(hp * pair, (hp + 1) * pair)
                k_p = kv_refs[src][idx, 0, :, cols]
                v_p = kv_refs[src][idx, 1, :, cols]
                m_p = m_ref[:, cols]
                halves = []
                for e in range(2):
                    q_e = q_ref[e, :, cols]
                    s = lax.dot_general(
                        q_e, k_p, (((1,), (1,)), ((), ())), preferred_element_type=jnp.float32
                    )
                    s = s * scale + bias
                    m_old = m_p[:, e * HD : e * HD + 1]
                    m_new = jnp.maximum(m_old, jnp.max(s, axis=1, keepdims=True))
                    alpha = jnp.exp(m_old - m_new)
                    p = jnp.exp(s - m_new)
                    total = jnp.sum(p, axis=1, keepdims=True)
                    pv = jnp.dot(p.astype(jnp.bfloat16), v_p, preferred_element_type=jnp.float32)
                    halves.append((m_new, alpha, total, pv))
                (m0, a0, t0, pv0), (m1, a1, t1, pv1) = halves
                alpha = jnp.where(low, a0, a1)
                m_ref[:, cols] = jnp.where(low, m0, m1)
                l_ref[:, cols] = alpha * l_ref[:, cols] + jnp.where(low, t0, t1)
                acc_ref[:, cols] = alpha * acc_ref[:, cols] + jnp.where(low, pv0, pv1)

    if final:
        out_ref[...] = (acc_ref[...] / l_ref[...]).astype(out_ref.dtype)


def whole_kernel(sources, flags_ref, q_ref, code_ref, qclip_ref, *refs):
    n_in = max(src for src, _ in sources) + 1
    kv_hbm = refs[:n_in]
    out_ref, bias_ref, m_ref, l_ref, acc_ref, kv_buf, sems = refs[n_in:]
    row_count, col_count = out_ref.shape
    sub_rows = code_ref.shape[1]
    piece = row_count // sub_rows
    pair = 2 * HD
    qclip = qclip_ref[...]
    low = lax.broadcasted_iota(jnp.int32, (row_count, pair), 1) < HD

    def fetch(b):
        src, idx = sources[b]
        return pltpu.make_async_copy(kv_hbm[src].at[idx], kv_buf.at[b], sems.at[b])

    for b in range(len(sources)):

        @pl.when(flags_ref[b] > 0)
        def _():
            fetch(b).start()

    for b in range(len(sources)):

        @pl.when(flags_ref[b] > 0)
        def _():
            code = code_ref[b]
            allowed = jnp.concatenate(
                [
                    jnp.broadcast_to(
                        qclip[i * piece : (i + 1) * piece] == code[i : i + 1, :],
                        (piece, code.shape[1]),
                    )
                    for i in range(sub_rows)
                ],
                axis=0,
            )
            bias_ref[b] = jnp.where(allowed, 0.0, -1e30).astype(jnp.float32)

    m_ref[...] = jnp.full(m_ref.shape, -1e30, jnp.float32)
    l_ref[...] = jnp.zeros(l_ref.shape, jnp.float32)
    acc_ref[...] = jnp.zeros(acc_ref.shape, jnp.float32)

    def scores(b, hp, e):
        cols = slice(hp * pair, (hp + 1) * pair)
        k_p = kv_buf[b, 0, :, cols]
        s = lax.dot_general(
            q_ref[e, :, cols], k_p, (((1,), (1,)), ((), ())), preferred_element_type=jnp.float32
        )
        return s + bias_ref[b]

    for b in range(len(sources)):

        @pl.when(flags_ref[b] > 0)
        def _():
            fetch(b).wait()
            for hp in range(col_count // pair):
                for e in range(2):
                    h = 2 * hp + e
                    m_ref[h] = jnp.maximum(m_ref[h], jnp.max(scores(b, hp, e), axis=1, keepdims=True))

    for b in range(len(sources)):

        @pl.when(flags_ref[b] > 0)
        def _():
            for hp in range(col_count // pair):
                cols = slice(hp * pair, (hp + 1) * pair)
                v_p = kv_buf[b, 1, :, cols]
                pvs = []
                for e in range(2):
                    h = 2 * hp + e
                    p = jnp.exp(scores(b, hp, e) - m_ref[h])
                    l_ref[h] = l_ref[h] + jnp.sum(p, axis=1, keepdims=True)
                    pvs.append(
                        jnp.dot(p.astype(jnp.bfloat16), v_p, preferred_element_type=jnp.float32)
                    )
                acc_ref[:, cols] = acc_ref[:, cols] + jnp.where(low, pvs[0], pvs[1])

    for hp in range(col_count // pair):
        cols = slice(hp * pair, (hp + 1) * pair)
        den = jnp.where(low, l_ref[2 * hp], l_ref[2 * hp + 1])
        out_ref[:, cols] = (acc_ref[:, cols] / den).astype(out_ref.dtype)


def attend_chunk(state_now, q_split, query_clip, mask_rows, clip_ends, total, inputs, blocks):
    block_total = mask_rows.shape[1]
    sub_rows = mask_rows.shape[0]
    key_pos = jnp.stack([pos for _, _, pos in blocks])
    key_block = key_pos[:, ::BLK] // BLK
    valid = (key_block >= 0) & (key_block < block_total)
    live = jnp.take(mask_rows, jnp.clip(key_block, 0, block_total - 1), axis=1)
    live = jnp.repeat((live == 1) & valid[None], BLK, axis=2)
    key_clip = clip_index(key_pos.reshape(-1), clip_ends).reshape(key_pos.shape)
    code = jnp.where(live, key_clip[None], -1).transpose(1, 0, 2)
    query_sub = query_clip.reshape(sub_rows, -1)
    flags = jnp.any(
        query_sub[None, :, :, None] == code[:, :, None, :], axis=(1, 2, 3)
    ).astype(jnp.int32)
    sources = tuple((src, idx) for src, idx, _ in blocks)
    n_in = len(inputs)
    has_state = state_now is not None
    final = not has_state
    row_count, col_count = q_split.shape[1:]
    state_shape = jax.ShapeDtypeStruct((row_count, col_count), jnp.float32)
    if final:
        out_shape = jax.ShapeDtypeStruct((row_count, col_count), jnp.bfloat16)
        out_specs = pl.BlockSpec(memory_space=pltpu.VMEM)
        head_count = col_count // HD
        scratch = [
            pltpu.VMEM((len(blocks), row_count, row_count), jnp.float32),
            pltpu.VMEM((head_count, row_count, 1), jnp.float32),
            pltpu.VMEM((head_count, row_count, 1), jnp.float32),
            pltpu.VMEM((row_count, col_count), jnp.float32),
            pltpu.VMEM((len(blocks),) + inputs[0].shape[1:], inputs[0].dtype),
            pltpu.SemaphoreType.DMA((len(blocks),)),
        ]
        aliases = {}
        extra = ()
        q_split = (q_split.astype(jnp.float32) * (1.0 / math.sqrt(HD))).astype(jnp.bfloat16)
    else:
        out_shape = (state_shape,) * 3
        out_specs = [pl.BlockSpec(memory_space=pltpu.VMEM)] * 3
        scratch = []
        aliases = {4 + n_in: 0, 5 + n_in: 1, 6 + n_in: 2}
        extra = tuple(state_now)
    return pl.pallas_call(
        functools.partial(whole_kernel, sources)
        if final
        else functools.partial(chunk_kernel, sources, has_state, final),
        out_shape=out_shape,
        in_specs=[pl.BlockSpec(memory_space=pltpu.SMEM)]
        + [pl.BlockSpec(memory_space=pltpu.VMEM)] * 3
        + [pl.BlockSpec(memory_space=pl.ANY if final else pltpu.VMEM)] * n_in
        + [pl.BlockSpec(memory_space=pltpu.VMEM)] * len(extra),
        out_specs=out_specs,
        scratch_shapes=scratch,
        input_output_aliases=aliases,
        cost_estimate=pl.CostEstimate(
            flops=len(blocks) * 8 * row_count**2 * col_count,
            transcendentals=len(blocks) * 2 * row_count**2 * col_count // HD,
            bytes_accessed=sum(x.size * x.dtype.itemsize for x in inputs) + 8 * q_split.size,
        ),
    )(flags, q_split, code, query_clip[:, None], *inputs, *extra)


def body(query_rows, key_rows, value_rows, clip_lengths, block_mask, out_weight, norm_gain):
    row_count, col_count = query_rows.shape
    head_count = col_count // HD
    n_seq = lax.axis_size("seq")
    n_sub = lax.axis_size("sub")
    n_head = lax.axis_size("head")
    seq_i = lax.axis_index("seq")
    sub_i = lax.axis_index("sub")
    head_i = lax.axis_index("head")
    chip_rows = row_count * n_sub
    total = chip_rows * n_seq
    longest = total // 2
    reach = min(n_seq - 1, 1 + (longest - 2) // chip_rows)

    clip_ends = jnp.cumsum(clip_lengths)
    token_first = (seq_i * n_sub + sub_i) * row_count
    mask_height = row_count // BLK
    mask_rows = lax.dynamic_slice_in_dim(block_mask, sub_i * mask_height, mask_height, 0)
    query_clip = clip_index(token_first + jnp.arange(row_count, dtype=jnp.int32), clip_ends)
    local_pos = jnp.arange(row_count, dtype=jnp.int32)

    def block_pos(seq_off, sub_src):
        return ((seq_i + seq_off) * n_sub + sub_src) * row_count + local_pos

    lane = lax.broadcasted_iota(jnp.int32, (1, col_count), 1) % (2 * HD)
    q_split = jnp.stack(
        [jnp.where(lane < HD, query_rows, 0), jnp.where(lane >= HD, query_rows, 0)]
    ).astype(jnp.bfloat16)

    def fold(state_now, mine, theirs):
        inputs = [kv[None] for kv, _ in mine]
        blocks = [(n, 0, block_pos(off, sub_i)) for n, (_, off) in enumerate(mine)]
        for got, offs, src in theirs:
            if isinstance(got, list):
                for piece, off in zip(got, offs):
                    blocks.append((len(inputs), 0, block_pos(off, src)))
                    inputs.append(piece[None])
            else:
                blocks += [(len(inputs), b, block_pos(off, src)) for b, off in enumerate(offs)]
                inputs.append(got)
        return attend_chunk(
            state_now, q_split, query_clip, mask_rows, clip_ends, total, inputs, blocks
        )

    def to_partner(mine):
        offs = [jnp.asarray(off, jnp.int32) for _, off in mine]
        return [
            (jnp.stack([rotated(kv, "sub", n_sub, j) for kv, _ in mine]), offs, (sub_i - j) % n_sub)
            for j in range(1, n_sub)
        ]

    def to_partner_apart(mine):
        offs = [off for _, off in mine]
        return [
            ([rotated(kv, "sub", n_sub, j) for kv, _ in mine], offs, (sub_i - j) % n_sub)
            for j in range(1, n_sub)
        ]

    own = jnp.stack([key_rows, value_rows])
    if reach <= 4:
        to_partner = to_partner_apart
        mine = [(own, 0)]
        theirs = to_partner(mine)
        left = own
        right = own
        for step in range(1, reach + 1):
            right = shifted(right, "seq", n_seq, 1)
            left = shifted(left, "seq", n_seq, -1)
            near = [(left, -step), (right, step)]
            mine += near
            theirs += to_partner(near)
        attended = fold(None, mine, theirs)
    else:
        state = (
            jnp.full((row_count, col_count), -1e30, jnp.float32),
            jnp.zeros((row_count, col_count), jnp.float32),
            jnp.zeros((row_count, col_count), jnp.float32),
        )
        state = fold(state, [(own, 0)], [])
        pending = to_partner([(own, 0)])

        def seq_step(step, carry):
            state_now, left, right, pending_now = carry
            right = shifted(right, "seq", n_seq, 1)
            left = shifted(left, "seq", n_seq, -1)
            near = [(left, -step), (right, step)]
            state_now = fold(state_now, near, pending_now)
            return (state_now, left, right, to_partner(near))

        carry = seq_step(1, (state, own, own, pending))
        carry = lax.fori_loop(2, reach + 1, seq_step, carry)
        state = fold(carry[0], [], carry[3])
        row_max, running, weighted = state
        attended = (weighted / running).astype(jnp.bfloat16)

    n_dev = n_seq * n_sub
    width = out_weight.shape[1]
    projected = jnp.dot(
        attended,
        lax.dynamic_slice_in_dim(out_weight, head_i * col_count, col_count, 0),
        preferred_element_type=jnp.float32,
    )
    for j in range(1, n_head):
        got = rotated(attended, "head", n_head, j)
        src = (head_i - j) % n_head
        projected = projected + jnp.dot(
            got,
            lax.dynamic_slice_in_dim(out_weight, src * col_count, col_count, 0),
            preferred_element_type=jnp.float32,
        )
    prev_tail = shifted(
        projected[row_count - F :].astype(jnp.bfloat16), ("seq", "sub"), n_dev, -1
    ).astype(jnp.float32)
    next_head = shifted(projected[:F].astype(jnp.bfloat16), ("seq", "sub"), n_dev, 1).astype(
        jnp.float32
    )
    projected = jnp.concatenate([prev_tail, projected, next_head], axis=0)

    positions = token_first + jnp.arange(row_count, dtype=jnp.int32)
    clip_here = clip_index(positions, clip_ends)
    earlier = jnp.where(
        (clip_index(positions - F, clip_ends) == clip_here)[:, None], projected[:row_count], 0.0
    )
    later = jnp.where(
        (clip_index(positions + F, clip_ends) == clip_here)[:, None], projected[2 * F :], 0.0
    )
    blended = projected[F : F + row_count] + 0.5 * (earlier + later)
    squares = jnp.sum(blended * blended, axis=1)
    scale = lax.rsqrt(squares / width + 1e-06)
    own_cols = lax.dynamic_slice_in_dim(blended, head_i * col_count, col_count, 1)
    return (own_cols * scale[:, None] * norm_gain.astype(jnp.float32)).astype(jnp.bfloat16)


def solution(mesh):
    placed = (
        P(("grp", "seq", "sub"), "head"),
        P(("grp", "seq", "sub"), "head"),
        P(("grp", "seq", "sub"), "head"),
        P("grp"),
        P(("grp", "seq"), None),
        P(),
        P("head"),
    )
    return jax.shard_map(
        body,
        mesh=mesh,
        in_specs=placed,
        out_specs=P(("grp", "seq", "sub"), "head"),
        check_vma=False,
    )
```

```python
import functools
import math

import jax
import jax.numpy as jnp
from jax.experimental import pallas as pl
from jax.experimental.pallas import tpu as pltpu
from jax import lax
from jax.sharding import PartitionSpec as P

HD = 64
BLK = 64
F = 64


def clip_index(positions, clip_ends):
    return jnp.sum((clip_ends[None, :] <= positions[:, None]).astype(jnp.int32), axis=1)


def shifted(x, axis, count, step):
    pairs = [(i + step, i) for i in range(count) if 0 <= i + step < count]
    return lax.ppermute(x, axis, pairs)


def rotated(x, axis, count, step):
    return lax.ppermute(x, axis, [(i, (i + step) % count) for i in range(count)])


def chunk_kernel(sources, has_state, final, flags_ref, q_ref, code_ref, qclip_ref, *refs):
    n_in = max(src for src, _ in sources) + 1
    kv_refs = refs[:n_in]
    rest = refs[n_in:]
    if has_state:
        m_in, l_in, acc_in = rest[:3]
        rest = rest[3:]
    if final:
        out_ref, m_ref, l_ref, acc_ref = rest
    else:
        m_ref, l_ref, acc_ref = rest
    row_count, col_count = acc_ref.shape
    sub_rows = code_ref.shape[1]
    piece = row_count // sub_rows
    pair = 2 * HD
    scale = 1.0 / math.sqrt(HD)
    if has_state:
        m_ref[...] = m_in[...]
        l_ref[...] = l_in[...]
        acc_ref[...] = acc_in[...]
    else:
        m_ref[...] = jnp.full(m_ref.shape, -1e30, jnp.float32)
        l_ref[...] = jnp.zeros(l_ref.shape, jnp.float32)
        acc_ref[...] = jnp.zeros(acc_ref.shape, jnp.float32)
    qclip = qclip_ref[...]
    low = lax.broadcasted_iota(jnp.int32, (row_count, pair), 1) < HD
    for b, (src, idx) in enumerate(sources):

        @pl.when(flags_ref[b] > 0)
        def _():
            code = code_ref[b]
            allowed = jnp.concatenate(
                [
                    jnp.broadcast_to(
                        qclip[i * piece : (i + 1) * piece] == code[i : i + 1, :],
                        (piece, code.shape[1]),
                    )
                    for i in range(sub_rows)
                ],
                axis=0,
            )
            bias = jnp.where(allowed, 0.0, -1e30).astype(jnp.float32)
            for hp in range(col_count // pair):
                cols = slice(hp * pair, (hp + 1) * pair)
                k_p = kv_refs[src][idx, 0, :, cols]
                v_p = kv_refs[src][idx, 1, :, cols]
                m_p = m_ref[:, cols]
                halves = []
                for e in range(2):
                    q_e = q_ref[e, :, cols]
                    s = lax.dot_general(
                        q_e, k_p, (((1,), (1,)), ((), ())), preferred_element_type=jnp.float32
                    )
                    s = s * scale + bias
                    m_old = m_p[:, e * HD : e * HD + 1]
                    m_new = jnp.maximum(m_old, jnp.max(s, axis=1, keepdims=True))
                    alpha = jnp.exp(m_old - m_new)
                    p = jnp.exp(s - m_new)
                    total = jnp.sum(p, axis=1, keepdims=True)
                    pv = jnp.dot(p.astype(jnp.bfloat16), v_p, preferred_element_type=jnp.float32)
                    halves.append((m_new, alpha, total, pv))
                (m0, a0, t0, pv0), (m1, a1, t1, pv1) = halves
                alpha = jnp.where(low, a0, a1)
                m_ref[:, cols] = jnp.where(low, m0, m1)
                l_ref[:, cols] = alpha * l_ref[:, cols] + jnp.where(low, t0, t1)
                acc_ref[:, cols] = alpha * acc_ref[:, cols] + jnp.where(low, pv0, pv1)

    if final:
        out_ref[...] = (acc_ref[...] / l_ref[...]).astype(out_ref.dtype)


def whole_kernel(sources, flags_ref, q_ref, code_ref, qclip_ref, *refs):
    n_in = max(src for src, _ in sources) + 1
    kv_hbm = refs[:n_in]
    k_own, v_own = refs[n_in : n_in + 2]
    out_ref, bias_ref, m_ref, l_ref, acc_ref, kv_buf, sems = refs[n_in + 2 :]
    row_count, col_count = out_ref.shape
    sub_rows = code_ref.shape[1]
    piece = row_count // sub_rows
    pair = 2 * HD
    qclip = qclip_ref[...]
    low = lax.broadcasted_iota(jnp.int32, (row_count, pair), 1) < HD

    def fetch(b):
        src, idx = sources[b]
        if src < 0:
            return [
                pltpu.make_async_copy(k_own, kv_buf.at[b, 0], sems.at[b, 0]),
                pltpu.make_async_copy(v_own, kv_buf.at[b, 1], sems.at[b, 1]),
            ]
        return [pltpu.make_async_copy(kv_hbm[src].at[idx], kv_buf.at[b], sems.at[b, 0])]

    for b in range(len(sources)):

        @pl.when(flags_ref[b] > 0)
        def _():
            for copy in fetch(b):
                copy.start()

    for b in range(len(sources)):

        @pl.when(flags_ref[b] > 0)
        def _():
            code = code_ref[b]
            allowed = jnp.concatenate(
                [
                    jnp.broadcast_to(
                        qclip[i * piece : (i + 1) * piece] == code[i : i + 1, :],
                        (piece, code.shape[1]),
                    )
                    for i in range(sub_rows)
                ],
                axis=0,
            )
            bias_ref[b] = jnp.where(allowed, 0.0, -1e30).astype(jnp.float32)

    m_ref[...] = jnp.full(m_ref.shape, -1e30, jnp.float32)
    l_ref[...] = jnp.zeros(l_ref.shape, jnp.float32)
    acc_ref[...] = jnp.zeros(acc_ref.shape, jnp.float32)

    def scores(b, hp, e):
        cols = slice(hp * pair, (hp + 1) * pair)
        k_p = kv_buf[b, 0, :, cols]
        s = lax.dot_general(
            q_ref[e, :, cols], k_p, (((1,), (1,)), ((), ())), preferred_element_type=jnp.float32
        )
        return s + bias_ref[b]

    for b in range(len(sources)):

        @pl.when(flags_ref[b] > 0)
        def _():
            for copy in fetch(b):
                copy.wait()
            for hp in range(col_count // pair):
                for e in range(2):
                    h = 2 * hp + e
                    m_ref[h] = jnp.maximum(m_ref[h], jnp.max(scores(b, hp, e), axis=1, keepdims=True))

    for b in range(len(sources)):

        @pl.when(flags_ref[b] > 0)
        def _():
            for hp in range(col_count // pair):
                cols = slice(hp * pair, (hp + 1) * pair)
                v_p = kv_buf[b, 1, :, cols]
                pvs = []
                for e in range(2):
                    h = 2 * hp + e
                    p = jnp.exp(scores(b, hp, e) - m_ref[h])
                    l_ref[h] = l_ref[h] + jnp.sum(p, axis=1, keepdims=True)
                    pvs.append(
                        jnp.dot(p.astype(jnp.bfloat16), v_p, preferred_element_type=jnp.float32)
                    )
                acc_ref[:, cols] = acc_ref[:, cols] + jnp.where(low, pvs[0], pvs[1])

    for hp in range(col_count // pair):
        cols = slice(hp * pair, (hp + 1) * pair)
        den = jnp.where(low, l_ref[2 * hp], l_ref[2 * hp + 1])
        out_ref[:, cols] = (acc_ref[:, cols] / den).astype(out_ref.dtype)


def attend_chunk(
    state_now, q_split, query_clip, mask_rows, clip_ends, total, inputs, blocks, own_raw
):
    block_total = mask_rows.shape[1]
    sub_rows = mask_rows.shape[0]
    key_pos = jnp.stack([pos for _, _, pos in blocks])
    key_block = key_pos[:, ::BLK] // BLK
    valid = (key_block >= 0) & (key_block < block_total)
    live = jnp.take(mask_rows, jnp.clip(key_block, 0, block_total - 1), axis=1)
    live = jnp.repeat((live == 1) & valid[None], BLK, axis=2)
    key_clip = clip_index(key_pos.reshape(-1), clip_ends).reshape(key_pos.shape)
    code = jnp.where(live, key_clip[None], -1).transpose(1, 0, 2)
    query_sub = query_clip.reshape(sub_rows, -1)
    flags = jnp.any(
        query_sub[None, :, :, None] == code[:, :, None, :], axis=(1, 2, 3)
    ).astype(jnp.int32)
    sources = tuple((src, idx) for src, idx, _ in blocks)
    n_in = len(inputs)
    has_state = state_now is not None
    final = not has_state
    row_count, col_count = q_split.shape[1:]
    state_shape = jax.ShapeDtypeStruct((row_count, col_count), jnp.float32)
    if final:
        out_shape = jax.ShapeDtypeStruct((row_count, col_count), jnp.bfloat16)
        out_specs = pl.BlockSpec(memory_space=pltpu.VMEM)
        head_count = col_count // HD
        scratch = [
            pltpu.VMEM((len(blocks), row_count, row_count), jnp.float32),
            pltpu.VMEM((head_count, row_count, 1), jnp.float32),
            pltpu.VMEM((head_count, row_count, 1), jnp.float32),
            pltpu.VMEM((row_count, col_count), jnp.float32),
            pltpu.VMEM((len(blocks),) + inputs[0].shape[1:], inputs[0].dtype),
            pltpu.SemaphoreType.DMA((len(blocks), 2)),
        ]
        aliases = {}
        extra = own_raw
        q_split = (q_split.astype(jnp.float32) * (1.0 / math.sqrt(HD))).astype(jnp.bfloat16)
    else:
        out_shape = (state_shape,) * 3
        out_specs = [pl.BlockSpec(memory_space=pltpu.VMEM)] * 3
        scratch = []
        aliases = {4 + n_in: 0, 5 + n_in: 1, 6 + n_in: 2}
        extra = tuple(state_now)
    return pl.pallas_call(
        functools.partial(whole_kernel, sources)
        if final
        else functools.partial(chunk_kernel, sources, has_state, final),
        out_shape=out_shape,
        in_specs=[pl.BlockSpec(memory_space=pltpu.SMEM)]
        + [pl.BlockSpec(memory_space=pltpu.VMEM)] * 3
        + [pl.BlockSpec(memory_space=pl.ANY if final else pltpu.VMEM)] * (n_in + len(extra)),
        out_specs=out_specs,
        scratch_shapes=scratch,
        input_output_aliases=aliases,
        cost_estimate=pl.CostEstimate(
            flops=len(blocks) * 8 * row_count**2 * col_count,
            transcendentals=len(blocks) * 2 * row_count**2 * col_count // HD,
            bytes_accessed=sum(x.size * x.dtype.itemsize for x in inputs) + 8 * q_split.size,
        ),
    )(flags, q_split, code, query_clip[:, None], *inputs, *extra)


def body(query_rows, key_rows, value_rows, clip_lengths, block_mask, out_weight, norm_gain):
    row_count, col_count = query_rows.shape
    head_count = col_count // HD
    n_seq = lax.axis_size("seq")
    n_sub = lax.axis_size("sub")
    n_head = lax.axis_size("head")
    seq_i = lax.axis_index("seq")
    sub_i = lax.axis_index("sub")
    head_i = lax.axis_index("head")
    chip_rows = row_count * n_sub
    total = chip_rows * n_seq
    longest = total // 2
    reach = min(n_seq - 1, 1 + (longest - 2) // chip_rows)

    clip_ends = jnp.cumsum(clip_lengths)
    token_first = (seq_i * n_sub + sub_i) * row_count
    mask_height = row_count // BLK
    mask_rows = lax.dynamic_slice_in_dim(block_mask, sub_i * mask_height, mask_height, 0)
    query_clip = clip_index(token_first + jnp.arange(row_count, dtype=jnp.int32), clip_ends)
    local_pos = jnp.arange(row_count, dtype=jnp.int32)

    def block_pos(seq_off, sub_src):
        return ((seq_i + seq_off) * n_sub + sub_src) * row_count + local_pos

    lane = lax.broadcasted_iota(jnp.int32, (1, col_count), 1) % (2 * HD)
    q_split = jnp.stack(
        [jnp.where(lane < HD, query_rows, 0), jnp.where(lane >= HD, query_rows, 0)]
    ).astype(jnp.bfloat16)

    def fold(state_now, mine, theirs):
        if state_now is None:
            inputs = [kv[None] for kv, _ in mine[1:]]
            blocks = [(-1, 0, block_pos(mine[0][1], sub_i))]
            blocks += [(n, 0, block_pos(off, sub_i)) for n, (_, off) in enumerate(mine[1:])]
        else:
            inputs = [kv[None] for kv, _ in mine]
            blocks = [(n, 0, block_pos(off, sub_i)) for n, (_, off) in enumerate(mine)]
        for got, offs, src in theirs:
            if isinstance(got, list):
                for piece, off in zip(got, offs):
                    blocks.append((len(inputs), 0, block_pos(off, src)))
                    inputs.append(piece[None])
            else:
                blocks += [(len(inputs), b, block_pos(off, src)) for b, off in enumerate(offs)]
                inputs.append(got)
        return attend_chunk(
            state_now, q_split, query_clip, mask_rows, clip_ends, total, inputs, blocks,
            (key_rows, value_rows),
        )

    def to_partner(mine):
        offs = [jnp.asarray(off, jnp.int32) for _, off in mine]
        return [
            (jnp.stack([rotated(kv, "sub", n_sub, j) for kv, _ in mine]), offs, (sub_i - j) % n_sub)
            for j in range(1, n_sub)
        ]

    def to_partner_apart(mine):
        offs = [off for _, off in mine]
        return [
            ([rotated(kv, "sub", n_sub, j) for kv, _ in mine], offs, (sub_i - j) % n_sub)
            for j in range(1, n_sub)
        ]

    own = jnp.stack([key_rows, value_rows])
    if reach <= 4:
        to_partner = to_partner_apart
        mine = [(own, 0)]
        theirs = to_partner(mine)
        left = own
        right = own
        for step in range(1, reach + 1):
            right = shifted(right, "seq", n_seq, 1)
            left = shifted(left, "seq", n_seq, -1)
            near = [(left, -step), (right, step)]
            mine += near
            theirs += to_partner(near)
        attended = fold(None, mine, theirs)
    else:
        state = (
            jnp.full((row_count, col_count), -1e30, jnp.float32),
            jnp.zeros((row_count, col_count), jnp.float32),
            jnp.zeros((row_count, col_count), jnp.float32),
        )
        state = fold(state, [(own, 0)], [])
        pending = to_partner([(own, 0)])

        def seq_step(step, carry):
            state_now, left, right, pending_now = carry
            right = shifted(right, "seq", n_seq, 1)
            left = shifted(left, "seq", n_seq, -1)
            near = [(left, -step), (right, step)]
            state_now = fold(state_now, near, pending_now)
            return (state_now, left, right, to_partner(near))

        carry = seq_step(1, (state, own, own, pending))
        carry = lax.fori_loop(2, reach + 1, seq_step, carry)
        state = fold(carry[0], [], carry[3])
        row_max, running, weighted = state
        attended = (weighted / running).astype(jnp.bfloat16)

    n_dev = n_seq * n_sub
    width = out_weight.shape[1]
    projected = jnp.dot(
        attended,
        lax.dynamic_slice_in_dim(out_weight, head_i * col_count, col_count, 0),
        preferred_element_type=jnp.float32,
    )
    for j in range(1, n_head):
        got = rotated(attended, "head", n_head, j)
        src = (head_i - j) % n_head
        projected = projected + jnp.dot(
            got,
            lax.dynamic_slice_in_dim(out_weight, src * col_count, col_count, 0),
            preferred_element_type=jnp.float32,
        )
    prev_tail = shifted(
        projected[row_count - F :].astype(jnp.bfloat16), ("seq", "sub"), n_dev, -1
    ).astype(jnp.float32)
    next_head = shifted(projected[:F].astype(jnp.bfloat16), ("seq", "sub"), n_dev, 1).astype(
        jnp.float32
    )
    projected = jnp.concatenate([prev_tail, projected, next_head], axis=0)

    positions = token_first + jnp.arange(row_count, dtype=jnp.int32)
    clip_here = clip_index(positions, clip_ends)
    earlier = jnp.where(
        (clip_index(positions - F, clip_ends) == clip_here)[:, None], projected[:row_count], 0.0
    )
    later = jnp.where(
        (clip_index(positions + F, clip_ends) == clip_here)[:, None], projected[2 * F :], 0.0
    )
    blended = projected[F : F + row_count] + 0.5 * (earlier + later)
    squares = jnp.sum(blended * blended, axis=1)
    scale = lax.rsqrt(squares / width + 1e-06)
    own_cols = lax.dynamic_slice_in_dim(blended, head_i * col_count, col_count, 1)
    return (own_cols * scale[:, None] * norm_gain.astype(jnp.float32)).astype(jnp.bfloat16)


def solution(mesh):
    placed = (
        P(("grp", "seq", "sub"), "head"),
        P(("grp", "seq", "sub"), "head"),
        P(("grp", "seq", "sub"), "head"),
        P("grp"),
        P(("grp", "seq"), None),
        P(),
        P("head"),
    )
    return jax.shard_map(
        body,
        mesh=mesh,
        in_specs=placed,
        out_specs=P(("grp", "seq", "sub"), "head"),
        check_vma=False,
    )
```
